32 devices in a mesh: groups: 2 (over x), ctx: 8 (over z, y), head: 2 (over core).
Axes of the slice: x: 2, y: 2, z: 4, core: 2. Of those that a mesh axis runs over, the one named last changes fastest.
Arguments:
- query_linear: bfloat16 [4096, 32, 128], P(('groups', 'ctx'), 'head'), parts along dimension 0, may hold values from -6 to 6
- key_linear: bfloat16 [4096, 32, 128], P(('groups', 'ctx'), 'head'), parts along dimension 0, may hold values from -6 to 6
- value_linear: bfloat16 [4096, 32, 128], P(('groups', 'ctx'), 'head'), parts along dimension 0, may hold values from -6 to 6
- gate_logits: bfloat16 [4096, 32, 128], P(('groups', 'ctx'), 'head'), parts along dimension 0, may hold values from -8 to 8
- norm_gain: float32 [32, 128], P('head'), may hold values from 0.5 to 1.5
- decay_code: int32 [32], P('head'), may hold values from 16 to 32767
- query_soft: bfloat16 [4096, 32, 128], P(('groups', 'ctx'), 'head'), parts along dimension 0, may hold values from -9 to 9
- key_soft: bfloat16 [4096, 32, 128], P(('groups', 'ctx'), 'head'), parts along dimension 0, may hold values from -9 to 9
- yarn_factor: int32 [1], replicated, may hold values from 2 to 32
Outputs:
- attended: bfloat16 [4096, 32, 128], P(('groups', 'ctx'), 'head'), parts along dimension 0
The draws below stay inside these ranges and needn't reach their ends.
There are 2 independent parts, one for each index of `groups`. The reference program is written for one: setup_inputs(seed, part) draws one part's arguments, and reference() takes and returns one part's arrays. A program takes and returns all parts, laid end to end along the dimension named above; an argument that names none is the same for every part. Nothing has to cross between parts.
All inputs are finite; a program needn't handle non-finite values.
Results may differ from the reference program's by a relative error of at most 0.0085.
Values may be sent and summed in bfloat16 or wider, within the bound.
No kernel may reach another device: no remote copies, remote signals or barrier semaphores. Data moves between devices by JAX's collectives and lax.ppermute only.
A program may use at most 320 MiB of HBM per device.

```python
import math
import jax
import jax.numpy as jnp
from jax import lax

HEADS = 32
HEAD_DIM = 128
BLOCK = 64
ORIG_CTX = 8192
SEQ = 2048


def draw_decay_code(key, part):
    key_exp, key_extra, key_high, key_low = jax.random.split(key, 4)
    exponent = jax.random.randint(key_exp, (HEADS,), 4, 15)
    base_code = jnp.left_shift(jnp.ones((HEADS,), jnp.int32), exponent)
    extra_code = jax.random.randint(key_extra, (HEADS,), 0, 16384) % base_code
    codes = base_code + extra_code
    high_head = jax.random.randint(key_high, (), 0, HEADS)
    low_head = (high_head + 1 + jax.random.randint(key_low, (), 0, HEADS - 1)) % HEADS
    head_ids = jnp.arange(HEADS)
    codes = jnp.where(head_ids == high_head, 32767, codes)
    codes = jnp.where(head_ids == low_head, 16, codes)
    return codes.astype(jnp.int32)


def drawn_pair(key):
    base_key = jax.random.fold_in(key, 41)
    key_query, key_keys = jax.random.split(base_key, 2)
    full_shape = (SEQ, HEADS, HEAD_DIM)
    query_part = jnp.clip(jax.random.normal(key_query, full_shape, jnp.float32), -6.0, 6.0)
    key_part = jnp.clip(jax.random.normal(key_keys, full_shape, jnp.float32), -6.0, 6.0)
    return (query_part, key_part)


def draw_query_soft(key, part):
    return drawn_pair(key)[0].astype(jnp.bfloat16)


def draw_key_soft(key, part):
    return drawn_pair(key)[1].astype(jnp.bfloat16)


def level_of(key, shape, cuts, smallest, high):
    def one(axis_at, shards_of):
        heights = jax.random.uniform(jax.random.fold_in(jax.random.fold_in(key, 6), axis_at), (shards_of,), jnp.float32, smallest / len(cuts), high / len(cuts))
        return jnp.repeat(jnp.exp(heights), shape[axis_at] // shards_of).reshape((-1,) + (1,) * (len(shape) - axis_at - 1))

    factor_of = one(*cuts[0])
    for cut in cuts[1:]:
        factor_of = factor_of * one(*cut)
    return factor_of


def scatter_about(stream_key, extent, scale, bound, cuts=(), kind=jnp.bfloat16):
    entries = scale * jax.random.normal(stream_key, extent, jnp.float32)
    if cuts:
        entries = entries * level_of(stream_key, extent, cuts, -0.22, 0.18)
    return jnp.clip(entries, -bound, bound).astype(kind)


def setup_inputs(seed: int = 0, part: int = 0) -> dict:
    seeds = jax.random.split(jax.random.key(seed), 10)
    own_keys = jax.random.split(jax.random.fold_in(seeds[9], part), 10)
    query_linear = scatter_about(own_keys[0], (SEQ, HEADS, HEAD_DIM), 1.0, 6.0, ((0, 8), (1, 2)))
    key_linear = scatter_about(own_keys[1], (SEQ, HEADS, HEAD_DIM), 1.0, 6.0, ((0, 8), (1, 2)))
    value_linear = scatter_about(own_keys[2], (SEQ, HEADS, HEAD_DIM), 1.0, 6.0, ((0, 8), (1, 2)))
    gate_logits = scatter_about(own_keys[3], (SEQ, HEADS, HEAD_DIM), 1.5, 8.0, ((0, 8), (1, 2)))
    norm_gain = jnp.clip(0.5 + 1.0 * jax.random.uniform(seeds[4], (HEADS, HEAD_DIM), jnp.float32) ** level_of(seeds[4], (HEADS, HEAD_DIM), ((0, 2),), -0.2, 0.2), 0.5, 1.5)
    decay_code = draw_decay_code(jax.random.fold_in(seeds[9], 71), part)
    query_soft = draw_query_soft(jax.random.fold_in(jax.random.fold_in(seeds[9], part), 71), part)
    key_soft = draw_key_soft(jax.random.fold_in(jax.random.fold_in(seeds[9], part), 71), part)
    yarn_factor = jax.random.randint(seeds[8], (1,), 2, 33).astype(jnp.int32)
    return dict(query_linear=query_linear, key_linear=key_linear, value_linear=value_linear, gate_logits=gate_logits, norm_gain=norm_gain, decay_code=decay_code, query_soft=query_soft, key_soft=key_soft, yarn_factor=yarn_factor)


rope_base = 10000.0
beta_fast = 32.0
beta_slow = 1.0
norm_eps = 1e-05

def yarn_table(yarn_factor, head_width):
    factor = yarn_factor[0].astype(jnp.float32)
    pair_ids = jnp.arange(head_width // 2, dtype=jnp.float32)
    base_freq = rope_base ** (-2.0 * pair_ids / head_width)
    wavelength = 2.0 * math.pi / base_freq
    ramp = jnp.clip((ORIG_CTX / wavelength - beta_slow) / (beta_fast - beta_slow), 0.0, 1.0)
    freq = base_freq * (ramp + (1.0 - ramp) / factor)
    mscale = 0.1 * jnp.log(factor) + 1.0
    return (freq, mscale * mscale / math.sqrt(head_width))

def rotate(values_in, positions, freq):
    angle = positions[:, None] * freq[None, :]
    cosine = jnp.cos(angle)[:, None, :]
    sine = jnp.sin(angle)[:, None, :]
    half_width = values_in.shape[2] // 2
    first = values_in[:, :, :half_width].astype(jnp.float32)
    second = values_in[:, :, half_width:].astype(jnp.float32)
    joined = jnp.concatenate([first * cosine - second * sine, second * cosine + first * sine], axis=2)
    return joined.astype(jnp.bfloat16)

def lightning(q_hat, k_hat, value_linear, logdec):
    tok_rows, head_count, head_width = q_hat.shape
    block_count = tok_rows // BLOCK
    offsets = jnp.arange(BLOCK, dtype=jnp.float32)
    step_gap = offsets[:, None] - offsets[None, :]
    causal = step_gap >= 0
    intra_decay = jnp.where(causal[None], jnp.exp(logdec[:, None, None] * jnp.where(causal, step_gap, 0.0)[None]), 0.0)
    query_decay = jnp.exp(logdec[None, :] * (offsets[:, None] + 1.0))
    key_decay = jnp.exp(logdec[None, :] * (BLOCK - 1.0 - offsets[:, None]))
    block_decay = jnp.exp(logdec * BLOCK)

    def advance(carry_state, inputs):
        q_block, k_block, v_block = inputs
        q_float = q_block.astype(jnp.float32)
        k_float = k_block.astype(jnp.float32)
        v_float = v_block.astype(jnp.float32)
        scores = jnp.einsum('thd,shd->hts', q_float, k_float)
        weights = (scores * intra_decay).astype(jnp.bfloat16)
        intra_part = jnp.einsum('hts,shd->thd', weights.astype(jnp.float32), v_float)
        carried = jnp.einsum('thd,hde->the', q_float * query_decay[:, :, None], carry_state, precision=lax.Precision.HIGHEST)
        fresh_state = jnp.einsum('thd,the->hde', k_float * key_decay[:, :, None], v_float, precision=lax.Precision.HIGHEST)
        return (carry_state * block_decay[:, None, None] + fresh_state, intra_part + carried)

    def split_blocks(array_in):
        return array_in.reshape(block_count, BLOCK, head_count, head_width)
    zero_state = jnp.zeros((head_count, head_width, head_width), jnp.float32)
    final_state, outputs = lax.scan(advance, zero_state, (split_blocks(q_hat), split_blocks(k_hat), split_blocks(value_linear)))
    return (final_state, outputs.reshape(tok_rows, head_count, head_width))

def reference(query_linear, key_linear, value_linear, gate_logits, norm_gain, decay_code, query_soft, key_soft, yarn_factor):
    logdec = jnp.log1p(-decay_code.astype(jnp.float32) * 2.0 ** (-20))
    q_hat = jax.nn.silu(query_linear.astype(jnp.float32)).astype(jnp.bfloat16)
    k_hat = jax.nn.silu(key_linear.astype(jnp.float32)).astype(jnp.bfloat16)
    final_state, linear_out = lightning(q_hat, k_hat, value_linear, logdec)
    mean_sq = lax.optimization_barrier(jnp.mean(linear_out * linear_out, axis=(1, 2)))
    normed = linear_out * lax.rsqrt(mean_sq + norm_eps)[:, None, None] * norm_gain[None] * jax.nn.sigmoid(gate_logits.astype(jnp.float32))
    values_soft = normed.astype(jnp.bfloat16)
    freq, logit_scale = yarn_table(yarn_factor, query_soft.shape[2])
    positions = jnp.arange(SEQ, dtype=jnp.float32)
    query_rot = rotate(query_soft, positions, freq)
    key_rot = rotate(key_soft, positions, freq)
    row_ids = jnp.arange(SEQ, dtype=jnp.int32)
    allowed = row_ids[None, :] <= row_ids[:, None]

    def one_head(inputs):
        query_head, key_head, value_head = inputs
        scores = jnp.dot(query_head, key_head.T, preferred_element_type=jnp.float32) * logit_scale
        scores = jnp.where(allowed, scores, -jnp.inf)
        top = lax.optimization_barrier(jnp.max(scores, axis=1, keepdims=True))
        probs = jnp.exp(scores - top)
        denom = lax.optimization_barrier(jnp.sum(probs, axis=1))
        numer = jnp.dot(probs.astype(jnp.bfloat16), value_head, preferred_element_type=jnp.float32)
        return (numer / denom[:, None]).astype(jnp.bfloat16)
    per_head = lax.map(one_head, (query_rot.transpose(1, 0, 2), key_rot.transpose(1, 0, 2), values_soft.transpose(1, 0, 2)))
    return per_head.transpose(1, 0, 2)
```

```python
import math

import jax
import jax.numpy as jnp
from jax import lax
from jax.sharding import PartitionSpec as P

BLOCK = 64
ORIG_CTX = 8192


rope_base = 10000.0
beta_fast = 32.0
beta_slow = 1.0
norm_eps = 1e-05
low_floor = -1e30


def yarn_table(yarn_factor, head_width):
    factor = yarn_factor[0].astype(jnp.float32)
    pair_ids = jnp.arange(head_width // 2, dtype=jnp.float32)
    base_freq = rope_base ** (-2.0 * pair_ids / head_width)
    wavelength = 2.0 * math.pi / base_freq
    ramp = jnp.clip((ORIG_CTX / wavelength - beta_slow) / (beta_fast - beta_slow), 0.0, 1.0)
    freq = base_freq * (ramp + (1.0 - ramp) / factor)
    mscale = 0.1 * jnp.log(factor) + 1.0
    return (freq, mscale * mscale / math.sqrt(head_width))


def rotate(values_in, positions, freq):
    angle = positions[:, None] * freq[None, :]
    cosine = jnp.cos(angle)[:, None, :]
    sine = jnp.sin(angle)[:, None, :]
    half_width = values_in.shape[2] // 2
    first = values_in[:, :, :half_width].astype(jnp.float32)
    second = values_in[:, :, half_width:].astype(jnp.float32)
    joined = jnp.concatenate(
        [first * cosine - second * sine, second * cosine + first * sine], axis=2
    )
    return joined.astype(jnp.bfloat16)


def lightning_local(q_hat, k_hat, value_linear, logdec):
    tok_rows, head_count, head_width = q_hat.shape
    block_count = tok_rows // BLOCK
    offsets = jnp.arange(BLOCK, dtype=jnp.float32)
    step_gap = offsets[:, None] - offsets[None, :]
    causal = step_gap >= 0
    intra_decay = jnp.where(
        causal[None], jnp.exp(logdec[:, None, None] * jnp.where(causal, step_gap, 0.0)[None]), 0.0
    )
    query_decay = jnp.exp(logdec[None, :] * (offsets[:, None] + 1.0))
    key_decay = jnp.exp(logdec[None, :] * (BLOCK - 1.0 - offsets[:, None]))
    block_decay = jnp.exp(logdec * BLOCK)

    def advance(carry_state, inputs):
        q_block, k_block, v_block = inputs
        scores = jnp.einsum("thd,shd->hts", q_block, k_block, preferred_element_type=jnp.float32)
        weights = (scores * intra_decay).astype(jnp.bfloat16)
        intra_part = jnp.einsum(
            "hts,shd->thd", weights, v_block, preferred_element_type=jnp.float32
        )
        carried = jnp.einsum(
            "thd,hde->the",
            q_block.astype(jnp.float32) * query_decay[:, :, None],
            carry_state,
            precision=lax.Precision.HIGHEST,
        )
        fresh_state = jnp.einsum(
            "thd,the->hde",
            k_block.astype(jnp.float32) * key_decay[:, :, None],
            v_block.astype(jnp.float32),
            precision=lax.Precision.HIGHEST,
        )
        return (carry_state * block_decay[:, None, None] + fresh_state, intra_part + carried)

    def split_blocks(array_in):
        return array_in.reshape(block_count, BLOCK, head_count, head_width)

    zero_state = jnp.zeros((head_count, head_width, head_width), jnp.float32)
    final_state, outputs = lax.scan(
        advance, zero_state, (split_blocks(q_hat), split_blocks(k_hat), split_blocks(value_linear))
    )
    return (final_state, outputs.reshape(tok_rows, head_count, head_width))


def exclusive_scan(slab_state, logdec, tok_rows):
    count = lax.axis_size("ctx")
    shift_one = [(i, i + 1) for i in range(count - 1)]
    running = lax.ppermute(slab_state.astype(jnp.bfloat16), "ctx", shift_one).astype(jnp.float32)
    offset = 1
    while offset < count:
        pairs = [(i, i + offset) for i in range(count - offset)]
        moved = lax.ppermute(running.astype(jnp.bfloat16), "ctx", pairs).astype(jnp.float32)
        scale = jnp.exp(logdec * (tok_rows * offset))
        running = running + moved * scale[:, None, None]
        offset *= 2
    return running


def local(
    query_linear,
    key_linear,
    value_linear,
    gate_logits,
    norm_gain,
    decay_code,
    query_soft,
    key_soft,
    yarn_factor,
):
    tok_rows, head_count, head_width = query_linear.shape
    my_slab = lax.axis_index("ctx")
    freq, logit_scale = yarn_table(yarn_factor, head_width)
    first_row = my_slab * tok_rows
    query_pos = first_row + jnp.arange(tok_rows, dtype=jnp.int32)
    positions = query_pos.astype(jnp.float32)
    query_rot = rotate(query_soft, positions, freq)
    key_rot = rotate(key_soft, positions, freq)
    keys_all = lax.all_gather(key_rot, "ctx", axis=0, tiled=True)

    logdec = jnp.log1p(-decay_code.astype(jnp.float32) * 2.0 ** (-20))
    q_hat = jax.nn.silu(query_linear.astype(jnp.float32)).astype(jnp.bfloat16)
    k_hat = jax.nn.silu(key_linear.astype(jnp.float32)).astype(jnp.bfloat16)
    slab_state, local_out = lightning_local(q_hat, k_hat, value_linear, logdec)
    incoming = exclusive_scan(slab_state, logdec, tok_rows)
    local_pos = jnp.arange(tok_rows, dtype=jnp.float32)
    query_decay = jnp.exp(logdec[None, :] * (local_pos[:, None] + 1.0))
    carried = jnp.einsum(
        "thd,hde->the",
        q_hat.astype(jnp.float32) * query_decay[:, :, None],
        incoming,
        precision=lax.Precision.HIGHEST,
    )
    linear_out = local_out + carried
    square_sum = jnp.sum(linear_out * linear_out, axis=(1, 2))
    total_square = lax.psum(square_sum, "head")
    mean_sq = total_square / (head_count * lax.axis_size("head") * head_width)
    normed = (
        linear_out
        * lax.rsqrt(mean_sq + norm_eps)[:, None, None]
        * norm_gain[None]
        * jax.nn.sigmoid(gate_logits.astype(jnp.float32))
    )
    values_soft = normed.astype(jnp.bfloat16)
    values_all = lax.all_gather(values_soft, "ctx", axis=0, tiled=True)
    piece_rows = keys_all.shape[0]

    scores = (
        jnp.einsum("thd,shd->hts", query_rot, keys_all, preferred_element_type=jnp.float32)
        * logit_scale
    )
    key_pos = jnp.arange(piece_rows, dtype=jnp.int32)
    allowed = key_pos[None, :] <= query_pos[:, None]
    scores = jnp.where(allowed[None], scores, -jnp.inf)
    top = jnp.max(scores, axis=2)
    probs = jnp.exp(scores - top[:, :, None])
    total = jnp.sum(probs, axis=2)
    accum = jnp.einsum(
        "hts,shd->htd", probs.astype(jnp.bfloat16), values_all, preferred_element_type=jnp.float32
    )
    result = accum / total[:, :, None]
    return result.transpose(1, 0, 2).astype(jnp.bfloat16)


def solution(mesh):
    in_specs = (
        P(("groups", "ctx"), "head", None),
        P(("groups", "ctx"), "head", None),
        P(("groups", "ctx"), "head", None),
        P(("groups", "ctx"), "head", None),
        P("head", None),
        P("head"),
        P(("groups", "ctx"), "head", None),
        P(("groups", "ctx"), "head", None),
        P(),
    )
    out_specs = P(("groups", "ctx"), "head", None)
    return jax.shard_map(local, mesh=mesh, in_specs=in_specs, out_specs=out_specs, check_vma=False)
```

```python
import functools
import math

import jax
import numpy as np
import jax.numpy as jnp
from jax import lax
from jax.sharding import PartitionSpec as P

BLOCK = 64
ORIG_CTX = 8192


rope_base = 10000.0
beta_fast = 32.0
beta_slow = 1.0
norm_eps = 1e-05
low_floor = -1e30


def yarn_table(yarn_factor, head_width):
    factor = yarn_factor[0].astype(jnp.float32)
    pair_ids = jnp.arange(head_width // 2, dtype=jnp.float32)
    base_freq = rope_base ** (-2.0 * pair_ids / head_width)
    wavelength = 2.0 * math.pi / base_freq
    ramp = jnp.clip((ORIG_CTX / wavelength - beta_slow) / (beta_fast - beta_slow), 0.0, 1.0)
    freq = base_freq * (ramp + (1.0 - ramp) / factor)
    mscale = 0.1 * jnp.log(factor) + 1.0
    return (freq, mscale * mscale / math.sqrt(head_width))


def rotate(values_in, positions, freq):
    angle = positions[:, None] * freq[None, :]
    cosine = jnp.cos(angle)[:, None, :]
    sine = jnp.sin(angle)[:, None, :]
    half_width = values_in.shape[2] // 2
    first = values_in[:, :, :half_width].astype(jnp.float32)
    second = values_in[:, :, half_width:].astype(jnp.float32)
    joined = jnp.concatenate(
        [first * cosine - second * sine, second * cosine + first * sine], axis=2
    )
    return joined.astype(jnp.bfloat16)


def lightning_local(q_hat, k_hat, value_linear, logdec):
    tok_rows, head_count, head_width = q_hat.shape
    block_count = tok_rows // BLOCK
    offsets = jnp.arange(BLOCK, dtype=jnp.float32)
    step_gap = offsets[:, None] - offsets[None, :]
    causal = step_gap >= 0
    intra_decay = jnp.where(
        causal[None], jnp.exp(logdec[:, None, None] * jnp.where(causal, step_gap, 0.0)[None]), 0.0
    )
    query_decay = jnp.exp(logdec[None, :] * (offsets[:, None] + 1.0))
    key_decay = jnp.exp(logdec[None, :] * (BLOCK - 1.0 - offsets[:, None]))
    block_decay = jnp.exp(logdec * BLOCK)

    def advance(carry_state, inputs):
        q_block, k_block, v_block = inputs
        scores = jnp.einsum("thd,shd->hts", q_block, k_block, preferred_element_type=jnp.float32)
        weights = (scores * intra_decay).astype(jnp.bfloat16)
        intra_part = jnp.einsum(
            "hts,shd->thd", weights, v_block, preferred_element_type=jnp.float32
        )
        carried = jnp.einsum(
            "thd,hde->the",
            q_block.astype(jnp.float32) * query_decay[:, :, None],
            carry_state,
            precision=lax.Precision.HIGHEST,
        )
        fresh_state = jnp.einsum(
            "thd,the->hde",
            k_block.astype(jnp.float32) * key_decay[:, :, None],
            v_block.astype(jnp.float32),
            precision=lax.Precision.HIGHEST,
        )
        return (carry_state * block_decay[:, None, None] + fresh_state, intra_part + carried)

    def split_blocks(array_in):
        return array_in.reshape(block_count, BLOCK, head_count, head_width)

    zero_state = jnp.zeros((head_count, head_width, head_width), jnp.float32)
    final_state, outputs = lax.scan(
        advance, zero_state, (split_blocks(q_hat), split_blocks(k_hat), split_blocks(value_linear))
    )
    return (final_state, outputs.reshape(tok_rows, head_count, head_width))


def exclusive_scan(slab_state, logdec, tok_rows):
    count = lax.axis_size("ctx")
    shift_one = [(i, i + 1) for i in range(count - 1)]
    running = lax.ppermute(slab_state.astype(jnp.bfloat16), "ctx", shift_one).astype(jnp.float32)
    offset = 1
    while offset < count:
        pairs = [(i, i + offset) for i in range(count - offset)]
        moved = lax.ppermute(running.astype(jnp.bfloat16), "ctx", pairs).astype(jnp.float32)
        scale = jnp.exp(logdec * (tok_rows * offset))
        running = running + moved * scale[:, None, None]
        offset *= 2
    return running


def local(
    ring,
    query_linear,
    key_linear,
    value_linear,
    gate_logits,
    norm_gain,
    decay_code,
    query_soft,
    key_soft,
    yarn_factor,
):
    tok_rows, head_count, head_width = query_linear.shape
    my_slab = lax.axis_index("ctx")
    freq, logit_scale = yarn_table(yarn_factor, head_width)
    first_row = my_slab * tok_rows
    query_pos = first_row + jnp.arange(tok_rows, dtype=jnp.int32)
    positions = query_pos.astype(jnp.float32)
    query_rot = rotate(query_soft, positions, freq)
    key_rot = rotate(key_soft, positions, freq)
    keys_all = lax.all_gather(key_rot, "ctx", axis=0, tiled=True)

    logdec = jnp.log1p(-decay_code.astype(jnp.float32) * 2.0 ** (-20))
    q_hat = jax.nn.silu(query_linear.astype(jnp.float32)).astype(jnp.bfloat16)
    k_hat = jax.nn.silu(key_linear.astype(jnp.float32)).astype(jnp.bfloat16)
    slab_state, local_out = lightning_local(q_hat, k_hat, value_linear, logdec)
    incoming = exclusive_scan(slab_state, logdec, tok_rows)
    local_pos = jnp.arange(tok_rows, dtype=jnp.float32)
    query_decay = jnp.exp(logdec[None, :] * (local_pos[:, None] + 1.0))
    carried = jnp.einsum(
        "thd,hde->the",
        q_hat.astype(jnp.float32) * query_decay[:, :, None],
        incoming,
        precision=lax.Precision.HIGHEST,
    )
    linear_out = local_out + carried
    square_sum = jnp.sum(linear_out * linear_out, axis=(1, 2))
    total_square = lax.psum(square_sum, "head")
    mean_sq = total_square / (head_count * lax.axis_size("head") * head_width)
    normed = (
        linear_out
        * lax.rsqrt(mean_sq + norm_eps)[:, None, None]
        * norm_gain[None]
        * jax.nn.sigmoid(gate_logits.astype(jnp.float32))
    )
    values_soft = normed.astype(jnp.bfloat16)
    piece_rows = keys_all.shape[0]
    scores = (
        jnp.einsum("thd,shd->hts", query_rot, keys_all, preferred_element_type=jnp.float32)
        * logit_scale
    )
    key_pos = jnp.arange(piece_rows, dtype=jnp.int32)
    allowed = key_pos[None, :] <= query_pos[:, None]
    scores = jnp.where(allowed[None], scores, -jnp.inf)
    top = jnp.max(scores, axis=2)
    probs = jnp.exp(scores - top[:, :, None])
    total = jnp.sum(probs, axis=2)
    weights = probs.astype(jnp.bfloat16)

    def chunk_of(slab):
        return lax.dynamic_slice_in_dim(weights, slab * tok_rows, tok_rows, axis=2)

    accum = jnp.einsum(
        "hts,shd->htd", chunk_of(my_slab), values_soft, preferred_element_type=jnp.float32
    )
    count = len(ring)
    ring_table = jnp.asarray(ring, jnp.int32)
    spot_table = jnp.asarray(np.argsort(np.asarray(ring)), jnp.int32)
    my_spot = spot_table[my_slab]
    forward = [(ring[i], ring[(i + 1) % count]) for i in range(count)]
    backward = [(ring[i], ring[(i - 1) % count]) for i in range(count)]
    ahead = values_soft
    behind = values_soft
    for step in range(1, count // 2 + 1):
        ahead = lax.ppermute(ahead, "ctx", forward)
        source = ring_table[(my_spot - step) % count]
        accum = accum + jnp.einsum(
            "hts,shd->htd", chunk_of(source), ahead, preferred_element_type=jnp.float32
        )
        if step <= (count - 1) // 2:
            behind = lax.ppermute(behind, "ctx", backward)
            source = ring_table[(my_spot + step) % count]
            accum = accum + jnp.einsum(
                "hts,shd->htd", chunk_of(source), behind, preferred_element_type=jnp.float32
            )
    result = accum / total[:, :, None]
    return result.transpose(1, 0, 2).astype(jnp.bfloat16)


def ring_of(mesh):
    devices = np.moveaxis(np.asarray(mesh.devices), mesh.axis_names.index("ctx"), 0)
    line = devices.reshape(devices.shape[0], -1)[:, 0]
    count = len(line)
    try:
        spots = [tuple(int(v) for v in dev.coords) for dev in line]
    except (AttributeError, TypeError):
        return list(range(count))
    varying = [k for k in range(len(spots[0])) if len({s[k] for s in spots}) > 1]
    if len(varying) != 2:
        return sorted(range(count), key=lambda c: spots[c])
    varying.sort(key=lambda k: len({s[k] for s in spots}))
    outer, inner = varying
    order = []
    for turn, value in enumerate(sorted({s[outer] for s in spots})):
        members = [c for c in range(count) if spots[c][outer] == value]
        members.sort(key=lambda c: spots[c][inner], reverse=turn % 2 == 1)
        order += members
    return order


def solution(mesh):
    in_specs = (
        P(("groups", "ctx"), "head", None),
        P(("groups", "ctx"), "head", None),
        P(("groups", "ctx"), "head", None),
        P(("groups", "ctx"), "head", None),
        P("head", None),
        P("head"),
        P(("groups", "ctx"), "head", None),
        P(("groups", "ctx"), "head", None),
        P(),
    )
    out_specs = P(("groups", "ctx"), "head", None)
    body = functools.partial(local, ring_of(mesh))
    return jax.shard_map(body, mesh=mesh, in_specs=in_specs, out_specs=out_specs, check_vma=False)
```

```python
import functools
import math

import jax
import numpy as np
import jax.numpy as jnp
from jax import lax
from jax.sharding import PartitionSpec as P

BLOCK = 64
ORIG_CTX = 8192


rope_base = 10000.0
beta_fast = 32.0
beta_slow = 1.0
norm_eps = 1e-05
low_floor = -1e30


def yarn_table(yarn_factor, head_width):
    factor = yarn_factor[0].astype(jnp.float32)
    pair_ids = jnp.arange(head_width // 2, dtype=jnp.float32)
    base_freq = rope_base ** (-2.0 * pair_ids / head_width)
    wavelength = 2.0 * math.pi / base_freq
    ramp = jnp.clip((ORIG_CTX / wavelength - beta_slow) / (beta_fast - beta_slow), 0.0, 1.0)
    freq = base_freq * (ramp + (1.0 - ramp) / factor)
    mscale = 0.1 * jnp.log(factor) + 1.0
    return (freq, mscale * mscale / math.sqrt(head_width))


def rotate(values_in, positions, freq):
    angle = positions[:, None] * freq[None, :]
    cosine = jnp.cos(angle)[:, None, :]
    sine = jnp.sin(angle)[:, None, :]
    half_width = values_in.shape[2] // 2
    first = values_in[:, :, :half_width].astype(jnp.float32)
    second = values_in[:, :, half_width:].astype(jnp.float32)
    joined = jnp.concatenate(
        [first * cosine - second * sine, second * cosine + first * sine], axis=2
    )
    return joined.astype(jnp.bfloat16)


def lightning_local(q_hat, k_hat, value_linear, logdec):
    tok_rows, head_count, head_width = q_hat.shape
    block_count = tok_rows // BLOCK
    offsets = jnp.arange(BLOCK, dtype=jnp.float32)
    step_gap = offsets[:, None] - offsets[None, :]
    causal = step_gap >= 0
    intra_decay = jnp.where(
        causal[None], jnp.exp(logdec[:, None, None] * jnp.where(causal, step_gap, 0.0)[None]), 0.0
    )
    query_decay = jnp.exp(logdec[None, :] * (offsets[:, None] + 1.0))
    key_decay = jnp.exp(logdec[None, :] * (BLOCK - 1.0 - offsets[:, None]))
    block_decay = jnp.exp(logdec * BLOCK)

    def advance(carry_state, inputs):
        q_block, k_block, v_block = inputs
        scores = jnp.einsum("thd,shd->hts", q_block, k_block, preferred_element_type=jnp.float32)
        weights = (scores * intra_decay).astype(jnp.bfloat16)
        intra_part = jnp.einsum(
            "hts,shd->thd", weights, v_block, preferred_element_type=jnp.float32
        )
        carried = jnp.einsum(
            "thd,hde->the",
            q_block.astype(jnp.float32) * query_decay[:, :, None],
            carry_state,
            precision=lax.Precision.HIGHEST,
        )
        fresh_state = jnp.einsum(
            "thd,the->hde",
            k_block.astype(jnp.float32) * key_decay[:, :, None],
            v_block.astype(jnp.float32),
            precision=lax.Precision.HIGHEST,
        )
        return (carry_state * block_decay[:, None, None] + fresh_state, intra_part + carried)

    def split_blocks(array_in):
        return array_in.reshape(block_count, BLOCK, head_count, head_width)

    zero_state = jnp.zeros((head_count, head_width, head_width), jnp.float32)
    final_state, outputs = lax.scan(
        advance, zero_state, (split_blocks(q_hat), split_blocks(k_hat), split_blocks(value_linear))
    )
    return (final_state, outputs.reshape(tok_rows, head_count, head_width))


def exclusive_scan(slab_state, logdec, tok_rows):
    count = lax.axis_size("ctx")
    shift_one = [(i, i + 1) for i in range(count - 1)]
    running = lax.ppermute(slab_state.astype(jnp.bfloat16), "ctx", shift_one).astype(jnp.float32)
    offset = 1
    while offset < count:
        pairs = [(i, i + offset) for i in range(count - offset)]
        moved = lax.ppermute(running.astype(jnp.bfloat16), "ctx", pairs).astype(jnp.float32)
        scale = jnp.exp(logdec * (tok_rows * offset))
        running = running + moved * scale[:, None, None]
        offset *= 2
    return running


def local(
    ring,
    query_linear,
    key_linear,
    value_linear,
    gate_logits,
    norm_gain,
    decay_code,
    query_soft,
    key_soft,
    yarn_factor,
):
    tok_rows, head_count, head_width = query_linear.shape
    my_slab = lax.axis_index("ctx")
    freq, logit_scale = yarn_table(yarn_factor, head_width)
    first_row = my_slab * tok_rows
    query_pos = first_row + jnp.arange(tok_rows, dtype=jnp.int32)
    positions = query_pos.astype(jnp.float32)
    query_rot = rotate(query_soft, positions, freq)
    key_rot = rotate(key_soft, positions, freq)
    count = len(ring)
    ring_table = jnp.asarray(ring, jnp.int32)
    spot_table = jnp.asarray(np.argsort(np.asarray(ring)), jnp.int32)
    my_spot = spot_table[my_slab]
    forward = [(ring[i], ring[(i + 1) % count]) for i in range(count)]
    backward = [(ring[i], ring[(i - 1) % count]) for i in range(count)]
    routes = [(None, my_slab)]
    for step in range(1, count // 2 + 1):
        routes.append((("ahead", forward), ring_table[(my_spot - step) % count]))
        if step <= (count - 1) // 2:
            routes.append((("behind", backward), ring_table[(my_spot + step) % count]))

    def score_chunk(keys_in, slab):
        raw = jnp.einsum("thd,shd->hts", query_rot, keys_in, preferred_element_type=jnp.float32)
        key_pos = slab * tok_rows + jnp.arange(tok_rows, dtype=jnp.int32)
        allowed = key_pos[None, :] <= query_pos[:, None]
        return jnp.where(allowed[None], raw * logit_scale, -jnp.inf)

    held = {"ahead": key_rot, "behind": key_rot}
    score_chunks = []
    for route, slab in routes:
        if route is None:
            score_chunks.append(score_chunk(key_rot, slab))
            continue
        name, pairs = route
        held[name] = lax.ppermute(held[name], "ctx", pairs)
        score_chunks.append(score_chunk(held[name], slab))
    top = score_chunks[0].max(axis=2)
    for chunk in score_chunks[1:]:
        top = jnp.maximum(top, chunk.max(axis=2))
    prob_chunks = [jnp.exp(chunk - top[:, :, None]) for chunk in score_chunks]
    total = prob_chunks[0].sum(axis=2)
    for chunk in prob_chunks[1:]:
        total = total + chunk.sum(axis=2)
    weight_chunks = [chunk.astype(jnp.bfloat16) for chunk in prob_chunks]

    logdec = jnp.log1p(-decay_code.astype(jnp.float32) * 2.0 ** (-20))
    q_hat = jax.nn.silu(query_linear.astype(jnp.float32)).astype(jnp.bfloat16)
    k_hat = jax.nn.silu(key_linear.astype(jnp.float32)).astype(jnp.bfloat16)
    slab_state, local_out = lightning_local(q_hat, k_hat, value_linear, logdec)
    incoming = exclusive_scan(slab_state, logdec, tok_rows)
    local_pos = jnp.arange(tok_rows, dtype=jnp.float32)
    query_decay = jnp.exp(logdec[None, :] * (local_pos[:, None] + 1.0))
    carried = jnp.einsum(
        "thd,hde->the",
        q_hat.astype(jnp.float32) * query_decay[:, :, None],
        incoming,
        precision=lax.Precision.HIGHEST,
    )
    linear_out = local_out + carried
    square_sum = jnp.sum(linear_out * linear_out, axis=(1, 2))
    total_square = lax.psum(square_sum, "head")
    mean_sq = total_square / (head_count * lax.axis_size("head") * head_width)
    normed = (
        linear_out
        * lax.rsqrt(mean_sq + norm_eps)[:, None, None]
        * norm_gain[None]
        * jax.nn.sigmoid(gate_logits.astype(jnp.float32))
    )
    values_soft = normed.astype(jnp.bfloat16)
    held = {"ahead": values_soft, "behind": values_soft}
    accum = None
    for (route, slab), weight in zip(routes, weight_chunks):
        if route is None:
            values_in = values_soft
        else:
            name, pairs = route
            held[name] = lax.ppermute(held[name], "ctx", pairs)
            values_in = held[name]
        term = jnp.einsum("hts,shd->htd", weight, values_in, preferred_element_type=jnp.float32)
        accum = term if accum is None else accum + term
    result = accum / total[:, :, None]
    return result.transpose(1, 0, 2).astype(jnp.bfloat16)


def ring_of(mesh):
    devices = np.moveaxis(np.asarray(mesh.devices), mesh.axis_names.index("ctx"), 0)
    line = devices.reshape(devices.shape[0], -1)[:, 0]
    count = len(line)
    try:
        spots = [tuple(int(v) for v in dev.coords) for dev in line]
    except (AttributeError, TypeError):
        return list(range(count))
    varying = [k for k in range(len(spots[0])) if len({s[k] for s in spots}) > 1]
    if len(varying) != 2:
        return sorted(range(count), key=lambda c: spots[c])
    varying.sort(key=lambda k: len({s[k] for s in spots}))
    outer, inner = varying
    order = []
    for turn, value in enumerate(sorted({s[outer] for s in spots})):
        members = [c for c in range(count) if spots[c][outer] == value]
        members.sort(key=lambda c: spots[c][inner], reverse=turn % 2 == 1)
        order += members
    return order


def solution(mesh):
    in_specs = (
        P(("groups", "ctx"), "head", None),
        P(("groups", "ctx"), "head", None),
        P(("groups", "ctx"), "head", None),
        P(("groups", "ctx"), "head", None),
        P("head", None),
        P("head"),
        P(("groups", "ctx"), "head", None),
        P(("groups", "ctx"), "head", None),
        P(),
    )
    out_specs = P(("groups", "ctx"), "head", None)
    body = functools.partial(local, ring_of(mesh))
    return jax.shard_map(body, mesh=mesh, in_specs=in_specs, out_specs=out_specs, check_vma=False)
```

```python
import functools
import math

import jax
import numpy as np
import jax.numpy as jnp
from jax import lax
from jax.sharding import PartitionSpec as P

BLOCK = 64
ORIG_CTX = 8192


rope_base = 10000.0
beta_fast = 32.0
beta_slow = 1.0
norm_eps = 1e-05
low_floor = -1e30


def yarn_table(yarn_factor, head_width):
    factor = yarn_factor[0].astype(jnp.float32)
    pair_ids = jnp.arange(head_width // 2, dtype=jnp.float32)
    base_freq = rope_base ** (-2.0 * pair_ids / head_width)
    wavelength = 2.0 * math.pi / base_freq
    ramp = jnp.clip((ORIG_CTX / wavelength - beta_slow) / (beta_fast - beta_slow), 0.0, 1.0)
    freq = base_freq * (ramp + (1.0 - ramp) / factor)
    mscale = 0.1 * jnp.log(factor) + 1.0
    return (freq, mscale * mscale / math.sqrt(head_width))


def rotate(values_in, positions, freq):
    angle = positions[:, None] * freq[None, :]
    cosine = jnp.cos(angle)[:, None, :]
    sine = jnp.sin(angle)[:, None, :]
    half_width = values_in.shape[2] // 2
    first = values_in[:, :, :half_width].astype(jnp.float32)
    second = values_in[:, :, half_width:].astype(jnp.float32)
    joined = jnp.concatenate(
        [first * cosine - second * sine, second * cosine + first * sine], axis=2
    )
    return joined.astype(jnp.bfloat16)


def lightning_local(q_hat, k_hat, value_linear, logdec):
    tok_rows, head_count, head_width = q_hat.shape
    block_count = tok_rows // BLOCK
    offsets = jnp.arange(BLOCK, dtype=jnp.float32)
    step_gap = offsets[:, None] - offsets[None, :]
    causal = step_gap >= 0
    intra_decay = jnp.where(
        causal[None], jnp.exp(logdec[:, None, None] * jnp.where(causal, step_gap, 0.0)[None]), 0.0
    )
    query_decay = jnp.exp(logdec[None, :] * (offsets[:, None] + 1.0))
    key_decay = jnp.exp(logdec[None, :] * (BLOCK - 1.0 - offsets[:, None]))
    block_decay = jnp.exp(logdec * BLOCK)

    def advance(carry_state, inputs):
        q_block, k_block, v_block = inputs
        scores = jnp.einsum("thd,shd->hts", q_block, k_block, preferred_element_type=jnp.float32)
        weights = (scores * intra_decay).astype(jnp.bfloat16)
        intra_part = jnp.einsum(
            "hts,shd->thd", weights, v_block, preferred_element_type=jnp.float32
        )
        carried = jnp.einsum(
            "thd,hde->the",
            q_block.astype(jnp.float32) * query_decay[:, :, None],
            carry_state,
            precision=lax.Precision.HIGHEST,
        )
        fresh_state = jnp.einsum(
            "thd,the->hde",
            k_block.astype(jnp.float32) * key_decay[:, :, None],
            v_block.astype(jnp.float32),
            precision=lax.Precision.HIGHEST,
        )
        return (carry_state * block_decay[:, None, None] + fresh_state, intra_part + carried)

    def split_blocks(array_in):
        return array_in.reshape(block_count, BLOCK, head_count, head_width)

    zero_state = jnp.zeros((head_count, head_width, head_width), jnp.float32)
    final_state, outputs = lax.scan(
        advance,
        zero_state,
        (split_blocks(q_hat), split_blocks(k_hat), split_blocks(value_linear)),
        unroll=True,
    )
    return (final_state, outputs.reshape(tok_rows, head_count, head_width))


def exclusive_scan(slab_state, logdec, tok_rows):
    count = lax.axis_size("ctx")
    shift_one = [(i, i + 1) for i in range(count - 1)]
    running = lax.ppermute(slab_state.astype(jnp.bfloat16), "ctx", shift_one).astype(jnp.float32)
    offset = 1
    while offset < count:
        pairs = [(i, i + offset) for i in range(count - offset)]
        moved = lax.ppermute(running.astype(jnp.bfloat16), "ctx", pairs).astype(jnp.float32)
        scale = jnp.exp(logdec * (tok_rows * offset))
        running = running + moved * scale[:, None, None]
        offset *= 2
    return running


def local(
    ring,
    query_linear,
    key_linear,
    value_linear,
    gate_logits,
    norm_gain,
    decay_code,
    query_soft,
    key_soft,
    yarn_factor,
):
    tok_rows, head_count, head_width = query_linear.shape
    my_slab = lax.axis_index("ctx")
    freq, logit_scale = yarn_table(yarn_factor, head_width)
    first_row = my_slab * tok_rows
    query_pos = first_row + jnp.arange(tok_rows, dtype=jnp.int32)
    positions = query_pos.astype(jnp.float32)
    query_rot = rotate(query_soft, positions, freq)
    key_rot = rotate(key_soft, positions, freq)
    count = len(ring)
    ring_table = jnp.asarray(ring, jnp.int32)
    spot_table = jnp.asarray(np.argsort(np.asarray(ring)), jnp.int32)
    my_spot = spot_table[my_slab]
    forward = [(ring[i], ring[(i + 1) % count]) for i in range(count)]
    backward = [(ring[i], ring[(i - 1) % count]) for i in range(count)]
    routes = [(None, my_slab)]
    for step in range(1, count // 2 + 1):
        routes.append((("ahead", forward), ring_table[(my_spot - step) % count]))
        if step <= (count - 1) // 2:
            routes.append((("behind", backward), ring_table[(my_spot + step) % count]))

    def score_chunk(keys_in, slab):
        raw = jnp.einsum("thd,shd->hts", query_rot, keys_in, preferred_element_type=jnp.float32)
        key_pos = slab * tok_rows + jnp.arange(tok_rows, dtype=jnp.int32)
        allowed = key_pos[None, :] <= query_pos[:, None]
        return jnp.where(allowed[None], raw * logit_scale, -jnp.inf)

    held = {"ahead": key_rot, "behind": key_rot}
    score_chunks = []
    for route, slab in routes:
        if route is None:
            score_chunks.append(score_chunk(key_rot, slab))
            continue
        name, pairs = route
        held[name] = lax.ppermute(held[name], "ctx", pairs)
        score_chunks.append(score_chunk(held[name], slab))
    top = score_chunks[0].max(axis=2)
    for chunk in score_chunks[1:]:
        top = jnp.maximum(top, chunk.max(axis=2))
    prob_chunks = [jnp.exp(chunk - top[:, :, None]) for chunk in score_chunks]
    total = prob_chunks[0].sum(axis=2)
    for chunk in prob_chunks[1:]:
        total = total + chunk.sum(axis=2)
    weight_chunks = [chunk.astype(jnp.bfloat16) for chunk in prob_chunks]

    logdec = jnp.log1p(-decay_code.astype(jnp.float32) * 2.0 ** (-20))
    q_hat = jax.nn.silu(query_linear.astype(jnp.float32)).astype(jnp.bfloat16)
    k_hat = jax.nn.silu(key_linear.astype(jnp.float32)).astype(jnp.bfloat16)
    slab_state, local_out = lightning_local(q_hat, k_hat, value_linear, logdec)
    incoming = exclusive_scan(slab_state, logdec, tok_rows)
    local_pos = jnp.arange(tok_rows, dtype=jnp.float32)
    query_decay = jnp.exp(logdec[None, :] * (local_pos[:, None] + 1.0))
    carried = jnp.einsum(
        "thd,hde->the",
        q_hat.astype(jnp.float32) * query_decay[:, :, None],
        incoming,
        precision=lax.Precision.HIGHEST,
    )
    linear_out = local_out + carried
    square_sum = jnp.sum(linear_out * linear_out, axis=(1, 2))
    total_square = lax.psum(square_sum, "head")
    mean_sq = total_square / (head_count * lax.axis_size("head") * head_width)
    normed = (
        linear_out
        * lax.rsqrt(mean_sq + norm_eps)[:, None, None]
        * norm_gain[None]
        * jax.nn.sigmoid(gate_logits.astype(jnp.float32))
    )
    values_soft = normed.astype(jnp.bfloat16)
    values_soft, weight_chunks = lax.optimization_barrier((values_soft, weight_chunks))
    held = {"ahead": values_soft, "behind": values_soft}
    accum = None
    for (route, slab), weight in zip(routes, weight_chunks):
        if route is None:
            values_in = values_soft
        else:
            name, pairs = route
            held[name] = lax.ppermute(held[name], "ctx", pairs)
            values_in = held[name]
        term = jnp.einsum("hts,shd->htd", weight, values_in, preferred_element_type=jnp.float32)
        accum = term if accum is None else accum + term
    result = accum / total[:, :, None]
    return result.transpose(1, 0, 2).astype(jnp.bfloat16)


def ring_of(mesh):
    devices = np.moveaxis(np.asarray(mesh.devices), mesh.axis_names.index("ctx"), 0)
    line = devices.reshape(devices.shape[0], -1)[:, 0]
    count = len(line)
    try:
        spots = [tuple(int(v) for v in dev.coords) for dev in line]
    except (AttributeError, TypeError):
        return list(range(count))
    varying = [k for k in range(len(spots[0])) if len({s[k] for s in spots}) > 1]
    if len(varying) != 2:
        return sorted(range(count), key=lambda c: spots[c])
    varying.sort(key=lambda k: len({s[k] for s in spots}))
    outer, inner = varying
    order = []
    for turn, value in enumerate(sorted({s[outer] for s in spots})):
        members = [c for c in range(count) if spots[c][outer] == value]
        members.sort(key=lambda c: spots[c][inner], reverse=turn % 2 == 1)
        order += members
    return order


def solution(mesh):
    in_specs = (
        P(("groups", "ctx"), "head", None),
        P(("groups", "ctx"), "head", None),
        P(("groups", "ctx"), "head", None),
        P(("groups", "ctx"), "head", None),
        P("head", None),
        P("head"),
        P(("groups", "ctx"), "head", None),
        P(("groups", "ctx"), "head", None),
        P(),
    )
    out_specs = P(("groups", "ctx"), "head", None)
    body = functools.partial(local, ring_of(mesh))
    return jax.shard_map(body, mesh=mesh, in_specs=in_specs, out_specs=out_specs, check_vma=False)
```

```python
import functools
import math

import jax
import numpy as np
import jax.numpy as jnp
from jax import lax
from jax.sharding import PartitionSpec as P

BLOCK = 64
ORIG_CTX = 8192


rope_base = 10000.0
beta_fast = 32.0
beta_slow = 1.0
norm_eps = 1e-05
low_floor = -1e30


def yarn_table(yarn_factor, head_width):
    factor = yarn_factor[0].astype(jnp.float32)
    pair_ids = jnp.arange(head_width // 2, dtype=jnp.float32)
    base_freq = rope_base ** (-2.0 * pair_ids / head_width)
    wavelength = 2.0 * math.pi / base_freq
    ramp = jnp.clip((ORIG_CTX / wavelength - beta_slow) / (beta_fast - beta_slow), 0.0, 1.0)
    freq = base_freq * (ramp + (1.0 - ramp) / factor)
    mscale = 0.1 * jnp.log(factor) + 1.0
    return (freq, mscale * mscale / math.sqrt(head_width))


def rotate(values_in, positions, freq):
    angle = positions[:, None] * freq[None, :]
    cosine = jnp.cos(angle)[:, None, :]
    sine = jnp.sin(angle)[:, None, :]
    half_width = values_in.shape[2] // 2
    first = values_in[:, :, :half_width].astype(jnp.float32)
    second = values_in[:, :, half_width:].astype(jnp.float32)
    joined = jnp.concatenate(
        [first * cosine - second * sine, second * cosine + first * sine], axis=2
    )
    return joined.astype(jnp.bfloat16)


def lightning_local(q_hat, k_hat, value_linear, logdec):
    tok_rows, head_count, head_width = q_hat.shape
    block_count = tok_rows // BLOCK
    offsets = jnp.arange(BLOCK, dtype=jnp.float32)
    step_gap = offsets[:, None] - offsets[None, :]
    causal = step_gap >= 0
    intra_decay = jnp.where(
        causal[None], jnp.exp(logdec[:, None, None] * jnp.where(causal, step_gap, 0.0)[None]), 0.0
    )
    query_decay = jnp.exp(logdec[None, :] * (offsets[:, None] + 1.0))
    key_decay = jnp.exp(logdec[None, :] * (BLOCK - 1.0 - offsets[:, None]))
    block_decay = jnp.exp(logdec * BLOCK)

    def advance(carry_state, inputs):
        q_block, k_block, v_block = inputs
        scores = jnp.einsum("thd,shd->hts", q_block, k_block, preferred_element_type=jnp.float32)
        weights = (scores * intra_decay).astype(jnp.bfloat16)
        intra_part = jnp.einsum(
            "hts,shd->thd", weights, v_block, preferred_element_type=jnp.float32
        )
        carried = jnp.einsum(
            "thd,hde->the",
            q_block.astype(jnp.float32) * query_decay[:, :, None],
            carry_state,
            precision=lax.Precision.HIGHEST,
        )
        fresh_state = jnp.einsum(
            "thd,the->hde",
            k_block.astype(jnp.float32) * key_decay[:, :, None],
            v_block.astype(jnp.float32),
            precision=lax.Precision.HIGHEST,
        )
        return (carry_state * block_decay[:, None, None] + fresh_state, intra_part + carried)

    def split_blocks(array_in):
        return array_in.reshape(block_count, BLOCK, head_count, head_width)

    zero_state = jnp.zeros((head_count, head_width, head_width), jnp.float32)
    final_state, outputs = lax.scan(
        advance,
        zero_state,
        (split_blocks(q_hat), split_blocks(k_hat), split_blocks(value_linear)),
        unroll=True,
    )
    return (final_state, outputs.reshape(tok_rows, head_count, head_width))


def exclusive_scan(slab_state, logdec, tok_rows):
    count = lax.axis_size("ctx")
    shift_one = [(i, i + 1) for i in range(count - 1)]
    running = lax.ppermute(slab_state.astype(jnp.bfloat16), "ctx", shift_one).astype(jnp.float32)
    offset = 1
    while offset < count:
        pairs = [(i, i + offset) for i in range(count - offset)]
        moved = lax.ppermute(running.astype(jnp.bfloat16), "ctx", pairs).astype(jnp.float32)
        scale = jnp.exp(logdec * (tok_rows * offset))
        running = running + moved * scale[:, None, None]
        offset *= 2
    return running


def local(
    ring,
    query_linear,
    key_linear,
    value_linear,
    gate_logits,
    norm_gain,
    decay_code,
    query_soft,
    key_soft,
    yarn_factor,
):
    tok_rows, head_count, head_width = query_linear.shape
    my_slab = lax.axis_index("ctx")
    freq, logit_scale = yarn_table(yarn_factor, head_width)
    first_row = my_slab * tok_rows
    query_pos = first_row + jnp.arange(tok_rows, dtype=jnp.int32)
    positions = query_pos.astype(jnp.float32)
    query_rot = rotate(query_soft, positions, freq)
    key_rot = rotate(key_soft, positions, freq)
    count = len(ring)
    ring_table = jnp.asarray(ring, jnp.int32)
    spot_table = jnp.asarray(np.argsort(np.asarray(ring)), jnp.int32)
    my_spot = spot_table[my_slab]
    forward = [(ring[i], ring[(i + 1) % count]) for i in range(count)]
    backward = [(ring[i], ring[(i - 1) % count]) for i in range(count)]
    steps = []
    for step in range(1, count // 2 + 1):
        moves = [("ahead", forward, ring_table[(my_spot - step) % count])]
        if step <= (count - 1) // 2:
            moves.append(("behind", backward, ring_table[(my_spot + step) % count]))
        steps.append(moves)

    def score_chunk(keys_in, slab):
        raw = jnp.einsum("thd,shd->hts", query_rot, keys_in, preferred_element_type=jnp.float32)
        key_pos = slab * tok_rows + jnp.arange(tok_rows, dtype=jnp.int32)
        allowed = key_pos[None, :] <= query_pos[:, None]
        return jnp.where(allowed[None], raw * logit_scale, -jnp.inf)

    held = {"ahead": key_rot, "behind": key_rot}
    score_chunks = [score_chunk(key_rot, my_slab)]

    def key_step(moves):
        for name, pairs, slab in moves:
            held[name] = lax.ppermute(held[name], "ctx", pairs)
            score_chunks.append(score_chunk(held[name], slab))

    early = (len(steps) + 1) // 2
    for moves in steps[:early]:
        key_step(moves)
    logdec = jnp.log1p(-decay_code.astype(jnp.float32) * 2.0 ** (-20))
    q_hat = jax.nn.silu(query_linear.astype(jnp.float32)).astype(jnp.bfloat16)
    k_hat = jax.nn.silu(key_linear.astype(jnp.float32)).astype(jnp.bfloat16)
    slab_state, local_out = lightning_local(q_hat, k_hat, value_linear, logdec)
    ring_keys = (held["ahead"], held["behind"])
    ring_keys, slab_state = lax.optimization_barrier((ring_keys, slab_state))
    held["ahead"], held["behind"] = ring_keys
    incoming = exclusive_scan(slab_state, logdec, tok_rows)
    ring_keys = (held["ahead"], held["behind"])
    ring_keys, incoming = lax.optimization_barrier((ring_keys, incoming))
    held["ahead"], held["behind"] = ring_keys
    for moves in steps[early:]:
        key_step(moves)
    local_pos = jnp.arange(tok_rows, dtype=jnp.float32)
    query_decay = jnp.exp(logdec[None, :] * (local_pos[:, None] + 1.0))
    carried = jnp.einsum(
        "thd,hde->the",
        q_hat.astype(jnp.float32) * query_decay[:, :, None],
        incoming,
        precision=lax.Precision.HIGHEST,
    )
    linear_out = local_out + carried
    square_sum = jnp.sum(linear_out * linear_out, axis=(1, 2))
    total_square = lax.psum(square_sum, "head")
    mean_sq = total_square / (head_count * lax.axis_size("head") * head_width)
    normed = (
        linear_out
        * lax.rsqrt(mean_sq + norm_eps)[:, None, None]
        * norm_gain[None]
        * jax.nn.sigmoid(gate_logits.astype(jnp.float32))
    )
    values_soft = normed.astype(jnp.bfloat16)
    ring_keys = (held["ahead"], held["behind"])
    ring_keys, values_soft = lax.optimization_barrier((ring_keys, values_soft))
    top = score_chunks[0].max(axis=2)
    for chunk in score_chunks[1:]:
        top = jnp.maximum(top, chunk.max(axis=2))
    prob_chunks = [jnp.exp(chunk - top[:, :, None]) for chunk in score_chunks]
    total = prob_chunks[0].sum(axis=2)
    for chunk in prob_chunks[1:]:
        total = total + chunk.sum(axis=2)
    weight_chunks = [chunk.astype(jnp.bfloat16) for chunk in prob_chunks]

    held = {"ahead": values_soft, "behind": values_soft}
    accum = jnp.einsum(
        "hts,shd->htd", weight_chunks[0], values_soft, preferred_element_type=jnp.float32
    )
    chunk_at = 1
    for moves in steps:
        for name, pairs, slab in moves:
            held[name] = lax.ppermute(held[name], "ctx", pairs)
            accum = accum + jnp.einsum(
                "hts,shd->htd",
                weight_chunks[chunk_at],
                held[name],
                preferred_element_type=jnp.float32,
            )
            chunk_at += 1
    result = accum / total[:, :, None]
    return result.transpose(1, 0, 2).astype(jnp.bfloat16)


def ring_of(mesh):
    devices = np.moveaxis(np.asarray(mesh.devices), mesh.axis_names.index("ctx"), 0)
    line = devices.reshape(devices.shape[0], -1)[:, 0]
    count = len(line)
    try:
        spots = [tuple(int(v) for v in dev.coords) for dev in line]
    except (AttributeError, TypeError):
        return list(range(count))
    varying = [k for k in range(len(spots[0])) if len({s[k] for s in spots}) > 1]
    if len(varying) != 2:
        return sorted(range(count), key=lambda c: spots[c])
    varying.sort(key=lambda k: len({s[k] for s in spots}))
    outer, inner = varying
    order = []
    for turn, value in enumerate(sorted({s[outer] for s in spots})):
        members = [c for c in range(count) if spots[c][outer] == value]
        members.sort(key=lambda c: spots[c][inner], reverse=turn % 2 == 1)
        order += members
    return order


def solution(mesh):
    in_specs = (
        P(("groups", "ctx"), "head", None),
        P(("groups", "ctx"), "head", None),
        P(("groups", "ctx"), "head", None),
        P(("groups", "ctx"), "head", None),
        P("head", None),
        P("head"),
        P(("groups", "ctx"), "head", None),
        P(("groups", "ctx"), "head", None),
        P(),
    )
    out_specs = P(("groups", "ctx"), "head", None)
    body = functools.partial(local, ring_of(mesh))
    return jax.shard_map(body, mesh=mesh, in_specs=in_specs, out_specs=out_specs, check_vma=False)
```

```python
import functools
import math

import jax
import numpy as np
import jax.numpy as jnp
from jax import lax
from jax.sharding import PartitionSpec as P

BLOCK = 64
ORIG_CTX = 8192


rope_base = 10000.0
beta_fast = 32.0
beta_slow = 1.0
norm_eps = 1e-05
low_floor = -1e30


def yarn_table(yarn_factor, head_width):
    factor = yarn_factor[0].astype(jnp.float32)
    pair_ids = jnp.arange(head_width // 2, dtype=jnp.float32)
    base_freq = rope_base ** (-2.0 * pair_ids / head_width)
    wavelength = 2.0 * math.pi / base_freq
    ramp = jnp.clip((ORIG_CTX / wavelength - beta_slow) / (beta_fast - beta_slow), 0.0, 1.0)
    freq = base_freq * (ramp + (1.0 - ramp) / factor)
    mscale = 0.1 * jnp.log(factor) + 1.0
    return (freq, mscale * mscale / math.sqrt(head_width))


def rotate(values_in, positions, freq):
    angle = positions[:, None] * freq[None, :]
    cosine = jnp.cos(angle)[:, None, :]
    sine = jnp.sin(angle)[:, None, :]
    half_width = values_in.shape[2] // 2
    first = values_in[:, :, :half_width].astype(jnp.float32)
    second = values_in[:, :, half_width:].astype(jnp.float32)
    joined = jnp.concatenate(
        [first * cosine - second * sine, second * cosine + first * sine], axis=2
    )
    return joined.astype(jnp.bfloat16)


def lightning_local(q_hat, k_hat, value_linear, logdec):
    tok_rows, head_count, head_width = q_hat.shape
    block_count = tok_rows // BLOCK
    offsets = jnp.arange(BLOCK, dtype=jnp.float32)
    step_gap = offsets[:, None] - offsets[None, :]
    causal = step_gap >= 0
    intra_decay = jnp.where(
        causal[None], jnp.exp(logdec[:, None, None] * jnp.where(causal, step_gap, 0.0)[None]), 0.0
    )
    query_decay = jnp.exp(logdec[None, :] * (offsets[:, None] + 1.0))
    key_decay = jnp.exp(logdec[None, :] * (BLOCK - 1.0 - offsets[:, None]))
    block_decay = jnp.exp(logdec * BLOCK)

    def advance(carry_state, inputs):
        q_block, k_block, v_block = inputs
        scores = jnp.einsum("thd,shd->hts", q_block, k_block, preferred_element_type=jnp.float32)
        weights = (scores * intra_decay).astype(jnp.bfloat16)
        intra_part = jnp.einsum(
            "hts,shd->thd", weights, v_block, preferred_element_type=jnp.float32
        )
        carried = query_decay[:, :, None] * split_dot("thd,hde->the", q_block, carry_state)
        fresh_state = split_dot(
            "thd,the->hde", k_block, key_decay[:, :, None] * v_block.astype(jnp.float32)
        )
        return (carry_state * block_decay[:, None, None] + fresh_state, intra_part + carried)

    def split_blocks(array_in):
        return array_in.reshape(block_count, BLOCK, head_count, head_width)

    zero_state = jnp.zeros((head_count, head_width, head_width), jnp.float32)
    final_state, outputs = lax.scan(
        advance,
        zero_state,
        (split_blocks(q_hat), split_blocks(k_hat), split_blocks(value_linear)),
        unroll=True,
    )
    return (final_state, outputs.reshape(tok_rows, head_count, head_width))


def exclusive_scan(slab_state, logdec, tok_rows):
    count = lax.axis_size("ctx")
    decay = jnp.exp(logdec * tok_rows)[:, None, None]
    sent = slab_state.astype(jnp.bfloat16)
    running = lax.ppermute(sent, "ctx", [(i, i + 1) for i in range(count - 1)]).astype(jnp.float32)
    if count > 2:
        two_back = lax.ppermute(sent, "ctx", [(i, i + 2) for i in range(count - 2)])
        running = running + two_back.astype(jnp.float32) * decay
    offset = 2
    while offset < count:
        pairs = [(i, i + offset) for i in range(count - offset)]
        moved = lax.ppermute(running.astype(jnp.bfloat16), "ctx", pairs).astype(jnp.float32)
        scale = jnp.exp(logdec * (tok_rows * offset))
        running = running + moved * scale[:, None, None]
        offset *= 2
    return running


def split_dot(spec, exact, wide):
    high = wide.astype(jnp.bfloat16)
    low = (wide - high.astype(jnp.float32)).astype(jnp.bfloat16)
    first = jnp.einsum(spec, exact, high, preferred_element_type=jnp.float32)
    return first + jnp.einsum(spec, exact, low, preferred_element_type=jnp.float32)


def local(
    ring,
    query_linear,
    key_linear,
    value_linear,
    gate_logits,
    norm_gain,
    decay_code,
    query_soft,
    key_soft,
    yarn_factor,
):
    tok_rows, head_count, head_width = query_linear.shape
    my_slab = lax.axis_index("ctx")
    freq, logit_scale = yarn_table(yarn_factor, head_width)
    first_row = my_slab * tok_rows
    query_pos = first_row + jnp.arange(tok_rows, dtype=jnp.int32)
    positions = query_pos.astype(jnp.float32)
    query_rot = rotate(query_soft, positions, freq)
    key_rot = rotate(key_soft, positions, freq)
    count = len(ring)
    ring_table = jnp.asarray(ring, jnp.int32)
    spot_table = jnp.asarray(np.argsort(np.asarray(ring)), jnp.int32)
    my_spot = spot_table[my_slab]
    forward = [(ring[i], ring[(i + 1) % count]) for i in range(count)]
    backward = [(ring[i], ring[(i - 1) % count]) for i in range(count)]
    steps = []
    for step in range(1, count // 2 + 1):
        moves = [("ahead", forward, ring_table[(my_spot - step) % count])]
        if step <= (count - 1) // 2:
            moves.append(("behind", backward, ring_table[(my_spot + step) % count]))
        steps.append(moves)

    def score_chunk(keys_in, slab):
        raw = jnp.einsum("thd,shd->hts", query_rot, keys_in, preferred_element_type=jnp.float32)
        key_pos = slab * tok_rows + jnp.arange(tok_rows, dtype=jnp.int32)
        allowed = key_pos[None, :] <= query_pos[:, None]
        return jnp.where(allowed[None], raw * logit_scale, -jnp.inf)

    held = {"ahead": key_rot, "behind": key_rot}
    score_chunks = [score_chunk(key_rot, my_slab)]

    def key_step(moves):
        for name, pairs, slab in moves:
            held[name] = lax.ppermute(held[name], "ctx", pairs)
            score_chunks.append(score_chunk(held[name], slab))

    early = (len(steps) + 1) // 2
    for moves in steps[:early]:
        key_step(moves)
    logdec = jnp.log1p(-decay_code.astype(jnp.float32) * 2.0 ** (-20))
    q_hat = jax.nn.silu(query_linear.astype(jnp.float32)).astype(jnp.bfloat16)
    k_hat = jax.nn.silu(key_linear.astype(jnp.float32)).astype(jnp.bfloat16)
    slab_state, local_out = lightning_local(q_hat, k_hat, value_linear, logdec)
    ring_keys = (held["ahead"], held["behind"])
    ring_keys, slab_state = lax.optimization_barrier((ring_keys, slab_state))
    held["ahead"], held["behind"] = ring_keys
    incoming = exclusive_scan(slab_state, logdec, tok_rows)
    ring_keys = (held["ahead"], held["behind"])
    ring_keys, incoming = lax.optimization_barrier((ring_keys, incoming))
    held["ahead"], held["behind"] = ring_keys
    for moves in steps[early:]:
        key_step(moves)
    local_pos = jnp.arange(tok_rows, dtype=jnp.float32)
    query_decay = jnp.exp(logdec[None, :] * (local_pos[:, None] + 1.0))
    carried = query_decay[:, :, None] * split_dot("thd,hde->the", q_hat, incoming)
    linear_out = local_out + carried
    square_sum = jnp.sum(linear_out * linear_out, axis=(1, 2))
    total_square = lax.psum(square_sum, "head")
    mean_sq = total_square / (head_count * lax.axis_size("head") * head_width)
    normed = (
        linear_out
        * lax.rsqrt(mean_sq + norm_eps)[:, None, None]
        * norm_gain[None]
        * jax.nn.sigmoid(gate_logits.astype(jnp.float32))
    )
    values_soft = normed.astype(jnp.bfloat16)
    ring_keys = (held["ahead"], held["behind"])
    ring_keys, values_soft = lax.optimization_barrier((ring_keys, values_soft))
    top = score_chunks[0].max(axis=2)
    for chunk in score_chunks[1:]:
        top = jnp.maximum(top, chunk.max(axis=2))
    prob_chunks = [jnp.exp(chunk - top[:, :, None]) for chunk in score_chunks]
    total = prob_chunks[0].sum(axis=2)
    for chunk in prob_chunks[1:]:
        total = total + chunk.sum(axis=2)
    weight_chunks = [chunk.astype(jnp.bfloat16) for chunk in prob_chunks]

    held = {"ahead": values_soft, "behind": values_soft}
    accum = jnp.einsum(
        "hts,shd->htd", weight_chunks[0], values_soft, preferred_element_type=jnp.float32
    )
    chunk_at = 1
    for moves in steps:
        for name, pairs, slab in moves:
            held[name] = lax.ppermute(held[name], "ctx", pairs)
            accum = accum + jnp.einsum(
                "hts,shd->htd",
                weight_chunks[chunk_at],
                held[name],
                preferred_element_type=jnp.float32,
            )
            chunk_at += 1
    result = accum / total[:, :, None]
    return result.transpose(1, 0, 2).astype(jnp.bfloat16)


def ring_of(mesh):
    devices = np.moveaxis(np.asarray(mesh.devices), mesh.axis_names.index("ctx"), 0)
    line = devices.reshape(devices.shape[0], -1)[:, 0]
    count = len(line)
    try:
        spots = [tuple(int(v) for v in dev.coords) for dev in line]
    except (AttributeError, TypeError):
        return list(range(count))
    varying = [k for k in range(len(spots[0])) if len({s[k] for s in spots}) > 1]
    if len(varying) != 2:
        return sorted(range(count), key=lambda c: spots[c])
    varying.sort(key=lambda k: len({s[k] for s in spots}))
    outer, inner = varying
    order = []
    for turn, value in enumerate(sorted({s[outer] for s in spots})):
        members = [c for c in range(count) if spots[c][outer] == value]
        members.sort(key=lambda c: spots[c][inner], reverse=turn % 2 == 1)
        order += members
    return order


def solution(mesh):
    in_specs = (
        P(("groups", "ctx"), "head", None),
        P(("groups", "ctx"), "head", None),
        P(("groups", "ctx"), "head", None),
        P(("groups", "ctx"), "head", None),
        P("head", None),
        P("head"),
        P(("groups", "ctx"), "head", None),
        P(("groups", "ctx"), "head", None),
        P(),
    )
    out_specs = P(("groups", "ctx"), "head", None)
    body = functools.partial(local, ring_of(mesh))
    return jax.shard_map(body, mesh=mesh, in_specs=in_specs, out_specs=out_specs, check_vma=False)
```

```python
import functools
import math

import jax
import numpy as np
import jax.numpy as jnp
from jax import lax
from jax.sharding import PartitionSpec as P

BLOCK = 64
ORIG_CTX = 8192


rope_base = 10000.0
beta_fast = 32.0
beta_slow = 1.0
norm_eps = 1e-05
low_floor = -1e30


def yarn_table(yarn_factor, head_width):
    factor = yarn_factor[0].astype(jnp.float32)
    pair_ids = jnp.arange(head_width // 2, dtype=jnp.float32)
    base_freq = rope_base ** (-2.0 * pair_ids / head_width)
    wavelength = 2.0 * math.pi / base_freq
    ramp = jnp.clip((ORIG_CTX / wavelength - beta_slow) / (beta_fast - beta_slow), 0.0, 1.0)
    freq = base_freq * (ramp + (1.0 - ramp) / factor)
    mscale = 0.1 * jnp.log(factor) + 1.0
    return (freq, mscale * mscale / math.sqrt(head_width))


def rotate(values_in, positions, freq):
    angle = positions[:, None] * freq[None, :]
    cosine = jnp.cos(angle)[:, None, :]
    sine = jnp.sin(angle)[:, None, :]
    half_width = values_in.shape[2] // 2
    first = values_in[:, :, :half_width].astype(jnp.float32)
    second = values_in[:, :, half_width:].astype(jnp.float32)
    joined = jnp.concatenate(
        [first * cosine - second * sine, second * cosine + first * sine], axis=2
    )
    return joined.astype(jnp.bfloat16)


def lightning_local(q_hat, k_hat, value_linear, logdec):
    tok_rows, head_count, head_width = q_hat.shape
    block_count = tok_rows // BLOCK
    offsets = jnp.arange(BLOCK, dtype=jnp.float32)
    step_gap = offsets[:, None] - offsets[None, :]
    causal = step_gap >= 0
    intra_decay = jnp.where(
        causal[None], jnp.exp(logdec[:, None, None] * jnp.where(causal, step_gap, 0.0)[None]), 0.0
    )
    query_decay = jnp.exp(logdec[None, :] * (offsets[:, None] + 1.0))
    key_decay = jnp.exp(logdec[None, :] * (BLOCK - 1.0 - offsets[:, None]))
    block_decay = jnp.exp(logdec * BLOCK)

    def advance(carry_state, inputs):
        q_block, k_block, v_block = inputs
        scores = jnp.einsum("thd,shd->hts", q_block, k_block, preferred_element_type=jnp.float32)
        weights = (scores * intra_decay).astype(jnp.bfloat16)
        intra_part = jnp.einsum(
            "hts,shd->thd", weights, v_block, preferred_element_type=jnp.float32
        )
        carried = query_decay[:, :, None] * split_dot("thd,hde->the", q_block, carry_state)
        fresh_state = split_dot(
            "thd,the->hde", k_block, key_decay[:, :, None] * v_block.astype(jnp.float32)
        )
        return (carry_state * block_decay[:, None, None] + fresh_state, intra_part + carried)

    def split_blocks(array_in):
        return array_in.reshape(block_count, BLOCK, head_count, head_width)

    zero_state = jnp.zeros((head_count, head_width, head_width), jnp.float32)
    final_state, outputs = lax.scan(
        advance,
        zero_state,
        (split_blocks(q_hat), split_blocks(k_hat), split_blocks(value_linear)),
        unroll=True,
    )
    return (final_state, outputs.reshape(tok_rows, head_count, head_width))


def exclusive_scan(slab_state, logdec, tok_rows):
    count = lax.axis_size("ctx")
    decay = jnp.exp(logdec * tok_rows)[:, None, None]
    sent = slab_state.astype(jnp.bfloat16)
    running = lax.ppermute(sent, "ctx", [(i, i + 1) for i in range(count - 1)]).astype(jnp.float32)
    if count > 2:
        two_back = lax.ppermute(sent, "ctx", [(i, i + 2) for i in range(count - 2)])
        running = running + two_back.astype(jnp.float32) * decay
    offset = 2
    while offset < count:
        pairs = [(i, i + offset) for i in range(count - offset)]
        moved = lax.ppermute(running.astype(jnp.bfloat16), "ctx", pairs).astype(jnp.float32)
        scale = jnp.exp(logdec * (tok_rows * offset))
        running = running + moved * scale[:, None, None]
        offset *= 2
    return running


def split_dot(spec, exact, wide):
    high = wide.astype(jnp.bfloat16)
    low = (wide - high.astype(jnp.float32)).astype(jnp.bfloat16)
    first = jnp.einsum(spec, exact, high, preferred_element_type=jnp.float32)
    return first + jnp.einsum(spec, exact, low, preferred_element_type=jnp.float32)


def local(
    ring,
    query_linear,
    key_linear,
    value_linear,
    gate_logits,
    norm_gain,
    decay_code,
    query_soft,
    key_soft,
    yarn_factor,
):
    tok_rows, head_count, head_width = query_linear.shape
    my_slab = lax.axis_index("ctx")
    freq, logit_scale = yarn_table(yarn_factor, head_width)
    first_row = my_slab * tok_rows
    query_pos = first_row + jnp.arange(tok_rows, dtype=jnp.int32)
    positions = query_pos.astype(jnp.float32)
    query_rot = rotate(query_soft, positions, freq)
    key_rot = rotate(key_soft, positions, freq)
    count = len(ring)
    ring_table = jnp.asarray(ring, jnp.int32)
    spot_table = jnp.asarray(np.argsort(np.asarray(ring)), jnp.int32)
    my_spot = spot_table[my_slab]
    forward = [(ring[i], ring[(i + 1) % count]) for i in range(count)]
    backward = [(ring[i], ring[(i - 1) % count]) for i in range(count)]
    steps = []
    for step in range(1, count // 2 + 1):
        moves = [("ahead", forward, ring_table[(my_spot - step) % count])]
        if step <= (count - 1) // 2:
            moves.append(("behind", backward, ring_table[(my_spot + step) % count]))
        steps.append(moves)

    def score_chunk(keys_in, slab):
        raw = jnp.einsum("thd,shd->hts", query_rot, keys_in, preferred_element_type=jnp.float32)
        key_pos = slab * tok_rows + jnp.arange(tok_rows, dtype=jnp.int32)
        allowed = key_pos[None, :] <= query_pos[:, None]
        return jnp.where(allowed[None], raw * logit_scale, -jnp.inf)

    held = {"ahead": key_rot, "behind": key_rot}
    score_chunks = [score_chunk(key_rot, my_slab)]

    def key_step(moves):
        for name, pairs, slab in moves:
            held[name] = lax.ppermute(held[name], "ctx", pairs)
            score_chunks.append(score_chunk(held[name], slab))

    early = (len(steps) + 1) // 2
    for moves in steps[:early]:
        key_step(moves)
    logdec = jnp.log1p(-decay_code.astype(jnp.float32) * 2.0 ** (-20))
    q_hat = jax.nn.silu(query_linear.astype(jnp.float32)).astype(jnp.bfloat16)
    k_hat = jax.nn.silu(key_linear.astype(jnp.float32)).astype(jnp.bfloat16)
    slab_state, local_out = lightning_local(q_hat, k_hat, value_linear, logdec)
    ring_keys = (held["ahead"], held["behind"])
    ring_keys, slab_state = lax.optimization_barrier((ring_keys, slab_state))
    held["ahead"], held["behind"] = ring_keys
    for moves in steps[early:]:
        key_step(moves)
    incoming = exclusive_scan(slab_state, logdec, tok_rows)
    local_pos = jnp.arange(tok_rows, dtype=jnp.float32)
    query_decay = jnp.exp(logdec[None, :] * (local_pos[:, None] + 1.0))
    carried = query_decay[:, :, None] * split_dot("thd,hde->the", q_hat, incoming)
    linear_out = local_out + carried
    square_sum = jnp.sum(linear_out * linear_out, axis=(1, 2))
    total_square = lax.psum(square_sum, "head")
    mean_sq = total_square / (head_count * lax.axis_size("head") * head_width)
    normed = (
        linear_out
        * lax.rsqrt(mean_sq + norm_eps)[:, None, None]
        * norm_gain[None]
        * jax.nn.sigmoid(gate_logits.astype(jnp.float32))
    )
    values_soft = normed.astype(jnp.bfloat16)
    ring_keys = (held["ahead"], held["behind"])
    ring_keys, values_soft = lax.optimization_barrier((ring_keys, values_soft))
    top = score_chunks[0].max(axis=2)
    for chunk in score_chunks[1:]:
        top = jnp.maximum(top, chunk.max(axis=2))
    prob_chunks = [jnp.exp(chunk - top[:, :, None]) for chunk in score_chunks]
    total = prob_chunks[0].sum(axis=2)
    for chunk in prob_chunks[1:]:
        total = total + chunk.sum(axis=2)
    weight_chunks = [chunk.astype(jnp.bfloat16) for chunk in prob_chunks]

    held = {"ahead": values_soft, "behind": values_soft}
    accum = jnp.einsum(
        "hts,shd->htd", weight_chunks[0], values_soft, preferred_element_type=jnp.float32
    )
    chunk_at = 1
    for moves in steps:
        for name, pairs, slab in moves:
            held[name] = lax.ppermute(held[name], "ctx", pairs)
            accum = accum + jnp.einsum(
                "hts,shd->htd",
                weight_chunks[chunk_at],
                held[name],
                preferred_element_type=jnp.float32,
            )
            chunk_at += 1
    result = accum / total[:, :, None]
    return result.transpose(1, 0, 2).astype(jnp.bfloat16)


def ring_of(mesh):
    devices = np.moveaxis(np.asarray(mesh.devices), mesh.axis_names.index("ctx"), 0)
    line = devices.reshape(devices.shape[0], -1)[:, 0]
    count = len(line)
    try:
        spots = [tuple(int(v) for v in dev.coords) for dev in line]
    except (AttributeError, TypeError):
        return list(range(count))
    varying = [k for k in range(len(spots[0])) if len({s[k] for s in spots}) > 1]
    if len(varying) != 2:
        return sorted(range(count), key=lambda c: spots[c])
    varying.sort(key=lambda k: len({s[k] for s in spots}))
    outer, inner = varying
    order = []
    for turn, value in enumerate(sorted({s[outer] for s in spots})):
        members = [c for c in range(count) if spots[c][outer] == value]
        members.sort(key=lambda c: spots[c][inner], reverse=turn % 2 == 1)
        order += members
    return order


def solution(mesh):
    in_specs = (
        P(("groups", "ctx"), "head", None),
        P(("groups", "ctx"), "head", None),
        P(("groups", "ctx"), "head", None),
        P(("groups", "ctx"), "head", None),
        P("head", None),
        P("head"),
        P(("groups", "ctx"), "head", None),
        P(("groups", "ctx"), "head", None),
        P(),
    )
    out_specs = P(("groups", "ctx"), "head", None)
    body = functools.partial(local, ring_of(mesh))
    return jax.shard_map(body, mesh=mesh, in_specs=in_specs, out_specs=out_specs, check_vma=False)
```

```python
import functools
import math

import jax
import numpy as np
import jax.numpy as jnp
from jax import lax
from jax.sharding import PartitionSpec as P

BLOCK = 64
ORIG_CTX = 8192


rope_base = 10000.0
beta_fast = 32.0
beta_slow = 1.0
norm_eps = 1e-05
low_floor = -1e30


def yarn_table(yarn_factor, head_width):
    factor = yarn_factor[0].astype(jnp.float32)
    pair_ids = jnp.arange(head_width // 2, dtype=jnp.float32)
    base_freq = rope_base ** (-2.0 * pair_ids / head_width)
    wavelength = 2.0 * math.pi / base_freq
    ramp = jnp.clip((ORIG_CTX / wavelength - beta_slow) / (beta_fast - beta_slow), 0.0, 1.0)
    freq = base_freq * (ramp + (1.0 - ramp) / factor)
    mscale = 0.1 * jnp.log(factor) + 1.0
    return (freq, mscale * mscale / math.sqrt(head_width))


def rotate(values_in, positions, freq):
    angle = positions[:, None] * freq[None, :]
    cosine = jnp.cos(angle)[:, None, :]
    sine = jnp.sin(angle)[:, None, :]
    half_width = values_in.shape[2] // 2
    first = values_in[:, :, :half_width].astype(jnp.float32)
    second = values_in[:, :, half_width:].astype(jnp.float32)
    joined = jnp.concatenate(
        [first * cosine - second * sine, second * cosine + first * sine], axis=2
    )
    return joined.astype(jnp.bfloat16)


def lightning_local(q_hat, k_hat, value_linear, logdec):
    tok_rows, head_count, head_width = q_hat.shape
    block_count = tok_rows // BLOCK
    offsets = jnp.arange(BLOCK, dtype=jnp.float32)
    step_gap = offsets[:, None] - offsets[None, :]
    causal = step_gap >= 0
    intra_decay = jnp.where(
        causal[None], jnp.exp(logdec[:, None, None] * jnp.where(causal, step_gap, 0.0)[None]), 0.0
    )
    query_decay = jnp.exp(logdec[None, :] * (offsets[:, None] + 1.0))
    key_decay = jnp.exp(logdec[None, :] * (BLOCK - 1.0 - offsets[:, None]))
    block_decay = jnp.exp(logdec * BLOCK)

    def advance(carry_state, inputs):
        q_block, k_block, v_block = inputs
        scores = jnp.einsum("thd,shd->hts", q_block, k_block, preferred_element_type=jnp.float32)
        weights = (scores * intra_decay).astype(jnp.bfloat16)
        intra_part = jnp.einsum(
            "hts,shd->thd", weights, v_block, preferred_element_type=jnp.float32
        )
        carried = query_decay[:, :, None] * split_dot("thd,hde->the", q_block, carry_state)
        fresh_state = split_dot(
            "thd,the->hde", k_block, key_decay[:, :, None] * v_block.astype(jnp.float32)
        )
        return (carry_state * block_decay[:, None, None] + fresh_state, intra_part + carried)

    def split_blocks(array_in):
        return array_in.reshape(block_count, BLOCK, head_count, head_width)

    zero_state = jnp.zeros((head_count, head_width, head_width), jnp.float32)
    final_state, outputs = lax.scan(
        advance,
        zero_state,
        (split_blocks(q_hat), split_blocks(k_hat), split_blocks(value_linear)),
        unroll=True,
    )
    return (final_state, outputs.reshape(tok_rows, head_count, head_width))


def exclusive_scan(slab_state, logdec, tok_rows):
    count = lax.axis_size("ctx")
    decay = jnp.exp(logdec * tok_rows)[:, None, None]
    sent = slab_state.astype(jnp.bfloat16)
    running = lax.ppermute(sent, "ctx", [(i, i + 1) for i in range(count - 1)]).astype(jnp.float32)
    if count > 2:
        two_back = lax.ppermute(sent, "ctx", [(i, i + 2) for i in range(count - 2)])
        running = running + two_back.astype(jnp.float32) * decay
    offset = 2
    while offset < count:
        pairs = [(i, i + offset) for i in range(count - offset)]
        moved = lax.ppermute(running.astype(jnp.bfloat16), "ctx", pairs).astype(jnp.float32)
        scale = jnp.exp(logdec * (tok_rows * offset))
        running = running + moved * scale[:, None, None]
        offset *= 2
    return running


def split_dot(spec, exact, wide):
    high = wide.astype(jnp.bfloat16)
    low = (wide - high.astype(jnp.float32)).astype(jnp.bfloat16)
    first = jnp.einsum(spec, exact, high, preferred_element_type=jnp.float32)
    return first + jnp.einsum(spec, exact, low, preferred_element_type=jnp.float32)


def local(
    ring,
    query_linear,
    key_linear,
    value_linear,
    gate_logits,
    norm_gain,
    decay_code,
    query_soft,
    key_soft,
    yarn_factor,
):
    tok_rows, head_count, head_width = query_linear.shape
    my_slab = lax.axis_index("ctx")
    freq, logit_scale = yarn_table(yarn_factor, head_width)
    first_row = my_slab * tok_rows
    query_pos = first_row + jnp.arange(tok_rows, dtype=jnp.int32)
    positions = query_pos.astype(jnp.float32)
    query_rot = rotate(query_soft, positions, freq)
    key_rot = rotate(key_soft, positions, freq)
    count = len(ring)
    ring_table = jnp.asarray(ring, jnp.int32)
    spot_table = jnp.asarray(np.argsort(np.asarray(ring)), jnp.int32)
    my_spot = spot_table[my_slab]
    forward = [(ring[i], ring[(i + 1) % count]) for i in range(count)]
    backward = [(ring[i], ring[(i - 1) % count]) for i in range(count)]
    steps = []
    for step in range(1, count // 2 + 1):
        moves = [("ahead", forward, ring_table[(my_spot - step) % count])]
        if 2 * step == count:
            moves = [("split", None, moves[0][2])]
        else:
            moves.append(("behind", backward, ring_table[(my_spot + step) % count]))
        steps.append(moves)
    half = head_count // 2

    def travel(name, pairs):
        if name != "split":
            held[name] = lax.ppermute(held[name], "ctx", pairs)
            return held[name]
        front = lax.ppermute(held["ahead"][:, :half], "ctx", forward)
        back = lax.ppermute(held["behind"][:, half:], "ctx", backward)
        return jnp.concatenate([front, back], axis=1)

    def score_chunk(keys_in, slab):
        raw = jnp.einsum("thd,shd->hts", query_rot, keys_in, preferred_element_type=jnp.float32)
        key_pos = slab * tok_rows + jnp.arange(tok_rows, dtype=jnp.int32)
        allowed = key_pos[None, :] <= query_pos[:, None]
        return jnp.where(allowed[None], raw * logit_scale, -jnp.inf)

    held = {"ahead": key_rot, "behind": key_rot}
    score_chunks = [score_chunk(key_rot, my_slab)]

    def key_step(moves):
        for name, pairs, slab in moves:
            score_chunks.append(score_chunk(travel(name, pairs), slab))

    early = (len(steps) + 1) // 2
    for moves in steps[:early]:
        key_step(moves)
    logdec = jnp.log1p(-decay_code.astype(jnp.float32) * 2.0 ** (-20))
    q_hat = jax.nn.silu(query_linear.astype(jnp.float32)).astype(jnp.bfloat16)
    k_hat = jax.nn.silu(key_linear.astype(jnp.float32)).astype(jnp.bfloat16)
    slab_state, local_out = lightning_local(q_hat, k_hat, value_linear, logdec)
    ring_keys = (held["ahead"], held["behind"])
    ring_keys, slab_state = lax.optimization_barrier((ring_keys, slab_state))
    held["ahead"], held["behind"] = ring_keys
    for moves in steps[early:]:
        key_step(moves)
    incoming = exclusive_scan(slab_state, logdec, tok_rows)
    local_pos = jnp.arange(tok_rows, dtype=jnp.float32)
    query_decay = jnp.exp(logdec[None, :] * (local_pos[:, None] + 1.0))
    carried = query_decay[:, :, None] * split_dot("thd,hde->the", q_hat, incoming)
    linear_out = local_out + carried
    square_sum = jnp.sum(linear_out * linear_out, axis=(1, 2))
    total_square = lax.psum(square_sum, "head")
    mean_sq = total_square / (head_count * lax.axis_size("head") * head_width)
    normed = (
        linear_out
        * lax.rsqrt(mean_sq + norm_eps)[:, None, None]
        * norm_gain[None]
        * jax.nn.sigmoid(gate_logits.astype(jnp.float32))
    )
    values_soft = normed.astype(jnp.bfloat16)
    ring_keys = (held["ahead"], held["behind"])
    ring_keys, values_soft = lax.optimization_barrier((ring_keys, values_soft))
    top = score_chunks[0].max(axis=2)
    for chunk in score_chunks[1:]:
        top = jnp.maximum(top, chunk.max(axis=2))
    prob_chunks = [jnp.exp(chunk - top[:, :, None]) for chunk in score_chunks]
    total = prob_chunks[0].sum(axis=2)
    for chunk in prob_chunks[1:]:
        total = total + chunk.sum(axis=2)
    weight_chunks = [chunk.astype(jnp.bfloat16) for chunk in prob_chunks]

    held = {"ahead": values_soft, "behind": values_soft}
    accum = jnp.einsum(
        "hts,shd->htd", weight_chunks[0], values_soft, preferred_element_type=jnp.float32
    )
    chunk_at = 1
    for moves in steps:
        for name, pairs, slab in moves:
            accum = accum + jnp.einsum(
                "hts,shd->htd",
                weight_chunks[chunk_at],
                travel(name, pairs),
                preferred_element_type=jnp.float32,
            )
            chunk_at += 1
    result = accum / total[:, :, None]
    return result.transpose(1, 0, 2).astype(jnp.bfloat16)


def ring_of(mesh):
    devices = np.moveaxis(np.asarray(mesh.devices), mesh.axis_names.index("ctx"), 0)
    line = devices.reshape(devices.shape[0], -1)[:, 0]
    count = len(line)
    try:
        spots = [tuple(int(v) for v in dev.coords) for dev in line]
    except (AttributeError, TypeError):
        return list(range(count))
    varying = [k for k in range(len(spots[0])) if len({s[k] for s in spots}) > 1]
    if len(varying) != 2:
        return sorted(range(count), key=lambda c: spots[c])
    varying.sort(key=lambda k: len({s[k] for s in spots}))
    outer, inner = varying
    order = []
    for turn, value in enumerate(sorted({s[outer] for s in spots})):
        members = [c for c in range(count) if spots[c][outer] == value]
        members.sort(key=lambda c: spots[c][inner], reverse=turn % 2 == 1)
        order += members
    return order


def solution(mesh):
    in_specs = (
        P(("groups", "ctx"), "head", None),
        P(("groups", "ctx"), "head", None),
        P(("groups", "ctx"), "head", None),
        P(("groups", "ctx"), "head", None),
        P("head", None),
        P("head"),
        P(("groups", "ctx"), "head", None),
        P(("groups", "ctx"), "head", None),
        P(),
    )
    out_specs = P(("groups", "ctx"), "head", None)
    body = functools.partial(local, ring_of(mesh))
    return jax.shard_map(body, mesh=mesh, in_specs=in_specs, out_specs=out_specs, check_vma=False)
```

```python
import functools
import math

import jax
import numpy as np
import jax.numpy as jnp
from jax import lax
from jax.sharding import PartitionSpec as P

BLOCK = 64
ORIG_CTX = 8192


rope_base = 10000.0
beta_fast = 32.0
beta_slow = 1.0
norm_eps = 1e-05
low_floor = -1e30


def yarn_table(yarn_factor, head_width):
    factor = yarn_factor[0].astype(jnp.float32)
    pair_ids = jnp.arange(head_width // 2, dtype=jnp.float32)
    base_freq = rope_base ** (-2.0 * pair_ids / head_width)
    wavelength = 2.0 * math.pi / base_freq
    ramp = jnp.clip((ORIG_CTX / wavelength - beta_slow) / (beta_fast - beta_slow), 0.0, 1.0)
    freq = base_freq * (ramp + (1.0 - ramp) / factor)
    mscale = 0.1 * jnp.log(factor) + 1.0
    return (freq, mscale * mscale / math.sqrt(head_width))


def rotate(values_in, positions, freq):
    angle = positions[:, None] * freq[None, :]
    cosine = jnp.cos(angle)[:, None, :]
    sine = jnp.sin(angle)[:, None, :]
    half_width = values_in.shape[2] // 2
    first = values_in[:, :, :half_width].astype(jnp.float32)
    second = values_in[:, :, half_width:].astype(jnp.float32)
    joined = jnp.concatenate(
        [first * cosine - second * sine, second * cosine + first * sine], axis=2
    )
    return joined.astype(jnp.bfloat16)


def lightning_local(q_hat, k_hat, value_linear, logdec):
    tok_rows, head_count, head_width = q_hat.shape
    block_count = tok_rows // BLOCK
    offsets = jnp.arange(BLOCK, dtype=jnp.float32)
    step_gap = offsets[:, None] - offsets[None, :]
    causal = step_gap >= 0
    intra_decay = jnp.where(
        causal[None], jnp.exp(logdec[:, None, None] * jnp.where(causal, step_gap, 0.0)[None]), 0.0
    )
    query_decay = jnp.exp(logdec[None, :] * (offsets[:, None] + 1.0))
    key_decay = jnp.exp(logdec[None, :] * (BLOCK - 1.0 - offsets[:, None]))
    block_decay = jnp.exp(logdec * BLOCK)

    def advance(carry_state, inputs):
        q_block, k_block, v_block = inputs
        scores = jnp.einsum("thd,shd->hts", q_block, k_block, preferred_element_type=jnp.float32)
        weights = (scores * intra_decay).astype(jnp.bfloat16)
        intra_part = jnp.einsum(
            "hts,shd->thd", weights, v_block, preferred_element_type=jnp.float32
        )
        carried = query_decay[:, :, None] * split_dot("thd,hde->the", q_block, carry_state)
        fresh_state = split_dot(
            "thd,the->hde", k_block, key_decay[:, :, None] * v_block.astype(jnp.float32)
        )
        return (carry_state * block_decay[:, None, None] + fresh_state, intra_part + carried)

    def split_blocks(array_in):
        return array_in.reshape(block_count, BLOCK, head_count, head_width)

    zero_state = jnp.zeros((head_count, head_width, head_width), jnp.float32)
    final_state, outputs = lax.scan(
        advance,
        zero_state,
        (split_blocks(q_hat), split_blocks(k_hat), split_blocks(value_linear)),
        unroll=True,
    )
    return (final_state, outputs.reshape(tok_rows, head_count, head_width))


def exclusive_scan(slab_state, logdec, tok_rows):
    count = lax.axis_size("ctx")
    decay = jnp.exp(logdec * tok_rows)[:, None, None]
    sent = slab_state.astype(jnp.bfloat16)
    running = lax.ppermute(sent, "ctx", [(i, i + 1) for i in range(count - 1)]).astype(jnp.float32)
    if count > 2:
        two_back = lax.ppermute(sent, "ctx", [(i, i + 2) for i in range(count - 2)])
        running = running + two_back.astype(jnp.float32) * decay
    offset = 2
    while offset < count:
        pairs = [(i, i + offset) for i in range(count - offset)]
        moved = lax.ppermute(running.astype(jnp.bfloat16), "ctx", pairs).astype(jnp.float32)
        scale = jnp.exp(logdec * (tok_rows * offset))
        running = running + moved * scale[:, None, None]
        offset *= 2
    return running


def split_dot(spec, exact, wide):
    high = wide.astype(jnp.bfloat16)
    low = (wide - high.astype(jnp.float32)).astype(jnp.bfloat16)
    first = jnp.einsum(spec, exact, high, preferred_element_type=jnp.float32)
    return first + jnp.einsum(spec, exact, low, preferred_element_type=jnp.float32)


def local(
    ring,
    query_linear,
    key_linear,
    value_linear,
    gate_logits,
    norm_gain,
    decay_code,
    query_soft,
    key_soft,
    yarn_factor,
):
    tok_rows, head_count, head_width = query_linear.shape
    my_slab = lax.axis_index("ctx")
    freq, logit_scale = yarn_table(yarn_factor, head_width)
    first_row = my_slab * tok_rows
    query_pos = first_row + jnp.arange(tok_rows, dtype=jnp.int32)
    positions = query_pos.astype(jnp.float32)
    query_rot = rotate(query_soft, positions, freq)
    key_rot = rotate(key_soft, positions, freq)
    count = len(ring)
    ring_table = jnp.asarray(ring, jnp.int32)
    spot_table = jnp.asarray(np.argsort(np.asarray(ring)), jnp.int32)
    my_spot = spot_table[my_slab]
    forward = [(ring[i], ring[(i + 1) % count]) for i in range(count)]
    backward = [(ring[i], ring[(i - 1) % count]) for i in range(count)]
    steps = []
    for step in range(1, count // 2 + 1):
        moves = [("ahead", forward, ring_table[(my_spot - step) % count])]
        if 2 * step == count:
            moves = [("split", None, moves[0][2])]
        else:
            moves.append(("behind", backward, ring_table[(my_spot + step) % count]))
        steps.append(moves)
    half = head_count // 2

    def travel(name, pairs):
        if name != "split":
            held[name] = lax.ppermute(held[name], "ctx", pairs)
            return held[name]
        front = lax.ppermute(held["ahead"][:, :half], "ctx", forward)
        back = lax.ppermute(held["behind"][:, half:], "ctx", backward)
        return jnp.concatenate([front, back], axis=1)

    def score_chunk(keys_in, slab):
        raw = jnp.einsum("thd,shd->hts", query_rot, keys_in, preferred_element_type=jnp.float32)
        key_pos = slab * tok_rows + jnp.arange(tok_rows, dtype=jnp.int32)
        allowed = key_pos[None, :] <= query_pos[:, None]
        return jnp.where(allowed[None], raw * logit_scale, -jnp.inf)

    held = {"ahead": key_rot, "behind": key_rot}
    score_chunks = [score_chunk(key_rot, my_slab)]

    def key_step(moves):
        for name, pairs, slab in moves:
            score_chunks.append(score_chunk(travel(name, pairs), slab))

    early = (len(steps) + 1) // 2
    for moves in steps[:early]:
        key_step(moves)
    logdec = jnp.log1p(-decay_code.astype(jnp.float32) * 2.0 ** (-20))
    q_hat = jax.nn.silu(query_linear.astype(jnp.float32)).astype(jnp.bfloat16)
    k_hat = jax.nn.silu(key_linear.astype(jnp.float32)).astype(jnp.bfloat16)
    slab_state, local_out = lightning_local(q_hat, k_hat, value_linear, logdec)
    for moves in steps[early:]:
        key_step(moves)
    incoming = exclusive_scan(slab_state, logdec, tok_rows)
    local_pos = jnp.arange(tok_rows, dtype=jnp.float32)
    query_decay = jnp.exp(logdec[None, :] * (local_pos[:, None] + 1.0))
    carried = query_decay[:, :, None] * split_dot("thd,hde->the", q_hat, incoming)
    linear_out = local_out + carried
    square_sum = jnp.sum(linear_out * linear_out, axis=(1, 2))
    total_square = lax.psum(square_sum, "head")
    mean_sq = total_square / (head_count * lax.axis_size("head") * head_width)
    normed = (
        linear_out
        * lax.rsqrt(mean_sq + norm_eps)[:, None, None]
        * norm_gain[None]
        * jax.nn.sigmoid(gate_logits.astype(jnp.float32))
    )
    values_soft = normed.astype(jnp.bfloat16)
    ring_keys = (held["ahead"], held["behind"])
    ring_keys, values_soft = lax.optimization_barrier((ring_keys, values_soft))
    top = score_chunks[0].max(axis=2)
    for chunk in score_chunks[1:]:
        top = jnp.maximum(top, chunk.max(axis=2))
    prob_chunks = [jnp.exp(chunk - top[:, :, None]) for chunk in score_chunks]
    total = prob_chunks[0].sum(axis=2)
    for chunk in prob_chunks[1:]:
        total = total + chunk.sum(axis=2)
    weight_chunks = [chunk.astype(jnp.bfloat16) for chunk in prob_chunks]

    held = {"ahead": values_soft, "behind": values_soft}
    accum = jnp.einsum(
        "hts,shd->htd", weight_chunks[0], values_soft, preferred_element_type=jnp.float32
    )
    chunk_at = 1
    for moves in steps:
        for name, pairs, slab in moves:
            accum = accum + jnp.einsum(
                "hts,shd->htd",
                weight_chunks[chunk_at],
                travel(name, pairs),
                preferred_element_type=jnp.float32,
            )
            chunk_at += 1
    result = accum / total[:, :, None]
    return result.transpose(1, 0, 2).astype(jnp.bfloat16)


def ring_of(mesh):
    devices = np.moveaxis(np.asarray(mesh.devices), mesh.axis_names.index("ctx"), 0)
    line = devices.reshape(devices.shape[0], -1)[:, 0]
    count = len(line)
    try:
        spots = [tuple(int(v) for v in dev.coords) for dev in line]
    except (AttributeError, TypeError):
        return list(range(count))
    varying = [k for k in range(len(spots[0])) if len({s[k] for s in spots}) > 1]
    if len(varying) != 2:
        return sorted(range(count), key=lambda c: spots[c])
    varying.sort(key=lambda k: len({s[k] for s in spots}))
    outer, inner = varying
    order = []
    for turn, value in enumerate(sorted({s[outer] for s in spots})):
        members = [c for c in range(count) if spots[c][outer] == value]
        members.sort(key=lambda c: spots[c][inner], reverse=turn % 2 == 1)
        order += members
    return order


def solution(mesh):
    in_specs = (
        P(("groups", "ctx"), "head", None),
        P(("groups", "ctx"), "head", None),
        P(("groups", "ctx"), "head", None),
        P(("groups", "ctx"), "head", None),
        P("head", None),
        P("head"),
        P(("groups", "ctx"), "head", None),
        P(("groups", "ctx"), "head", None),
        P(),
    )
    out_specs = P(("groups", "ctx"), "head", None)
    body = functools.partial(local, ring_of(mesh))
    return jax.shard_map(body, mesh=mesh, in_specs=in_specs, out_specs=out_specs, check_vma=False)
```

```python
import functools
import math

import jax
import numpy as np
import jax.numpy as jnp
from jax import lax
from jax.sharding import PartitionSpec as P

BLOCK = 64
ORIG_CTX = 8192


rope_base = 10000.0
beta_fast = 32.0
beta_slow = 1.0
norm_eps = 1e-05
low_floor = -1e30


def yarn_table(yarn_factor, head_width):
    factor = yarn_factor[0].astype(jnp.float32)
    pair_ids = jnp.arange(head_width // 2, dtype=jnp.float32)
    base_freq = rope_base ** (-2.0 * pair_ids / head_width)
    wavelength = 2.0 * math.pi / base_freq
    ramp = jnp.clip((ORIG_CTX / wavelength - beta_slow) / (beta_fast - beta_slow), 0.0, 1.0)
    freq = base_freq * (ramp + (1.0 - ramp) / factor)
    mscale = 0.1 * jnp.log(factor) + 1.0
    return (freq, mscale * mscale / math.sqrt(head_width))


def rotate(values_in, positions, freq):
    angle = positions[:, None] * freq[None, :]
    cosine = jnp.cos(angle)[:, None, :]
    sine = jnp.sin(angle)[:, None, :]
    half_width = values_in.shape[2] // 2
    first = values_in[:, :, :half_width].astype(jnp.float32)
    second = values_in[:, :, half_width:].astype(jnp.float32)
    joined = jnp.concatenate(
        [first * cosine - second * sine, second * cosine + first * sine], axis=2
    )
    return joined.astype(jnp.bfloat16)


def lightning_local(q_hat, k_hat, value_linear, logdec):
    tok_rows, head_count, head_width = q_hat.shape
    block_count = tok_rows // BLOCK
    offsets = jnp.arange(BLOCK, dtype=jnp.float32)
    step_gap = offsets[:, None] - offsets[None, :]
    causal = step_gap >= 0
    intra_decay = jnp.where(
        causal[None], jnp.exp(logdec[:, None, None] * jnp.where(causal, step_gap, 0.0)[None]), 0.0
    )
    query_decay = jnp.exp(logdec[None, :] * (offsets[:, None] + 1.0))
    key_decay = jnp.exp(logdec[None, :] * (BLOCK - 1.0 - offsets[:, None]))
    block_decay = jnp.exp(logdec * BLOCK)

    def advance(carry_state, inputs):
        q_block, k_block, v_block = inputs
        scores = jnp.einsum("thd,shd->hts", q_block, k_block, preferred_element_type=jnp.float32)
        weights = (scores * intra_decay).astype(jnp.bfloat16)
        intra_part = jnp.einsum(
            "hts,shd->thd", weights, v_block, preferred_element_type=jnp.float32
        )
        carried = query_decay[:, :, None] * split_dot("thd,hde->the", q_block, carry_state)
        fresh_state = split_dot(
            "thd,the->hde", k_block, key_decay[:, :, None] * v_block.astype(jnp.float32)
        )
        return (carry_state * block_decay[:, None, None] + fresh_state, intra_part + carried)

    def split_blocks(array_in):
        return array_in.reshape(block_count, BLOCK, head_count, head_width)

    zero_state = jnp.zeros((head_count, head_width, head_width), jnp.float32)
    final_state, outputs = lax.scan(
        advance,
        zero_state,
        (split_blocks(q_hat), split_blocks(k_hat), split_blocks(value_linear)),
        unroll=True,
    )
    return (final_state, outputs.reshape(tok_rows, head_count, head_width))


def exclusive_scan(slab_state, logdec, tok_rows):
    count = lax.axis_size("ctx")
    decay = jnp.exp(logdec * tok_rows)[:, None, None]
    sent = slab_state.astype(jnp.bfloat16)
    running = lax.ppermute(sent, "ctx", [(i, i + 1) for i in range(count - 1)]).astype(jnp.float32)
    if count > 2:
        two_back = lax.ppermute(sent, "ctx", [(i, i + 2) for i in range(count - 2)])
        running = running + two_back.astype(jnp.float32) * decay
    offset = 2
    while offset < count:
        pairs = [(i, i + offset) for i in range(count - offset)]
        moved = lax.ppermute(running.astype(jnp.bfloat16), "ctx", pairs).astype(jnp.float32)
        scale = jnp.exp(logdec * (tok_rows * offset))
        running = running + moved * scale[:, None, None]
        offset *= 2
    return running


def split_dot(spec, exact, wide):
    high = wide.astype(jnp.bfloat16)
    low = (wide - high.astype(jnp.float32)).astype(jnp.bfloat16)
    first = jnp.einsum(spec, exact, high, preferred_element_type=jnp.float32)
    return first + jnp.einsum(spec, exact, low, preferred_element_type=jnp.float32)


def local(
    ring,
    query_linear,
    key_linear,
    value_linear,
    gate_logits,
    norm_gain,
    decay_code,
    query_soft,
    key_soft,
    yarn_factor,
):
    tok_rows, head_count, head_width = query_linear.shape
    my_slab = lax.axis_index("ctx")
    freq, logit_scale = yarn_table(yarn_factor, head_width)
    first_row = my_slab * tok_rows
    query_pos = first_row + jnp.arange(tok_rows, dtype=jnp.int32)
    positions = query_pos.astype(jnp.float32)
    query_rot = rotate(query_soft, positions, freq)
    key_rot = rotate(key_soft, positions, freq)
    count = len(ring)
    ring_table = jnp.asarray(ring, jnp.int32)
    spot_table = jnp.asarray(np.argsort(np.asarray(ring)), jnp.int32)
    my_spot = spot_table[my_slab]
    forward = [(ring[i], ring[(i + 1) % count]) for i in range(count)]
    backward = [(ring[i], ring[(i - 1) % count]) for i in range(count)]
    steps = []
    for step in range(1, count // 2 + 1):
        moves = [("ahead", forward, ring_table[(my_spot - step) % count])]
        if 2 * step == count:
            moves = [("split", None, moves[0][2])]
        else:
            moves.append(("behind", backward, ring_table[(my_spot + step) % count]))
        steps.append(moves)
    half = head_count // 2

    def travel(name, pairs):
        if name != "split":
            held[name] = lax.ppermute(held[name], "ctx", pairs)
            return held[name]
        front = lax.ppermute(held["ahead"][:, :half], "ctx", forward)
        back = lax.ppermute(held["behind"][:, half:], "ctx", backward)
        return jnp.concatenate([front, back], axis=1)

    def score_chunk(keys_in, slab):
        raw = jnp.einsum("thd,shd->hts", query_rot, keys_in, preferred_element_type=jnp.float32)
        key_pos = slab * tok_rows + jnp.arange(tok_rows, dtype=jnp.int32)
        allowed = key_pos[None, :] <= query_pos[:, None]
        return jnp.where(allowed[None], raw * logit_scale, -jnp.inf)

    held = {"ahead": key_rot, "behind": key_rot}
    score_chunks = [score_chunk(key_rot, my_slab)]

    def key_step(moves):
        for name, pairs, slab in moves:
            score_chunks.append(score_chunk(travel(name, pairs), slab))

    early = (len(steps) + 1) // 2
    for moves in steps[:early]:
        key_step(moves)
    logdec = jnp.log1p(-decay_code.astype(jnp.float32) * 2.0 ** (-20))
    q_hat = jax.nn.silu(query_linear.astype(jnp.float32)).astype(jnp.bfloat16)
    k_hat = jax.nn.silu(key_linear.astype(jnp.float32)).astype(jnp.bfloat16)
    slab_state, local_out = lightning_local(q_hat, k_hat, value_linear, logdec)
    for moves in steps[early:]:
        key_step(moves)
    incoming = exclusive_scan(slab_state, logdec, tok_rows)
    local_pos = jnp.arange(tok_rows, dtype=jnp.float32)
    query_decay = jnp.exp(logdec[None, :] * (local_pos[:, None] + 1.0))
    carried = query_decay[:, :, None] * split_dot("thd,hde->the", q_hat, incoming)
    linear_out = local_out + carried
    square_sum = jnp.sum(linear_out * linear_out, axis=(1, 2))
    total_square = lax.psum(square_sum, "head")
    mean_sq = total_square / (head_count * lax.axis_size("head") * head_width)
    normed = (
        linear_out
        * lax.rsqrt(mean_sq + norm_eps)[:, None, None]
        * norm_gain[None]
        * jax.nn.sigmoid(gate_logits.astype(jnp.float32))
    )
    values_soft = normed.astype(jnp.bfloat16)
    top = score_chunks[0].max(axis=2)
    for chunk in score_chunks[1:]:
        top = jnp.maximum(top, chunk.max(axis=2))
    prob_chunks = [jnp.exp(chunk - top[:, :, None]) for chunk in score_chunks]
    total = prob_chunks[0].sum(axis=2)
    for chunk in prob_chunks[1:]:
        total = total + chunk.sum(axis=2)
    weight_chunks = [chunk.astype(jnp.bfloat16) for chunk in prob_chunks]

    held = {"ahead": values_soft, "behind": values_soft}
    accum = jnp.einsum(
        "hts,shd->htd", weight_chunks[0], values_soft, preferred_element_type=jnp.float32
    )
    chunk_at = 1
    for moves in steps:
        for name, pairs, slab in moves:
            accum = accum + jnp.einsum(
                "hts,shd->htd",
                weight_chunks[chunk_at],
                travel(name, pairs),
                preferred_element_type=jnp.float32,
            )
            chunk_at += 1
    result = accum / total[:, :, None]
    return result.transpose(1, 0, 2).astype(jnp.bfloat16)


def ring_of(mesh):
    devices = np.moveaxis(np.asarray(mesh.devices), mesh.axis_names.index("ctx"), 0)
    line = devices.reshape(devices.shape[0], -1)[:, 0]
    count = len(line)
    try:
        spots = [tuple(int(v) for v in dev.coords) for dev in line]
    except (AttributeError, TypeError):
        return list(range(count))
    varying = [k for k in range(len(spots[0])) if len({s[k] for s in spots}) > 1]
    if len(varying) != 2:
        return sorted(range(count), key=lambda c: spots[c])
    varying.sort(key=lambda k: len({s[k] for s in spots}))
    outer, inner = varying
    order = []
    for turn, value in enumerate(sorted({s[outer] for s in spots})):
        members = [c for c in range(count) if spots[c][outer] == value]
        members.sort(key=lambda c: spots[c][inner], reverse=turn % 2 == 1)
        order += members
    return order


def solution(mesh):
    in_specs = (
        P(("groups", "ctx"), "head", None),
        P(("groups", "ctx"), "head", None),
        P(("groups", "ctx"), "head", None),
        P(("groups", "ctx"), "head", None),
        P("head", None),
        P("head"),
        P(("groups", "ctx"), "head", None),
        P(("groups", "ctx"), "head", None),
        P(),
    )
    out_specs = P(("groups", "ctx"), "head", None)
    body = functools.partial(local, ring_of(mesh))
    return jax.shard_map(body, mesh=mesh, in_specs=in_specs, out_specs=out_specs, check_vma=False)
```

```python
import functools
import math

import jax
import numpy as np
import jax.numpy as jnp
from jax import lax
from jax.sharding import PartitionSpec as P

BLOCK = 64
ORIG_CTX = 8192


rope_base = 10000.0
beta_fast = 32.0
beta_slow = 1.0
norm_eps = 1e-05
low_floor = -1e30


def yarn_table(yarn_factor, head_width):
    factor = yarn_factor[0].astype(jnp.float32)
    pair_ids = jnp.arange(head_width // 2, dtype=jnp.float32)
    base_freq = rope_base ** (-2.0 * pair_ids / head_width)
    wavelength = 2.0 * math.pi / base_freq
    ramp = jnp.clip((ORIG_CTX / wavelength - beta_slow) / (beta_fast - beta_slow), 0.0, 1.0)
    freq = base_freq * (ramp + (1.0 - ramp) / factor)
    mscale = 0.1 * jnp.log(factor) + 1.0
    return (freq, mscale * mscale / math.sqrt(head_width))


def rotate(values_in, positions, freq):
    angle = positions[:, None] * freq[None, :]
    cosine = jnp.cos(angle)[:, None, :]
    sine = jnp.sin(angle)[:, None, :]
    half_width = values_in.shape[2] // 2
    first = values_in[:, :, :half_width].astype(jnp.float32)
    second = values_in[:, :, half_width:].astype(jnp.float32)
    joined = jnp.concatenate(
        [first * cosine - second * sine, second * cosine + first * sine], axis=2
    )
    return joined.astype(jnp.bfloat16)


def lightning_local(q_hat, k_hat, value_linear, logdec):
    tok_rows, head_count, head_width = q_hat.shape
    block_count = tok_rows // BLOCK
    offsets = jnp.arange(BLOCK, dtype=jnp.float32)
    step_gap = offsets[:, None] - offsets[None, :]
    causal = step_gap >= 0
    intra_decay = jnp.where(
        causal[None], jnp.exp(logdec[:, None, None] * jnp.where(causal, step_gap, 0.0)[None]), 0.0
    )
    query_decay = jnp.exp(logdec[None, :] * (offsets[:, None] + 1.0))
    key_decay = jnp.exp(logdec[None, :] * (BLOCK - 1.0 - offsets[:, None]))
    block_decay = jnp.exp(logdec * BLOCK)

    def advance(carry_state, inputs):
        q_block, k_block, v_block = inputs
        scores = jnp.einsum("thd,shd->hts", q_block, k_block, preferred_element_type=jnp.float32)
        weights = (scores * intra_decay).astype(jnp.bfloat16)
        intra_part = jnp.einsum(
            "hts,shd->thd", weights, v_block, preferred_element_type=jnp.float32
        )
        carried = query_decay[:, :, None] * split_dot("thd,hde->the", q_block, carry_state)
        fresh_state = split_dot(
            "thd,the->hde", k_block, key_decay[:, :, None] * v_block.astype(jnp.float32)
        )
        return (carry_state * block_decay[:, None, None] + fresh_state, intra_part + carried)

    def split_blocks(array_in):
        return array_in.reshape(block_count, BLOCK, head_count, head_width)

    zero_state = jnp.zeros((head_count, head_width, head_width), jnp.float32)
    final_state, outputs = lax.scan(
        advance,
        zero_state,
        (split_blocks(q_hat), split_blocks(k_hat), split_blocks(value_linear)),
        unroll=True,
    )
    return (final_state, outputs.reshape(tok_rows, head_count, head_width))


def exclusive_scan(slab_state, logdec, tok_rows):
    count = lax.axis_size("ctx")
    decay = jnp.exp(logdec * tok_rows)[:, None, None]
    sent = slab_state.astype(jnp.bfloat16)
    running = lax.ppermute(sent, "ctx", [(i, i + 1) for i in range(count - 1)]).astype(jnp.float32)
    if count > 2:
        two_back = lax.ppermute(sent, "ctx", [(i, i + 2) for i in range(count - 2)])
        running = running + two_back.astype(jnp.float32) * decay
    offset = 2
    while offset < count:
        pairs = [(i, i + offset) for i in range(count - offset)]
        moved = lax.ppermute(running.astype(jnp.bfloat16), "ctx", pairs).astype(jnp.float32)
        scale = jnp.exp(logdec * (tok_rows * offset))
        running = running + moved * scale[:, None, None]
        offset *= 2
    return running


def split_dot(spec, exact, wide):
    high = wide.astype(jnp.bfloat16)
    low = (wide - high.astype(jnp.float32)).astype(jnp.bfloat16)
    first = jnp.einsum(spec, exact, high, preferred_element_type=jnp.float32)
    return first + jnp.einsum(spec, exact, low, preferred_element_type=jnp.float32)


def local(
    ring,
    query_linear,
    key_linear,
    value_linear,
    gate_logits,
    norm_gain,
    decay_code,
    query_soft,
    key_soft,
    yarn_factor,
):
    tok_rows, head_count, head_width = query_linear.shape
    my_slab = lax.axis_index("ctx")
    freq, logit_scale = yarn_table(yarn_factor, head_width)
    first_row = my_slab * tok_rows
    query_pos = first_row + jnp.arange(tok_rows, dtype=jnp.int32)
    positions = query_pos.astype(jnp.float32)
    query_rot = rotate(query_soft, positions, freq)
    key_rot = rotate(key_soft, positions, freq)
    count = len(ring)
    ring_table = jnp.asarray(ring, jnp.int32)
    spot_table = jnp.asarray(np.argsort(np.asarray(ring)), jnp.int32)
    my_spot = spot_table[my_slab]
    forward = [(ring[i], ring[(i + 1) % count]) for i in range(count)]
    backward = [(ring[i], ring[(i - 1) % count]) for i in range(count)]
    steps = []
    for step in range(1, count // 2 + 1):
        moves = [("ahead", forward, ring_table[(my_spot - step) % count])]
        if 2 * step == count:
            moves = [("split", None, moves[0][2])]
        else:
            moves.append(("behind", backward, ring_table[(my_spot + step) % count]))
        steps.append(moves)
    half = head_count // 2

    def travel(name, pairs):
        if name != "split":
            held[name] = lax.ppermute(held[name], "ctx", pairs)
            return held[name]
        front = lax.ppermute(held["ahead"][:, :half], "ctx", forward)
        back = lax.ppermute(held["behind"][:, half:], "ctx", backward)
        return jnp.concatenate([front, back], axis=1)

    def score_chunk(keys_in, slab):
        raw = jnp.einsum("thd,shd->hts", query_rot, keys_in, preferred_element_type=jnp.float32)
        key_pos = slab * tok_rows + jnp.arange(tok_rows, dtype=jnp.int32)
        allowed = key_pos[None, :] <= query_pos[:, None]
        return jnp.where(allowed[None], raw * logit_scale, -jnp.inf)

    held = {"ahead": key_rot, "behind": key_rot}
    score_chunks = [score_chunk(key_rot, my_slab)]

    def key_step(moves):
        for name, pairs, slab in moves:
            score_chunks.append(score_chunk(travel(name, pairs), slab))

    early = 1
    for moves in steps[:early]:
        key_step(moves)
    logdec = jnp.log1p(-decay_code.astype(jnp.float32) * 2.0 ** (-20))
    q_hat = jax.nn.silu(query_linear.astype(jnp.float32)).astype(jnp.bfloat16)
    k_hat = jax.nn.silu(key_linear.astype(jnp.float32)).astype(jnp.bfloat16)
    slab_state, local_out = lightning_local(q_hat, k_hat, value_linear, logdec)
    incoming = exclusive_scan(slab_state, logdec, tok_rows)
    ring_keys = (held["ahead"], held["behind"])
    ring_keys, incoming = lax.optimization_barrier((ring_keys, incoming))
    held["ahead"], held["behind"] = ring_keys
    for moves in steps[early:]:
        key_step(moves)
    local_pos = jnp.arange(tok_rows, dtype=jnp.float32)
    query_decay = jnp.exp(logdec[None, :] * (local_pos[:, None] + 1.0))
    carried = query_decay[:, :, None] * split_dot("thd,hde->the", q_hat, incoming)
    linear_out = local_out + carried
    square_sum = jnp.sum(linear_out * linear_out, axis=(1, 2))
    total_square = lax.psum(square_sum, "head")
    mean_sq = total_square / (head_count * lax.axis_size("head") * head_width)
    normed = (
        linear_out
        * lax.rsqrt(mean_sq + norm_eps)[:, None, None]
        * norm_gain[None]
        * jax.nn.sigmoid(gate_logits.astype(jnp.float32))
    )
    values_soft = normed.astype(jnp.bfloat16)
    ring_keys = (held["ahead"], held["behind"])
    ring_keys, values_soft = lax.optimization_barrier((ring_keys, values_soft))
    top = score_chunks[0].max(axis=2)
    for chunk in score_chunks[1:]:
        top = jnp.maximum(top, chunk.max(axis=2))
    prob_chunks = [jnp.exp(chunk - top[:, :, None]) for chunk in score_chunks]
    total = prob_chunks[0].sum(axis=2)
    for chunk in prob_chunks[1:]:
        total = total + chunk.sum(axis=2)
    weight_chunks = [chunk.astype(jnp.bfloat16) for chunk in prob_chunks]

    held = {"ahead": values_soft, "behind": values_soft}
    accum = jnp.einsum(
        "hts,shd->htd", weight_chunks[0], values_soft, preferred_element_type=jnp.float32
    )
    chunk_at = 1
    for moves in steps:
        for name, pairs, slab in moves:
            accum = accum + jnp.einsum(
                "hts,shd->htd",
                weight_chunks[chunk_at],
                travel(name, pairs),
                preferred_element_type=jnp.float32,
            )
            chunk_at += 1
    result = accum / total[:, :, None]
    return result.transpose(1, 0, 2).astype(jnp.bfloat16)


def ring_of(mesh):
    devices = np.moveaxis(np.asarray(mesh.devices), mesh.axis_names.index("ctx"), 0)
    line = devices.reshape(devices.shape[0], -1)[:, 0]
    count = len(line)
    try:
        spots = [tuple(int(v) for v in dev.coords) for dev in line]
    except (AttributeError, TypeError):
        return list(range(count))
    varying = [k for k in range(len(spots[0])) if len({s[k] for s in spots}) > 1]
    if len(varying) != 2:
        return sorted(range(count), key=lambda c: spots[c])
    varying.sort(key=lambda k: len({s[k] for s in spots}))
    outer, inner = varying
    order = []
    for turn, value in enumerate(sorted({s[outer] for s in spots})):
        members = [c for c in range(count) if spots[c][outer] == value]
        members.sort(key=lambda c: spots[c][inner], reverse=turn % 2 == 1)
        order += members
    return order


def solution(mesh):
    in_specs = (
        P(("groups", "ctx"), "head", None),
        P(("groups", "ctx"), "head", None),
        P(("groups", "ctx"), "head", None),
        P(("groups", "ctx"), "head", None),
        P("head", None),
        P("head"),
        P(("groups", "ctx"), "head", None),
        P(("groups", "ctx"), "head", None),
        P(),
    )
    out_specs = P(("groups", "ctx"), "head", None)
    body = functools.partial(local, ring_of(mesh))
    return jax.shard_map(body, mesh=mesh, in_specs=in_specs, out_specs=out_specs, check_vma=False)
```

```python
import functools
import math

import jax
import numpy as np
import jax.numpy as jnp
from jax import lax
from jax.sharding import PartitionSpec as P

BLOCK = 64
ORIG_CTX = 8192


rope_base = 10000.0
beta_fast = 32.0
beta_slow = 1.0
norm_eps = 1e-05
low_floor = -1e30


def yarn_table(yarn_factor, head_width):
    factor = yarn_factor[0].astype(jnp.float32)
    pair_ids = jnp.arange(head_width // 2, dtype=jnp.float32)
    base_freq = rope_base ** (-2.0 * pair_ids / head_width)
    wavelength = 2.0 * math.pi / base_freq
    ramp = jnp.clip((ORIG_CTX / wavelength - beta_slow) / (beta_fast - beta_slow), 0.0, 1.0)
    freq = base_freq * (ramp + (1.0 - ramp) / factor)
    mscale = 0.1 * jnp.log(factor) + 1.0
    return (freq, mscale * mscale / math.sqrt(head_width))


def rotate(values_in, positions, freq):
    angle = positions[:, None] * freq[None, :]
    cosine = jnp.cos(angle)[:, None, :]
    sine = jnp.sin(angle)[:, None, :]
    half_width = values_in.shape[2] // 2
    first = values_in[:, :, :half_width].astype(jnp.float32)
    second = values_in[:, :, half_width:].astype(jnp.float32)
    joined = jnp.concatenate(
        [first * cosine - second * sine, second * cosine + first * sine], axis=2
    )
    return joined.astype(jnp.bfloat16)


def lightning_local(q_hat, k_hat, value_linear, logdec):
    tok_rows, head_count, head_width = q_hat.shape
    block_count = tok_rows // BLOCK
    offsets = jnp.arange(BLOCK, dtype=jnp.float32)
    step_gap = offsets[:, None] - offsets[None, :]
    causal = step_gap >= 0
    intra_decay = jnp.where(
        causal[None], jnp.exp(logdec[:, None, None] * jnp.where(causal, step_gap, 0.0)[None]), 0.0
    )
    query_decay = jnp.exp(logdec[None, :] * (offsets[:, None] + 1.0))
    key_decay = jnp.exp(logdec[None, :] * (BLOCK - 1.0 - offsets[:, None]))
    block_decay = jnp.exp(logdec * BLOCK)

    def advance(carry_state, inputs):
        q_block, k_block, v_block = inputs
        scores = jnp.einsum("thd,shd->hts", q_block, k_block, preferred_element_type=jnp.float32)
        weights = (scores * intra_decay).astype(jnp.bfloat16)
        intra_part = jnp.einsum(
            "hts,shd->thd", weights, v_block, preferred_element_type=jnp.float32
        )
        carried = query_decay[:, :, None] * split_dot("thd,hde->the", q_block, carry_state)
        fresh_state = split_dot(
            "thd,the->hde", k_block, key_decay[:, :, None] * v_block.astype(jnp.float32)
        )
        return (carry_state * block_decay[:, None, None] + fresh_state, intra_part + carried)

    def split_blocks(array_in):
        return array_in.reshape(block_count, BLOCK, head_count, head_width)

    zero_state = jnp.zeros((head_count, head_width, head_width), jnp.float32)
    final_state, outputs = lax.scan(
        advance,
        zero_state,
        (split_blocks(q_hat), split_blocks(k_hat), split_blocks(value_linear)),
        unroll=True,
    )
    return (final_state, outputs.reshape(tok_rows, head_count, head_width))


def exclusive_scan(slab_state, logdec, tok_rows):
    count = lax.axis_size("ctx")
    decay = jnp.exp(logdec * tok_rows)[:, None, None]
    sent = slab_state.astype(jnp.bfloat16)
    running = lax.ppermute(sent, "ctx", [(i, i + 1) for i in range(count - 1)]).astype(jnp.float32)
    if count > 2:
        two_back = lax.ppermute(sent, "ctx", [(i, i + 2) for i in range(count - 2)])
        running = running + two_back.astype(jnp.float32) * decay
    offset = 2
    while offset < count:
        pairs = [(i, i + offset) for i in range(count - offset)]
        moved = lax.ppermute(running.astype(jnp.bfloat16), "ctx", pairs).astype(jnp.float32)
        scale = jnp.exp(logdec * (tok_rows * offset))
        running = running + moved * scale[:, None, None]
        offset *= 2
    return running


def split_dot(spec, exact, wide):
    high = wide.astype(jnp.bfloat16)
    low = (wide - high.astype(jnp.float32)).astype(jnp.bfloat16)
    first = jnp.einsum(spec, exact, high, preferred_element_type=jnp.float32)
    return first + jnp.einsum(spec, exact, low, preferred_element_type=jnp.float32)


def local(
    ring,
    query_linear,
    key_linear,
    value_linear,
    gate_logits,
    norm_gain,
    decay_code,
    query_soft,
    key_soft,
    yarn_factor,
):
    tok_rows, head_count, head_width = query_linear.shape
    my_slab = lax.axis_index("ctx")
    freq, logit_scale = yarn_table(yarn_factor, head_width)
    first_row = my_slab * tok_rows
    query_pos = first_row + jnp.arange(tok_rows, dtype=jnp.int32)
    positions = query_pos.astype(jnp.float32)
    query_rot = rotate(query_soft, positions, freq)
    key_rot = rotate(key_soft, positions, freq)
    count = len(ring)
    ring_table = jnp.asarray(ring, jnp.int32)
    spot_table = jnp.asarray(np.argsort(np.asarray(ring)), jnp.int32)
    my_spot = spot_table[my_slab]
    forward = [(ring[i], ring[(i + 1) % count]) for i in range(count)]
    backward = [(ring[i], ring[(i - 1) % count]) for i in range(count)]
    steps = []
    for step in range(1, count // 2 + 1):
        moves = [("ahead", forward, ring_table[(my_spot - step) % count])]
        if 2 * step == count:
            moves = [("split", None, moves[0][2])]
        else:
            moves.append(("behind", backward, ring_table[(my_spot + step) % count]))
        steps.append(moves)
    half = head_count // 2

    def travel(name, pairs):
        if name != "split":
            held[name] = lax.ppermute(held[name], "ctx", pairs)
            return held[name]
        front = lax.ppermute(held["ahead"][:, :half], "ctx", forward)
        back = lax.ppermute(held["behind"][:, half:], "ctx", backward)
        return jnp.concatenate([front, back], axis=1)

    def score_chunk(keys_in, slab):
        raw = jnp.einsum("thd,shd->hts", query_rot, keys_in, preferred_element_type=jnp.float32)
        key_pos = slab * tok_rows + jnp.arange(tok_rows, dtype=jnp.int32)
        allowed = key_pos[None, :] <= query_pos[:, None]
        return jnp.where(allowed[None], raw * logit_scale, -jnp.inf)

    held = {"ahead": key_rot, "behind": key_rot}
    score_chunks = [score_chunk(key_rot, my_slab)]

    def key_step(moves):
        for name, pairs, slab in moves:
            score_chunks.append(score_chunk(travel(name, pairs), slab))

    early = 0
    for moves in steps[:early]:
        key_step(moves)
    logdec = jnp.log1p(-decay_code.astype(jnp.float32) * 2.0 ** (-20))
    q_hat = jax.nn.silu(query_linear.astype(jnp.float32)).astype(jnp.bfloat16)
    k_hat = jax.nn.silu(key_linear.astype(jnp.float32)).astype(jnp.bfloat16)
    slab_state, local_out = lightning_local(q_hat, k_hat, value_linear, logdec)
    incoming = exclusive_scan(slab_state, logdec, tok_rows)
    ring_keys = (held["ahead"], held["behind"])
    ring_keys, incoming = lax.optimization_barrier((ring_keys, incoming))
    held["ahead"], held["behind"] = ring_keys
    for moves in steps[early:]:
        key_step(moves)
    local_pos = jnp.arange(tok_rows, dtype=jnp.float32)
    query_decay = jnp.exp(logdec[None, :] * (local_pos[:, None] + 1.0))
    carried = query_decay[:, :, None] * split_dot("thd,hde->the", q_hat, incoming)
    linear_out = local_out + carried
    square_sum = jnp.sum(linear_out * linear_out, axis=(1, 2))
    total_square = lax.psum(square_sum, "head")
    mean_sq = total_square / (head_count * lax.axis_size("head") * head_width)
    normed = (
        linear_out
        * lax.rsqrt(mean_sq + norm_eps)[:, None, None]
        * norm_gain[None]
        * jax.nn.sigmoid(gate_logits.astype(jnp.float32))
    )
    values_soft = normed.astype(jnp.bfloat16)
    ring_keys = (held["ahead"], held["behind"])
    ring_keys, values_soft = lax.optimization_barrier((ring_keys, values_soft))
    top = score_chunks[0].max(axis=2)
    for chunk in score_chunks[1:]:
        top = jnp.maximum(top, chunk.max(axis=2))
    prob_chunks = [jnp.exp(chunk - top[:, :, None]) for chunk in score_chunks]
    total = prob_chunks[0].sum(axis=2)
    for chunk in prob_chunks[1:]:
        total = total + chunk.sum(axis=2)
    weight_chunks = [chunk.astype(jnp.bfloat16) for chunk in prob_chunks]

    held = {"ahead": values_soft, "behind": values_soft}
    accum = jnp.einsum(
        "hts,shd->htd", weight_chunks[0], values_soft, preferred_element_type=jnp.float32
    )
    chunk_at = 1
    for moves in steps:
        for name, pairs, slab in moves:
            accum = accum + jnp.einsum(
                "hts,shd->htd",
                weight_chunks[chunk_at],
                travel(name, pairs),
                preferred_element_type=jnp.float32,
            )
            chunk_at += 1
    result = accum / total[:, :, None]
    return result.transpose(1, 0, 2).astype(jnp.bfloat16)


def ring_of(mesh):
    devices = np.moveaxis(np.asarray(mesh.devices), mesh.axis_names.index("ctx"), 0)
    line = devices.reshape(devices.shape[0], -1)[:, 0]
    count = len(line)
    try:
        spots = [tuple(int(v) for v in dev.coords) for dev in line]
    except (AttributeError, TypeError):
        return list(range(count))
    varying = [k for k in range(len(spots[0])) if len({s[k] for s in spots}) > 1]
    if len(varying) != 2:
        return sorted(range(count), key=lambda c: spots[c])
    varying.sort(key=lambda k: len({s[k] for s in spots}))
    outer, inner = varying
    order = []
    for turn, value in enumerate(sorted({s[outer] for s in spots})):
        members = [c for c in range(count) if spots[c][outer] == value]
        members.sort(key=lambda c: spots[c][inner], reverse=turn % 2 == 1)
        order += members
    return order


def solution(mesh):
    in_specs = (
        P(("groups", "ctx"), "head", None),
        P(("groups", "ctx"), "head", None),
        P(("groups", "ctx"), "head", None),
        P(("groups", "ctx"), "head", None),
        P("head", None),
        P("head"),
        P(("groups", "ctx"), "head", None),
        P(("groups", "ctx"), "head", None),
        P(),
    )
    out_specs = P(("groups", "ctx"), "head", None)
    body = functools.partial(local, ring_of(mesh))
    return jax.shard_map(body, mesh=mesh, in_specs=in_specs, out_specs=out_specs, check_vma=False)
```

```python
import functools
import math

import jax
import numpy as np
import jax.numpy as jnp
from jax import lax
from jax.sharding import PartitionSpec as P

BLOCK = 64
ORIG_CTX = 8192


rope_base = 10000.0
beta_fast = 32.0
beta_slow = 1.0
norm_eps = 1e-05
low_floor = -1e30


def yarn_table(yarn_factor, head_width):
    factor = yarn_factor[0].astype(jnp.float32)
    pair_ids = jnp.arange(head_width // 2, dtype=jnp.float32)
    base_freq = rope_base ** (-2.0 * pair_ids / head_width)
    wavelength = 2.0 * math.pi / base_freq
    ramp = jnp.clip((ORIG_CTX / wavelength - beta_slow) / (beta_fast - beta_slow), 0.0, 1.0)
    freq = base_freq * (ramp + (1.0 - ramp) / factor)
    mscale = 0.1 * jnp.log(factor) + 1.0
    return (freq, mscale * mscale / math.sqrt(head_width))


def rotate(values_in, positions, freq):
    angle = positions[:, None] * freq[None, :]
    cosine = jnp.cos(angle)[:, None, :]
    sine = jnp.sin(angle)[:, None, :]
    half_width = values_in.shape[2] // 2
    first = values_in[:, :, :half_width].astype(jnp.float32)
    second = values_in[:, :, half_width:].astype(jnp.float32)
    joined = jnp.concatenate(
        [first * cosine - second * sine, second * cosine + first * sine], axis=2
    )
    return joined.astype(jnp.bfloat16)


def lightning_local(q_hat, k_hat, value_linear, logdec):
    tok_rows, head_count, head_width = q_hat.shape
    block_count = tok_rows // BLOCK
    offsets = jnp.arange(BLOCK, dtype=jnp.float32)
    step_gap = offsets[:, None] - offsets[None, :]
    causal = step_gap >= 0
    intra_decay = jnp.where(
        causal[None], jnp.exp(logdec[:, None, None] * jnp.where(causal, step_gap, 0.0)[None]), 0.0
    )
    query_decay = jnp.exp(logdec[None, :] * (offsets[:, None] + 1.0))
    key_decay = jnp.exp(logdec[None, :] * (BLOCK - 1.0 - offsets[:, None]))
    block_decay = jnp.exp(logdec * BLOCK)

    def advance(carry_state, inputs):
        q_block, k_block, v_block = inputs
        scores = jnp.einsum("thd,shd->hts", q_block, k_block, preferred_element_type=jnp.float32)
        weights = (scores * intra_decay).astype(jnp.bfloat16)
        intra_part = jnp.einsum(
            "hts,shd->thd", weights, v_block, preferred_element_type=jnp.float32
        )
        carried = query_decay[:, :, None] * split_dot("thd,hde->the", q_block, carry_state)
        fresh_state = split_dot(
            "thd,the->hde", k_block, key_decay[:, :, None] * v_block.astype(jnp.float32)
        )
        return (carry_state * block_decay[:, None, None] + fresh_state, intra_part + carried)

    def split_blocks(array_in):
        return array_in.reshape(block_count, BLOCK, head_count, head_width)

    zero_state = jnp.zeros((head_count, head_width, head_width), jnp.float32)
    final_state, outputs = lax.scan(
        advance,
        zero_state,
        (split_blocks(q_hat), split_blocks(k_hat), split_blocks(value_linear)),
        unroll=True,
    )
    return (final_state, outputs.reshape(tok_rows, head_count, head_width))


def exclusive_scan(slab_state, logdec, tok_rows):
    count = lax.axis_size("ctx")
    decay = jnp.exp(logdec * tok_rows)[:, None, None]
    sent = slab_state.astype(jnp.bfloat16)
    running = lax.ppermute(sent, "ctx", [(i, i + 1) for i in range(count - 1)]).astype(jnp.float32)
    if count > 2:
        two_back = lax.ppermute(sent, "ctx", [(i, i + 2) for i in range(count - 2)])
        running = running + two_back.astype(jnp.float32) * decay
    offset = 2
    while offset < count:
        pairs = [(i, i + offset) for i in range(count - offset)]
        moved = lax.ppermute(running.astype(jnp.bfloat16), "ctx", pairs).astype(jnp.float32)
        scale = jnp.exp(logdec * (tok_rows * offset))
        running = running + moved * scale[:, None, None]
        offset *= 2
    return running


def split_dot(spec, exact, wide):
    high = wide.astype(jnp.bfloat16)
    low = (wide - high.astype(jnp.float32)).astype(jnp.bfloat16)
    first = jnp.einsum(spec, exact, high, preferred_element_type=jnp.float32)
    return first + jnp.einsum(spec, exact, low, preferred_element_type=jnp.float32)


def local(
    ring,
    query_linear,
    key_linear,
    value_linear,
    gate_logits,
    norm_gain,
    decay_code,
    query_soft,
    key_soft,
    yarn_factor,
):
    tok_rows, head_count, head_width = query_linear.shape
    my_slab = lax.axis_index("ctx")
    freq, logit_scale = yarn_table(yarn_factor, head_width)
    first_row = my_slab * tok_rows
    query_pos = first_row + jnp.arange(tok_rows, dtype=jnp.int32)
    positions = query_pos.astype(jnp.float32)
    query_rot = rotate(query_soft, positions, freq)
    key_rot = rotate(key_soft, positions, freq)
    count = len(ring)
    ring_table = jnp.asarray(ring, jnp.int32)
    spot_table = jnp.asarray(np.argsort(np.asarray(ring)), jnp.int32)
    my_spot = spot_table[my_slab]
    forward = [(ring[i], ring[(i + 1) % count]) for i in range(count)]
    last = count // 2

    def wanted(origin, step, sign):
        return any(ring[(origin + sign * j) % count] > ring[origin] for j in range(step, last + 1))

    def hops(step, sign):
        return [
            (ring[(q + sign * (step - 1)) % count], ring[(q + sign * step) % count])
            for q in range(count)
            if wanted(q, step, sign)
        ]

    steps = []
    for step in range(1, last + 1):
        source = ring_table[(my_spot - step) % count]
        if 2 * step == count:
            moves = [("split", (hops(step, 1), hops(step, -1)), source)]
        else:
            moves = [("ahead", hops(step, 1), source)]
            moves.append(("behind", hops(step, -1), ring_table[(my_spot + step) % count]))
        steps.append(moves)
    half = head_count // 2

    def send(block, pairs):
        if not pairs:
            return jnp.zeros_like(block)
        return lax.ppermute(block, "ctx", pairs)

    def travel(name, pairs):
        if name != "split":
            held[name] = send(held[name], pairs)
            return held[name]
        front = send(held["ahead"][:, :half], pairs[0])
        back = send(held["behind"][:, half:], pairs[1])
        return jnp.concatenate([front, back], axis=1)

    def score_chunk(keys_in, slab):
        raw = jnp.einsum("thd,shd->hts", query_rot, keys_in, preferred_element_type=jnp.float32)
        key_pos = slab * tok_rows + jnp.arange(tok_rows, dtype=jnp.int32)
        allowed = key_pos[None, :] <= query_pos[:, None]
        return jnp.where(allowed[None], raw * logit_scale, -jnp.inf)

    held = {"ahead": key_rot, "behind": key_rot}
    score_chunks = [score_chunk(key_rot, my_slab)]

    def key_step(moves):
        for name, pairs, slab in moves:
            score_chunks.append(score_chunk(travel(name, pairs), slab))

    early = (len(steps) + 1) // 2
    for moves in steps[:early]:
        key_step(moves)
    logdec = jnp.log1p(-decay_code.astype(jnp.float32) * 2.0 ** (-20))
    q_hat = jax.nn.silu(query_linear.astype(jnp.float32)).astype(jnp.bfloat16)
    k_hat = jax.nn.silu(key_linear.astype(jnp.float32)).astype(jnp.bfloat16)
    slab_state, local_out = lightning_local(q_hat, k_hat, value_linear, logdec)
    for moves in steps[early:]:
        key_step(moves)
    incoming = exclusive_scan(slab_state, logdec, tok_rows)
    local_pos = jnp.arange(tok_rows, dtype=jnp.float32)
    query_decay = jnp.exp(logdec[None, :] * (local_pos[:, None] + 1.0))
    carried = query_decay[:, :, None] * split_dot("thd,hde->the", q_hat, incoming)
    linear_out = local_out + carried
    square_sum = jnp.sum(linear_out * linear_out, axis=(1, 2))
    total_square = lax.psum(square_sum, "head")
    mean_sq = total_square / (head_count * lax.axis_size("head") * head_width)
    normed = (
        linear_out
        * lax.rsqrt(mean_sq + norm_eps)[:, None, None]
        * norm_gain[None]
        * jax.nn.sigmoid(gate_logits.astype(jnp.float32))
    )
    values_soft = normed.astype(jnp.bfloat16)
    ring_keys = (held["ahead"], held["behind"])
    ring_keys, values_soft = lax.optimization_barrier((ring_keys, values_soft))
    top = score_chunks[0].max(axis=2)
    for chunk in score_chunks[1:]:
        top = jnp.maximum(top, chunk.max(axis=2))
    prob_chunks = [jnp.exp(chunk - top[:, :, None]) for chunk in score_chunks]
    total = prob_chunks[0].sum(axis=2)
    for chunk in prob_chunks[1:]:
        total = total + chunk.sum(axis=2)
    weight_chunks = [chunk.astype(jnp.bfloat16) for chunk in prob_chunks]

    held = {"ahead": values_soft, "behind": values_soft}
    accum = jnp.einsum(
        "hts,shd->htd", weight_chunks[0], values_soft, preferred_element_type=jnp.float32
    )
    chunk_at = 1
    for moves in steps:
        for name, pairs, slab in moves:
            accum = accum + jnp.einsum(
                "hts,shd->htd",
                weight_chunks[chunk_at],
                travel(name, pairs),
                preferred_element_type=jnp.float32,
            )
            chunk_at += 1
    result = accum / total[:, :, None]
    return result.transpose(1, 0, 2).astype(jnp.bfloat16)


def ring_of(mesh):
    devices = np.moveaxis(np.asarray(mesh.devices), mesh.axis_names.index("ctx"), 0)
    line = devices.reshape(devices.shape[0], -1)[:, 0]
    count = len(line)
    try:
        spots = [tuple(int(v) for v in dev.coords) for dev in line]
    except (AttributeError, TypeError):
        return list(range(count))
    varying = [k for k in range(len(spots[0])) if len({s[k] for s in spots}) > 1]
    if len(varying) != 2:
        return sorted(range(count), key=lambda c: spots[c])
    varying.sort(key=lambda k: len({s[k] for s in spots}))
    outer, inner = varying
    order = []
    for turn, value in enumerate(sorted({s[outer] for s in spots})):
        members = [c for c in range(count) if spots[c][outer] == value]
        members.sort(key=lambda c: spots[c][inner], reverse=turn % 2 == 1)
        order += members
    return order


def solution(mesh):
    in_specs = (
        P(("groups", "ctx"), "head", None),
        P(("groups", "ctx"), "head", None),
        P(("groups", "ctx"), "head", None),
        P(("groups", "ctx"), "head", None),
        P("head", None),
        P("head"),
        P(("groups", "ctx"), "head", None),
        P(("groups", "ctx"), "head", None),
        P(),
    )
    out_specs = P(("groups", "ctx"), "head", None)
    body = functools.partial(local, ring_of(mesh))
    return jax.shard_map(body, mesh=mesh, in_specs=in_specs, out_specs=out_specs, check_vma=False)
```

```python
import functools
import math

import jax
import numpy as np
import jax.numpy as jnp
from jax import lax
from jax.sharding import PartitionSpec as P

BLOCK = 64
ORIG_CTX = 8192


rope_base = 10000.0
beta_fast = 32.0
beta_slow = 1.0
norm_eps = 1e-05
low_floor = -1e30


def yarn_table(yarn_factor, head_width):
    factor = yarn_factor[0].astype(jnp.float32)
    pair_ids = jnp.arange(head_width // 2, dtype=jnp.float32)
    base_freq = rope_base ** (-2.0 * pair_ids / head_width)
    wavelength = 2.0 * math.pi / base_freq
    ramp = jnp.clip((ORIG_CTX / wavelength - beta_slow) / (beta_fast - beta_slow), 0.0, 1.0)
    freq = base_freq * (ramp + (1.0 - ramp) / factor)
    mscale = 0.1 * jnp.log(factor) + 1.0
    return (freq, mscale * mscale / math.sqrt(head_width))


def rotate(values_in, positions, freq):
    angle = positions[:, None] * freq[None, :]
    cosine = jnp.cos(angle)[:, None, :]
    sine = jnp.sin(angle)[:, None, :]
    half_width = values_in.shape[2] // 2
    first = values_in[:, :, :half_width].astype(jnp.float32)
    second = values_in[:, :, half_width:].astype(jnp.float32)
    joined = jnp.concatenate(
        [first * cosine - second * sine, second * cosine + first * sine], axis=2
    )
    return joined.astype(jnp.bfloat16)


def lightning_local(q_hat, k_hat, value_linear, logdec):
    tok_rows, head_count, head_width = q_hat.shape
    block_count = tok_rows // BLOCK
    offsets = jnp.arange(BLOCK, dtype=jnp.float32)
    step_gap = offsets[:, None] - offsets[None, :]
    causal = step_gap >= 0
    intra_decay = jnp.where(
        causal[None], jnp.exp(logdec[:, None, None] * jnp.where(causal, step_gap, 0.0)[None]), 0.0
    )
    query_decay = jnp.exp(logdec[None, :] * (offsets[:, None] + 1.0))
    key_decay = jnp.exp(logdec[None, :] * (BLOCK - 1.0 - offsets[:, None]))
    block_decay = jnp.exp(logdec * BLOCK)

    def advance(carry_state, inputs):
        q_block, k_block, v_block = inputs
        scores = jnp.einsum("thd,shd->hts", q_block, k_block, preferred_element_type=jnp.float32)
        weights = (scores * intra_decay).astype(jnp.bfloat16)
        intra_part = jnp.einsum(
            "hts,shd->thd", weights, v_block, preferred_element_type=jnp.float32
        )
        carried = query_decay[:, :, None] * split_dot("thd,hde->the", q_block, carry_state)
        fresh_state = split_dot(
            "thd,the->hde", k_block, key_decay[:, :, None] * v_block.astype(jnp.float32)
        )
        return (carry_state * block_decay[:, None, None] + fresh_state, intra_part + carried)

    def split_blocks(array_in):
        return array_in.reshape(block_count, BLOCK, head_count, head_width)

    zero_state = jnp.zeros((head_count, head_width, head_width), jnp.float32)
    final_state, outputs = lax.scan(
        advance,
        zero_state,
        (split_blocks(q_hat), split_blocks(k_hat), split_blocks(value_linear)),
        unroll=True,
    )
    return (final_state, outputs.reshape(tok_rows, head_count, head_width))


def exclusive_scan(slab_state, logdec, tok_rows):
    count = lax.axis_size("ctx")
    decay = jnp.exp(logdec * tok_rows)[:, None, None]
    sent = slab_state.astype(jnp.bfloat16)
    running = lax.ppermute(sent, "ctx", [(i, i + 1) for i in range(count - 1)]).astype(jnp.float32)
    if count > 2:
        two_back = lax.ppermute(sent, "ctx", [(i, i + 2) for i in range(count - 2)])
        running = running + two_back.astype(jnp.float32) * decay
    offset = 2
    while offset < count:
        pairs = [(i, i + offset) for i in range(count - offset)]
        moved = lax.ppermute(running.astype(jnp.bfloat16), "ctx", pairs).astype(jnp.float32)
        scale = jnp.exp(logdec * (tok_rows * offset))
        running = running + moved * scale[:, None, None]
        offset *= 2
    return running


def split_dot(spec, exact, wide):
    high = wide.astype(jnp.bfloat16)
    low = (wide - high.astype(jnp.float32)).astype(jnp.bfloat16)
    first = jnp.einsum(spec, exact, high, preferred_element_type=jnp.float32)
    return first + jnp.einsum(spec, exact, low, preferred_element_type=jnp.float32)


def local(
    ring,
    query_linear,
    key_linear,
    value_linear,
    gate_logits,
    norm_gain,
    decay_code,
    query_soft,
    key_soft,
    yarn_factor,
):
    tok_rows, head_count, head_width = query_linear.shape
    my_slab = lax.axis_index("ctx")
    freq, logit_scale = yarn_table(yarn_factor, head_width)
    first_row = my_slab * tok_rows
    query_pos = first_row + jnp.arange(tok_rows, dtype=jnp.int32)
    positions = query_pos.astype(jnp.float32)
    query_rot = rotate(query_soft, positions, freq)
    key_rot = rotate(key_soft, positions, freq)
    count = len(ring)
    ring_table = jnp.asarray(ring, jnp.int32)
    spot_table = jnp.asarray(np.argsort(np.asarray(ring)), jnp.int32)
    my_spot = spot_table[my_slab]
    forward = [(ring[i], ring[(i + 1) % count]) for i in range(count)]
    backward = [(ring[i], ring[(i - 1) % count]) for i in range(count)]
    steps = []
    for step in range(1, count // 2 + 1):
        moves = [("ahead", forward, ring_table[(my_spot - step) % count])]
        if 2 * step == count:
            moves = [("split", None, moves[0][2])]
        else:
            moves.append(("behind", backward, ring_table[(my_spot + step) % count]))
        steps.append(moves)
    half = head_count // 2

    def travel(name, pairs):
        if name != "split":
            held[name] = lax.ppermute(held[name], "ctx", pairs)
            return held[name]
        front = lax.ppermute(held["ahead"][:, :half], "ctx", forward)
        back = lax.ppermute(held["behind"][:, half:], "ctx", backward)
        return jnp.concatenate([front, back], axis=1)

    def score_chunk(keys_in, slab):
        raw = jnp.einsum("thd,shd->hts", query_rot, keys_in, preferred_element_type=jnp.float32)
        key_pos = slab * tok_rows + jnp.arange(tok_rows, dtype=jnp.int32)
        allowed = key_pos[None, :] <= query_pos[:, None]
        return jnp.where(allowed[None], raw * logit_scale, -jnp.inf)

    held = {"ahead": key_rot, "behind": key_rot}
    score_chunks = [score_chunk(key_rot, my_slab)]

    def key_step(moves):
        for name, pairs, slab in moves:
            score_chunks.append(score_chunk(travel(name, pairs), slab))

    early = (len(steps) + 1) // 2
    for moves in steps[:early]:
        key_step(moves)
    gate_keys = (held["ahead"], held["behind"])
    logdec = jnp.log1p(-decay_code.astype(jnp.float32) * 2.0 ** (-20))
    q_hat = jax.nn.silu(query_linear.astype(jnp.float32)).astype(jnp.bfloat16)
    k_hat = jax.nn.silu(key_linear.astype(jnp.float32)).astype(jnp.bfloat16)
    slab_state, local_out = lightning_local(q_hat, k_hat, value_linear, logdec)
    for moves in steps[early:]:
        key_step(moves)
    incoming = exclusive_scan(slab_state, logdec, tok_rows)
    local_pos = jnp.arange(tok_rows, dtype=jnp.float32)
    query_decay = jnp.exp(logdec[None, :] * (local_pos[:, None] + 1.0))
    carried = query_decay[:, :, None] * split_dot("thd,hde->the", q_hat, incoming)
    linear_out = local_out + carried
    square_sum = jnp.sum(linear_out * linear_out, axis=(1, 2))
    total_square = lax.psum(square_sum, "head")
    mean_sq = total_square / (head_count * lax.axis_size("head") * head_width)
    normed = (
        linear_out
        * lax.rsqrt(mean_sq + norm_eps)[:, None, None]
        * norm_gain[None]
        * jax.nn.sigmoid(gate_logits.astype(jnp.float32))
    )
    values_soft = normed.astype(jnp.bfloat16)
    gate_keys, values_soft = lax.optimization_barrier((gate_keys, values_soft))
    top = score_chunks[0].max(axis=2)
    for chunk in score_chunks[1:]:
        top = jnp.maximum(top, chunk.max(axis=2))
    prob_chunks = [jnp.exp(chunk - top[:, :, None]) for chunk in score_chunks]
    total = prob_chunks[0].sum(axis=2)
    for chunk in prob_chunks[1:]:
        total = total + chunk.sum(axis=2)
    weight_chunks = [chunk.astype(jnp.bfloat16) for chunk in prob_chunks]

    held = {"ahead": values_soft, "behind": values_soft}
    accum = jnp.einsum(
        "hts,shd->htd", weight_chunks[0], values_soft, preferred_element_type=jnp.float32
    )
    chunk_at = 1
    for moves in steps:
        for name, pairs, slab in moves:
            accum = accum + jnp.einsum(
                "hts,shd->htd",
                weight_chunks[chunk_at],
                travel(name, pairs),
                preferred_element_type=jnp.float32,
            )
            chunk_at += 1
    result = accum / total[:, :, None]
    return result.transpose(1, 0, 2).astype(jnp.bfloat16)


def ring_of(mesh):
    devices = np.moveaxis(np.asarray(mesh.devices), mesh.axis_names.index("ctx"), 0)
    line = devices.reshape(devices.shape[0], -1)[:, 0]
    count = len(line)
    try:
        spots = [tuple(int(v) for v in dev.coords) for dev in line]
    except (AttributeError, TypeError):
        return list(range(count))
    varying = [k for k in range(len(spots[0])) if len({s[k] for s in spots}) > 1]
    if len(varying) != 2:
        return sorted(range(count), key=lambda c: spots[c])
    varying.sort(key=lambda k: len({s[k] for s in spots}))
    outer, inner = varying
    order = []
    for turn, value in enumerate(sorted({s[outer] for s in spots})):
        members = [c for c in range(count) if spots[c][outer] == value]
        members.sort(key=lambda c: spots[c][inner], reverse=turn % 2 == 1)
        order += members
    return order


def solution(mesh):
    in_specs = (
        P(("groups", "ctx"), "head", None),
        P(("groups", "ctx"), "head", None),
        P(("groups", "ctx"), "head", None),
        P(("groups", "ctx"), "head", None),
        P("head", None),
        P("head"),
        P(("groups", "ctx"), "head", None),
        P(("groups", "ctx"), "head", None),
        P(),
    )
    out_specs = P(("groups", "ctx"), "head", None)
    body = functools.partial(local, ring_of(mesh))
    return jax.shard_map(body, mesh=mesh, in_specs=in_specs, out_specs=out_specs, check_vma=False)
```

```python
import functools
import math

import jax
import numpy as np
import jax.numpy as jnp
from jax import lax
from jax.sharding import PartitionSpec as P

BLOCK = 64
ORIG_CTX = 8192


rope_base = 10000.0
beta_fast = 32.0
beta_slow = 1.0
norm_eps = 1e-05
low_floor = -1e30


def yarn_table(yarn_factor, head_width):
    factor = yarn_factor[0].astype(jnp.float32)
    pair_ids = jnp.arange(head_width // 2, dtype=jnp.float32)
    base_freq = rope_base ** (-2.0 * pair_ids / head_width)
    wavelength = 2.0 * math.pi / base_freq
    ramp = jnp.clip((ORIG_CTX / wavelength - beta_slow) / (beta_fast - beta_slow), 0.0, 1.0)
    freq = base_freq * (ramp + (1.0 - ramp) / factor)
    mscale = 0.1 * jnp.log(factor) + 1.0
    return (freq, mscale * mscale / math.sqrt(head_width))


def rotate(values_in, positions, freq):
    angle = positions[:, None] * freq[None, :]
    cosine = jnp.cos(angle)[:, None, :]
    sine = jnp.sin(angle)[:, None, :]
    half_width = values_in.shape[2] // 2
    first = values_in[:, :, :half_width].astype(jnp.float32)
    second = values_in[:, :, half_width:].astype(jnp.float32)
    joined = jnp.concatenate(
        [first * cosine - second * sine, second * cosine + first * sine], axis=2
    )
    return joined.astype(jnp.bfloat16)


def lightning_local(q_hat, k_hat, value_linear, logdec):
    tok_rows, head_count, head_width = q_hat.shape
    block_count = tok_rows // BLOCK
    offsets = jnp.arange(BLOCK, dtype=jnp.float32)
    step_gap = offsets[:, None] - offsets[None, :]
    causal = step_gap >= 0
    intra_decay = jnp.where(
        causal[None], jnp.exp(logdec[:, None, None] * jnp.where(causal, step_gap, 0.0)[None]), 0.0
    )
    query_decay = jnp.exp(logdec[None, :] * (offsets[:, None] + 1.0))
    key_decay = jnp.exp(logdec[None, :] * (BLOCK - 1.0 - offsets[:, None]))
    block_decay = jnp.exp(logdec * BLOCK)

    def split_blocks(array_in):
        return array_in.reshape(block_count, BLOCK, head_count, head_width)

    q_blocks, k_blocks, v_blocks = (split_blocks(x) for x in (q_hat, k_hat, value_linear))
    scores = jnp.einsum("bthd,bshd->bhts", q_blocks, k_blocks, preferred_element_type=jnp.float32)
    weights = (scores * intra_decay[None]).astype(jnp.bfloat16)
    intra_part = jnp.einsum(
        "bhts,bshd->bthd", weights, v_blocks, preferred_element_type=jnp.float32
    )
    fresh = split_dot(
        "bthd,bthe->bhde",
        k_blocks,
        key_decay[None, :, :, None] * v_blocks.astype(jnp.float32),
    )
    carry_state = jnp.zeros((head_count, head_width, head_width), jnp.float32)
    carries = []
    for block in range(block_count):
        carries.append(carry_state)
        carry_state = carry_state * block_decay[:, None, None] + fresh[block]
    carried = query_decay[None, :, :, None] * split_dot(
        "bthd,bhde->bthe", q_blocks, jnp.stack(carries)
    )
    outputs = intra_part + carried
    return (carry_state, outputs.reshape(tok_rows, head_count, head_width))


def exclusive_scan(slab_state, logdec, tok_rows):
    count = lax.axis_size("ctx")
    decay = jnp.exp(logdec * tok_rows)[:, None, None]
    sent = slab_state.astype(jnp.bfloat16)
    running = lax.ppermute(sent, "ctx", [(i, i + 1) for i in range(count - 1)]).astype(jnp.float32)
    if count > 2:
        two_back = lax.ppermute(sent, "ctx", [(i, i + 2) for i in range(count - 2)])
        running = running + two_back.astype(jnp.float32) * decay
    offset = 2
    while offset < count:
        pairs = [(i, i + offset) for i in range(count - offset)]
        moved = lax.ppermute(running.astype(jnp.bfloat16), "ctx", pairs).astype(jnp.float32)
        scale = jnp.exp(logdec * (tok_rows * offset))
        running = running + moved * scale[:, None, None]
        offset *= 2
    return running


def split_dot(spec, exact, wide):
    high = wide.astype(jnp.bfloat16)
    low = (wide - high.astype(jnp.float32)).astype(jnp.bfloat16)
    first = jnp.einsum(spec, exact, high, preferred_element_type=jnp.float32)
    return first + jnp.einsum(spec, exact, low, preferred_element_type=jnp.float32)


def local(
    ring,
    query_linear,
    key_linear,
    value_linear,
    gate_logits,
    norm_gain,
    decay_code,
    query_soft,
    key_soft,
    yarn_factor,
):
    tok_rows, head_count, head_width = query_linear.shape
    my_slab = lax.axis_index("ctx")
    freq, logit_scale = yarn_table(yarn_factor, head_width)
    first_row = my_slab * tok_rows
    query_pos = first_row + jnp.arange(tok_rows, dtype=jnp.int32)
    positions = query_pos.astype(jnp.float32)
    query_rot = rotate(query_soft, positions, freq)
    key_rot = rotate(key_soft, positions, freq)
    count = len(ring)
    ring_table = jnp.asarray(ring, jnp.int32)
    spot_table = jnp.asarray(np.argsort(np.asarray(ring)), jnp.int32)
    my_spot = spot_table[my_slab]
    forward = [(ring[i], ring[(i + 1) % count]) for i in range(count)]
    backward = [(ring[i], ring[(i - 1) % count]) for i in range(count)]
    steps = []
    for step in range(1, count // 2 + 1):
        moves = [("ahead", forward, ring_table[(my_spot - step) % count])]
        if 2 * step == count:
            moves = [("split", None, moves[0][2])]
        else:
            moves.append(("behind", backward, ring_table[(my_spot + step) % count]))
        steps.append(moves)
    half = head_count // 2

    def travel(name, pairs):
        if name != "split":
            held[name] = lax.ppermute(held[name], "ctx", pairs)
            return held[name]
        front = lax.ppermute(held["ahead"][:, :half], "ctx", forward)
        back = lax.ppermute(held["behind"][:, half:], "ctx", backward)
        return jnp.concatenate([front, back], axis=1)

    def score_chunk(keys_in, slab):
        raw = jnp.einsum("thd,shd->hts", query_rot, keys_in, preferred_element_type=jnp.float32)
        key_pos = slab * tok_rows + jnp.arange(tok_rows, dtype=jnp.int32)
        allowed = key_pos[None, :] <= query_pos[:, None]
        return jnp.where(allowed[None], raw * logit_scale, -jnp.inf)

    held = {"ahead": key_rot, "behind": key_rot}
    score_chunks = [score_chunk(key_rot, my_slab)]

    def key_step(moves):
        for name, pairs, slab in moves:
            score_chunks.append(score_chunk(travel(name, pairs), slab))

    early = (len(steps) + 1) // 2
    for moves in steps[:early]:
        key_step(moves)
    gate_keys = (held["ahead"], held["behind"])
    logdec = jnp.log1p(-decay_code.astype(jnp.float32) * 2.0 ** (-20))
    q_hat = jax.nn.silu(query_linear.astype(jnp.float32)).astype(jnp.bfloat16)
    k_hat = jax.nn.silu(key_linear.astype(jnp.float32)).astype(jnp.bfloat16)
    slab_state, local_out = lightning_local(q_hat, k_hat, value_linear, logdec)
    for moves in steps[early:]:
        key_step(moves)
    incoming = exclusive_scan(slab_state, logdec, tok_rows)
    local_pos = jnp.arange(tok_rows, dtype=jnp.float32)
    query_decay = jnp.exp(logdec[None, :] * (local_pos[:, None] + 1.0))
    carried = query_decay[:, :, None] * split_dot("thd,hde->the", q_hat, incoming)
    linear_out = local_out + carried
    square_sum = jnp.sum(linear_out * linear_out, axis=(1, 2))
    total_square = lax.psum(square_sum, "head")
    mean_sq = total_square / (head_count * lax.axis_size("head") * head_width)
    normed = (
        linear_out
        * lax.rsqrt(mean_sq + norm_eps)[:, None, None]
        * norm_gain[None]
        * jax.nn.sigmoid(gate_logits.astype(jnp.float32))
    )
    values_soft = normed.astype(jnp.bfloat16)
    gate_keys, values_soft = lax.optimization_barrier((gate_keys, values_soft))
    top = score_chunks[0].max(axis=2)
    for chunk in score_chunks[1:]:
        top = jnp.maximum(top, chunk.max(axis=2))
    prob_chunks = [jnp.exp(chunk - top[:, :, None]) for chunk in score_chunks]
    total = prob_chunks[0].sum(axis=2)
    for chunk in prob_chunks[1:]:
        total = total + chunk.sum(axis=2)
    weight_chunks = [chunk.astype(jnp.bfloat16) for chunk in prob_chunks]

    held = {"ahead": values_soft, "behind": values_soft}
    accum = jnp.einsum(
        "hts,shd->htd", weight_chunks[0], values_soft, preferred_element_type=jnp.float32
    )
    chunk_at = 1
    for moves in steps:
        for name, pairs, slab in moves:
            accum = accum + jnp.einsum(
                "hts,shd->htd",
                weight_chunks[chunk_at],
                travel(name, pairs),
                preferred_element_type=jnp.float32,
            )
            chunk_at += 1
    result = accum / total[:, :, None]
    return result.transpose(1, 0, 2).astype(jnp.bfloat16)


def ring_of(mesh):
    devices = np.moveaxis(np.asarray(mesh.devices), mesh.axis_names.index("ctx"), 0)
    line = devices.reshape(devices.shape[0], -1)[:, 0]
    count = len(line)
    try:
        spots = [tuple(int(v) for v in dev.coords) for dev in line]
    except (AttributeError, TypeError):
        return list(range(count))
    varying = [k for k in range(len(spots[0])) if len({s[k] for s in spots}) > 1]
    if len(varying) != 2:
        return sorted(range(count), key=lambda c: spots[c])
    varying.sort(key=lambda k: len({s[k] for s in spots}))
    outer, inner = varying
    order = []
    for turn, value in enumerate(sorted({s[outer] for s in spots})):
        members = [c for c in range(count) if spots[c][outer] == value]
        members.sort(key=lambda c: spots[c][inner], reverse=turn % 2 == 1)
        order += members
    return order


def solution(mesh):
    in_specs = (
        P(("groups", "ctx"), "head", None),
        P(("groups", "ctx"), "head", None),
        P(("groups", "ctx"), "head", None),
        P(("groups", "ctx"), "head", None),
        P("head", None),
        P("head"),
        P(("groups", "ctx"), "head", None),
        P(("groups", "ctx"), "head", None),
        P(),
    )
    out_specs = P(("groups", "ctx"), "head", None)
    body = functools.partial(local, ring_of(mesh))
    return jax.shard_map(body, mesh=mesh, in_specs=in_specs, out_specs=out_specs, check_vma=False)
```

```python
import functools
import math

import jax
import numpy as np
import jax.numpy as jnp
from jax import lax
from jax.sharding import PartitionSpec as P

BLOCK = 64
ORIG_CTX = 8192


rope_base = 10000.0
beta_fast = 32.0
beta_slow = 1.0
norm_eps = 1e-05
low_floor = -1e30


def yarn_table(yarn_factor, head_width):
    factor = yarn_factor[0].astype(jnp.float32)
    pair_ids = jnp.arange(head_width // 2, dtype=jnp.float32)
    base_freq = rope_base ** (-2.0 * pair_ids / head_width)
    wavelength = 2.0 * math.pi / base_freq
    ramp = jnp.clip((ORIG_CTX / wavelength - beta_slow) / (beta_fast - beta_slow), 0.0, 1.0)
    freq = base_freq * (ramp + (1.0 - ramp) / factor)
    mscale = 0.1 * jnp.log(factor) + 1.0
    return (freq, mscale * mscale / math.sqrt(head_width))


def rotate(values_in, positions, freq):
    angle = positions[:, None] * freq[None, :]
    cosine = jnp.cos(angle)[:, None, :]
    sine = jnp.sin(angle)[:, None, :]
    half_width = values_in.shape[2] // 2
    first = values_in[:, :, :half_width].astype(jnp.float32)
    second = values_in[:, :, half_width:].astype(jnp.float32)
    joined = jnp.concatenate(
        [first * cosine - second * sine, second * cosine + first * sine], axis=2
    )
    return joined.astype(jnp.bfloat16)


def lightning_local(q_hat, k_hat, value_linear, logdec):
    tok_rows, head_count, head_width = q_hat.shape
    block_count = tok_rows // BLOCK
    offsets = jnp.arange(BLOCK, dtype=jnp.float32)
    step_gap = offsets[:, None] - offsets[None, :]
    causal = step_gap >= 0
    intra_decay = jnp.where(
        causal[None], jnp.exp(logdec[:, None, None] * jnp.where(causal, step_gap, 0.0)[None]), 0.0
    )
    query_decay = jnp.exp(logdec[None, :] * (offsets[:, None] + 1.0))
    key_decay = jnp.exp(logdec[None, :] * (BLOCK - 1.0 - offsets[:, None]))
    block_decay = jnp.exp(logdec * BLOCK)

    def advance(carry_state, inputs):
        q_block, k_block, v_block = inputs
        scores = jnp.einsum("thd,shd->hts", q_block, k_block, preferred_element_type=jnp.float32)
        weights = (scores * intra_decay).astype(jnp.bfloat16)
        intra_part = jnp.einsum(
            "hts,shd->thd", weights, v_block, preferred_element_type=jnp.float32
        )
        carried = query_decay[:, :, None] * split_dot("thd,hde->the", q_block, carry_state)
        fresh_state = split_dot(
            "thd,the->hde", k_block, key_decay[:, :, None] * v_block.astype(jnp.float32)
        )
        return (carry_state * block_decay[:, None, None] + fresh_state, intra_part + carried)

    def split_blocks(array_in):
        return array_in.reshape(block_count, BLOCK, head_count, head_width)

    zero_state = jnp.zeros((head_count, head_width, head_width), jnp.float32)
    final_state, outputs = lax.scan(
        advance,
        zero_state,
        (split_blocks(q_hat), split_blocks(k_hat), split_blocks(value_linear)),
        unroll=True,
    )
    return (final_state, outputs.reshape(tok_rows, head_count, head_width))


def exclusive_scan(slab_state, logdec, tok_rows):
    count = lax.axis_size("ctx")
    decay = jnp.exp(logdec * tok_rows)[:, None, None]
    sent = slab_state.astype(jnp.bfloat16)
    width = min(4, count - 1)
    running = None
    for shift in range(width, 0, -1):
        moved = lax.ppermute(sent, "ctx", [(i, i + shift) for i in range(count - shift)])
        running = moved.astype(jnp.float32) if running is None else running * decay + moved
    offset = width
    while offset < count:
        pairs = [(i, i + offset) for i in range(count - offset)]
        moved = lax.ppermute(running.astype(jnp.bfloat16), "ctx", pairs).astype(jnp.float32)
        scale = jnp.exp(logdec * (tok_rows * offset))
        running = running + moved * scale[:, None, None]
        offset *= 2
    return running


def split_dot(spec, exact, wide):
    high = wide.astype(jnp.bfloat16)
    low = (wide - high.astype(jnp.float32)).astype(jnp.bfloat16)
    first = jnp.einsum(spec, exact, high, preferred_element_type=jnp.float32)
    return first + jnp.einsum(spec, exact, low, preferred_element_type=jnp.float32)


def local(
    ring,
    query_linear,
    key_linear,
    value_linear,
    gate_logits,
    norm_gain,
    decay_code,
    query_soft,
    key_soft,
    yarn_factor,
):
    tok_rows, head_count, head_width = query_linear.shape
    my_slab = lax.axis_index("ctx")
    freq, logit_scale = yarn_table(yarn_factor, head_width)
    first_row = my_slab * tok_rows
    query_pos = first_row + jnp.arange(tok_rows, dtype=jnp.int32)
    positions = query_pos.astype(jnp.float32)
    query_rot = rotate(query_soft, positions, freq)
    key_rot = rotate(key_soft, positions, freq)
    count = len(ring)
    ring_table = jnp.asarray(ring, jnp.int32)
    spot_table = jnp.asarray(np.argsort(np.asarray(ring)), jnp.int32)
    my_spot = spot_table[my_slab]
    forward = [(ring[i], ring[(i + 1) % count]) for i in range(count)]
    backward = [(ring[i], ring[(i - 1) % count]) for i in range(count)]
    steps = []
    for step in range(1, count // 2 + 1):
        moves = [("ahead", forward, ring_table[(my_spot - step) % count])]
        if 2 * step == count:
            moves = [("split", None, moves[0][2])]
        else:
            moves.append(("behind", backward, ring_table[(my_spot + step) % count]))
        steps.append(moves)
    half = head_count // 2

    def travel(name, pairs):
        if name != "split":
            held[name] = lax.ppermute(held[name], "ctx", pairs)
            return held[name]
        front = lax.ppermute(held["ahead"][:, :half], "ctx", forward)
        back = lax.ppermute(held["behind"][:, half:], "ctx", backward)
        return jnp.concatenate([front, back], axis=1)

    def score_chunk(keys_in, slab):
        raw = jnp.einsum("thd,shd->hts", query_rot, keys_in, preferred_element_type=jnp.float32)
        key_pos = slab * tok_rows + jnp.arange(tok_rows, dtype=jnp.int32)
        allowed = key_pos[None, :] <= query_pos[:, None]
        return jnp.where(allowed[None], raw * logit_scale, -jnp.inf)

    held = {"ahead": key_rot, "behind": key_rot}
    score_chunks = [score_chunk(key_rot, my_slab)]

    def key_step(moves):
        for name, pairs, slab in moves:
            score_chunks.append(score_chunk(travel(name, pairs), slab))

    early = (len(steps) + 1) // 2
    for moves in steps[:early]:
        key_step(moves)
    gate_keys = (held["ahead"], held["behind"])
    logdec = jnp.log1p(-decay_code.astype(jnp.float32) * 2.0 ** (-20))
    q_hat = jax.nn.silu(query_linear.astype(jnp.float32)).astype(jnp.bfloat16)
    k_hat = jax.nn.silu(key_linear.astype(jnp.float32)).astype(jnp.bfloat16)
    slab_state, local_out = lightning_local(q_hat, k_hat, value_linear, logdec)
    for moves in steps[early:]:
        key_step(moves)
    incoming = exclusive_scan(slab_state, logdec, tok_rows)
    local_pos = jnp.arange(tok_rows, dtype=jnp.float32)
    query_decay = jnp.exp(logdec[None, :] * (local_pos[:, None] + 1.0))
    carried = query_decay[:, :, None] * split_dot("thd,hde->the", q_hat, incoming)
    linear_out = local_out + carried
    square_sum = jnp.sum(linear_out * linear_out, axis=(1, 2))
    total_square = lax.psum(square_sum, "head")
    mean_sq = total_square / (head_count * lax.axis_size("head") * head_width)
    normed = (
        linear_out
        * lax.rsqrt(mean_sq + norm_eps)[:, None, None]
        * norm_gain[None]
        * jax.nn.sigmoid(gate_logits.astype(jnp.float32))
    )
    values_soft = normed.astype(jnp.bfloat16)
    gate_keys, values_soft = lax.optimization_barrier((gate_keys, values_soft))
    top = score_chunks[0].max(axis=2)
    for chunk in score_chunks[1:]:
        top = jnp.maximum(top, chunk.max(axis=2))
    prob_chunks = [jnp.exp(chunk - top[:, :, None]) for chunk in score_chunks]
    total = prob_chunks[0].sum(axis=2)
    for chunk in prob_chunks[1:]:
        total = total + chunk.sum(axis=2)
    weight_chunks = [chunk.astype(jnp.bfloat16) for chunk in prob_chunks]

    held = {"ahead": values_soft, "behind": values_soft}
    accum = jnp.einsum(
        "hts,shd->htd", weight_chunks[0], values_soft, preferred_element_type=jnp.float32
    )
    chunk_at = 1
    for moves in steps:
        for name, pairs, slab in moves:
            accum = accum + jnp.einsum(
                "hts,shd->htd",
                weight_chunks[chunk_at],
                travel(name, pairs),
                preferred_element_type=jnp.float32,
            )
            chunk_at += 1
    result = accum / total[:, :, None]
    return result.transpose(1, 0, 2).astype(jnp.bfloat16)


def ring_of(mesh):
    devices = np.moveaxis(np.asarray(mesh.devices), mesh.axis_names.index("ctx"), 0)
    line = devices.reshape(devices.shape[0], -1)[:, 0]
    count = len(line)
    try:
        spots = [tuple(int(v) for v in dev.coords) for dev in line]
    except (AttributeError, TypeError):
        return list(range(count))
    varying = [k for k in range(len(spots[0])) if len({s[k] for s in spots}) > 1]
    if len(varying) != 2:
        return sorted(range(count), key=lambda c: spots[c])
    varying.sort(key=lambda k: len({s[k] for s in spots}))
    outer, inner = varying
    order = []
    for turn, value in enumerate(sorted({s[outer] for s in spots})):
        members = [c for c in range(count) if spots[c][outer] == value]
        members.sort(key=lambda c: spots[c][inner], reverse=turn % 2 == 1)
        order += members
    return order


def solution(mesh):
    in_specs = (
        P(("groups", "ctx"), "head", None),
        P(("groups", "ctx"), "head", None),
        P(("groups", "ctx"), "head", None),
        P(("groups", "ctx"), "head", None),
        P("head", None),
        P("head"),
        P(("groups", "ctx"), "head", None),
        P(("groups", "ctx"), "head", None),
        P(),
    )
    out_specs = P(("groups", "ctx"), "head", None)
    body = functools.partial(local, ring_of(mesh))
    return jax.shard_map(body, mesh=mesh, in_specs=in_specs, out_specs=out_specs, check_vma=False)
```

```python
import functools
import math

import jax
import numpy as np
import jax.numpy as jnp
from jax import lax
from jax.sharding import PartitionSpec as P

BLOCK = 64
ORIG_CTX = 8192


rope_base = 10000.0
beta_fast = 32.0
beta_slow = 1.0
norm_eps = 1e-05
low_floor = -1e30


def yarn_table(yarn_factor, head_width):
    factor = yarn_factor[0].astype(jnp.float32)
    pair_ids = jnp.arange(head_width // 2, dtype=jnp.float32)
    base_freq = rope_base ** (-2.0 * pair_ids / head_width)
    wavelength = 2.0 * math.pi / base_freq
    ramp = jnp.clip((ORIG_CTX / wavelength - beta_slow) / (beta_fast - beta_slow), 0.0, 1.0)
    freq = base_freq * (ramp + (1.0 - ramp) / factor)
    mscale = 0.1 * jnp.log(factor) + 1.0
    return (freq, mscale * mscale / math.sqrt(head_width))


def rotate(values_in, positions, freq):
    angle = positions[:, None] * freq[None, :]
    cosine = jnp.cos(angle)[:, None, :]
    sine = jnp.sin(angle)[:, None, :]
    half_width = values_in.shape[2] // 2
    first = values_in[:, :, :half_width].astype(jnp.float32)
    second = values_in[:, :, half_width:].astype(jnp.float32)
    joined = jnp.concatenate(
        [first * cosine - second * sine, second * cosine + first * sine], axis=2
    )
    return joined.astype(jnp.bfloat16)


def lightning_local(q_hat, k_hat, value_linear, logdec):
    tok_rows, head_count, head_width = q_hat.shape
    block_count = tok_rows // BLOCK
    offsets = jnp.arange(BLOCK, dtype=jnp.float32)
    step_gap = offsets[:, None] - offsets[None, :]
    causal = step_gap >= 0
    intra_decay = jnp.where(
        causal[None], jnp.exp(logdec[:, None, None] * jnp.where(causal, step_gap, 0.0)[None]), 0.0
    )
    query_decay = jnp.exp(logdec[None, :] * (offsets[:, None] + 1.0))
    key_decay = jnp.exp(logdec[None, :] * (BLOCK - 1.0 - offsets[:, None]))
    block_decay = jnp.exp(logdec * BLOCK)

    def advance(carry_state, inputs):
        q_block, k_block, v_block = inputs
        scores = jnp.einsum("thd,shd->hts", q_block, k_block, preferred_element_type=jnp.float32)
        weights = (scores * intra_decay).astype(jnp.bfloat16)
        intra_part = jnp.einsum(
            "hts,shd->thd", weights, v_block, preferred_element_type=jnp.float32
        )
        carried = query_decay[:, :, None] * split_dot("thd,hde->the", q_block, carry_state)
        fresh_state = split_dot(
            "thd,the->hde", k_block, key_decay[:, :, None] * v_block.astype(jnp.float32)
        )
        return (carry_state * block_decay[:, None, None] + fresh_state, intra_part + carried)

    def split_blocks(array_in):
        return array_in.reshape(block_count, BLOCK, head_count, head_width)

    zero_state = jnp.zeros((head_count, head_width, head_width), jnp.float32)
    final_state, outputs = lax.scan(
        advance,
        zero_state,
        (split_blocks(q_hat), split_blocks(k_hat), split_blocks(value_linear)),
        unroll=True,
    )
    return (final_state, outputs.reshape(tok_rows, head_count, head_width))


def exclusive_scan(slab_state, logdec, tok_rows):
    count = lax.axis_size("ctx")
    decay = jnp.exp(logdec * tok_rows)[:, None, None]
    sent = slab_state.astype(jnp.bfloat16)
    running = lax.ppermute(sent, "ctx", [(i, i + 1) for i in range(count - 1)]).astype(jnp.float32)
    if count > 2:
        two_back = lax.ppermute(sent, "ctx", [(i, i + 2) for i in range(count - 2)])
        running = running + two_back.astype(jnp.float32) * decay
    offset = 2
    while offset < count:
        pairs = [(i, i + offset) for i in range(count - offset)]
        moved = lax.ppermute(running.astype(jnp.bfloat16), "ctx", pairs).astype(jnp.float32)
        scale = jnp.exp(logdec * (tok_rows * offset))
        running = running + moved * scale[:, None, None]
        offset *= 2
    return running


def split_dot(spec, exact, wide):
    high = wide.astype(jnp.bfloat16)
    low = (wide - high.astype(jnp.float32)).astype(jnp.bfloat16)
    first = jnp.einsum(spec, exact, high, preferred_element_type=jnp.float32)
    return first + jnp.einsum(spec, exact, low, preferred_element_type=jnp.float32)


def local(
    ring,
    query_linear,
    key_linear,
    value_linear,
    gate_logits,
    norm_gain,
    decay_code,
    query_soft,
    key_soft,
    yarn_factor,
):
    tok_rows, head_count, head_width = query_linear.shape
    my_slab = lax.axis_index("ctx")
    freq, logit_scale = yarn_table(yarn_factor, head_width)
    first_row = my_slab * tok_rows
    query_pos = first_row + jnp.arange(tok_rows, dtype=jnp.int32)
    positions = query_pos.astype(jnp.float32)
    query_rot = rotate(query_soft, positions, freq)
    key_rot = rotate(key_soft, positions, freq)
    count = len(ring)
    ring_table = jnp.asarray(ring, jnp.int32)
    spot_table = jnp.asarray(np.argsort(np.asarray(ring)), jnp.int32)
    my_spot = spot_table[my_slab]
    forward = [(ring[i], ring[(i + 1) % count]) for i in range(count)]
    backward = [(ring[i], ring[(i - 1) % count]) for i in range(count)]
    steps = []
    for step in range(1, count // 2 + 1):
        moves = [("ahead", forward, ring_table[(my_spot - step) % count])]
        if 2 * step == count:
            moves = [("split", None, moves[0][2])]
        else:
            moves.append(("behind", backward, ring_table[(my_spot + step) % count]))
        steps.append(moves)
    half = head_count // 2

    def travel(name, pairs):
        if name != "split":
            held[name] = lax.ppermute(held[name], "ctx", pairs)
            return held[name]
        front = lax.ppermute(held["ahead"][:, :half], "ctx", forward)
        back = lax.ppermute(held["behind"][:, half:], "ctx", backward)
        return jnp.concatenate([front, back], axis=1)

    def score_chunk(keys_in, slab):
        raw = jnp.einsum("thd,shd->hts", query_rot, keys_in, preferred_element_type=jnp.float32)
        key_pos = slab * tok_rows + jnp.arange(tok_rows, dtype=jnp.int32)
        allowed = key_pos[None, :] <= query_pos[:, None]
        return jnp.where(allowed[None], raw * logit_scale, -jnp.inf)

    held = {"ahead": key_rot, "behind": key_rot}
    score_chunks = [score_chunk(key_rot, my_slab)]

    def key_step(moves):
        for name, pairs, slab in moves:
            score_chunks.append(score_chunk(travel(name, pairs), slab))

    early = (len(steps) + 1) // 2
    for moves in steps[:early]:
        key_step(moves)
    gate_keys = (held["ahead"], held["behind"])
    logdec = jnp.log1p(-decay_code.astype(jnp.float32) * 2.0 ** (-20))
    q_hat = jax.nn.silu(query_linear.astype(jnp.float32)).astype(jnp.bfloat16)
    k_hat = jax.nn.silu(key_linear.astype(jnp.float32)).astype(jnp.bfloat16)
    slab_state, local_out = lightning_local(q_hat, k_hat, value_linear, logdec)
    for moves in steps[early:]:
        key_step(moves)
    incoming = exclusive_scan(slab_state, logdec, tok_rows)
    local_pos = jnp.arange(tok_rows, dtype=jnp.float32)
    query_decay = jnp.exp(logdec[None, :] * (local_pos[:, None] + 1.0))
    carried = query_decay[:, :, None] * split_dot("thd,hde->the", q_hat, incoming)
    linear_out = local_out + carried
    square_sum = jnp.sum(linear_out * linear_out, axis=(1, 2))
    sharers = lax.axis_size("head")
    total_square = square_sum
    for shift in range(1, sharers):
        total_square = total_square + lax.ppermute(
            square_sum, "head", [(i, (i + shift) % sharers) for i in range(sharers)]
        )
    mean_sq = total_square / (head_count * lax.axis_size("head") * head_width)
    normed = (
        linear_out
        * lax.rsqrt(mean_sq + norm_eps)[:, None, None]
        * norm_gain[None]
        * jax.nn.sigmoid(gate_logits.astype(jnp.float32))
    )
    values_soft = normed.astype(jnp.bfloat16)
    gate_keys, values_soft = lax.optimization_barrier((gate_keys, values_soft))
    top = score_chunks[0].max(axis=2)
    for chunk in score_chunks[1:]:
        top = jnp.maximum(top, chunk.max(axis=2))
    prob_chunks = [jnp.exp(chunk - top[:, :, None]) for chunk in score_chunks]
    total = prob_chunks[0].sum(axis=2)
    for chunk in prob_chunks[1:]:
        total = total + chunk.sum(axis=2)
    weight_chunks = [chunk.astype(jnp.bfloat16) for chunk in prob_chunks]

    held = {"ahead": values_soft, "behind": values_soft}
    accum = jnp.einsum(
        "hts,shd->htd", weight_chunks[0], values_soft, preferred_element_type=jnp.float32
    )
    chunk_at = 1
    for moves in steps:
        for name, pairs, slab in moves:
            accum = accum + jnp.einsum(
                "hts,shd->htd",
                weight_chunks[chunk_at],
                travel(name, pairs),
                preferred_element_type=jnp.float32,
            )
            chunk_at += 1
    result = accum / total[:, :, None]
    return result.transpose(1, 0, 2).astype(jnp.bfloat16)


def ring_of(mesh):
    devices = np.moveaxis(np.asarray(mesh.devices), mesh.axis_names.index("ctx"), 0)
    line = devices.reshape(devices.shape[0], -1)[:, 0]
    count = len(line)
    try:
        spots = [tuple(int(v) for v in dev.coords) for dev in line]
    except (AttributeError, TypeError):
        return list(range(count))
    varying = [k for k in range(len(spots[0])) if len({s[k] for s in spots}) > 1]
    if len(varying) != 2:
        return sorted(range(count), key=lambda c: spots[c])
    varying.sort(key=lambda k: len({s[k] for s in spots}))
    outer, inner = varying
    order = []
    for turn, value in enumerate(sorted({s[outer] for s in spots})):
        members = [c for c in range(count) if spots[c][outer] == value]
        members.sort(key=lambda c: spots[c][inner], reverse=turn % 2 == 1)
        order += members
    return order


def solution(mesh):
    in_specs = (
        P(("groups", "ctx"), "head", None),
        P(("groups", "ctx"), "head", None),
        P(("groups", "ctx"), "head", None),
        P(("groups", "ctx"), "head", None),
        P("head", None),
        P("head"),
        P(("groups", "ctx"), "head", None),
        P(("groups", "ctx"), "head", None),
        P(),
    )
    out_specs = P(("groups", "ctx"), "head", None)
    body = functools.partial(local, ring_of(mesh))
    return jax.shard_map(body, mesh=mesh, in_specs=in_specs, out_specs=out_specs, check_vma=False)
```

```python
import functools
import math

import jax
import numpy as np
import jax.numpy as jnp
from jax import lax
from jax.sharding import PartitionSpec as P

BLOCK = 64
ORIG_CTX = 8192


rope_base = 10000.0
beta_fast = 32.0
beta_slow = 1.0
norm_eps = 1e-05
low_floor = -1e30


def yarn_table(yarn_factor, head_width):
    factor = yarn_factor[0].astype(jnp.float32)
    pair_ids = jnp.arange(head_width // 2, dtype=jnp.float32)
    base_freq = rope_base ** (-2.0 * pair_ids / head_width)
    wavelength = 2.0 * math.pi / base_freq
    ramp = jnp.clip((ORIG_CTX / wavelength - beta_slow) / (beta_fast - beta_slow), 0.0, 1.0)
    freq = base_freq * (ramp + (1.0 - ramp) / factor)
    mscale = 0.1 * jnp.log(factor) + 1.0
    return (freq, mscale * mscale / math.sqrt(head_width))


def rotate(values_in, positions, freq):
    angle = positions[:, None] * freq[None, :]
    cosine = jnp.cos(angle)[:, None, :]
    sine = jnp.sin(angle)[:, None, :]
    half_width = values_in.shape[2] // 2
    first = values_in[:, :, :half_width].astype(jnp.float32)
    second = values_in[:, :, half_width:].astype(jnp.float32)
    joined = jnp.concatenate(
        [first * cosine - second * sine, second * cosine + first * sine], axis=2
    )
    return joined.astype(jnp.bfloat16)


def lightning_local(q_hat, k_hat, value_linear, logdec):
    tok_rows, head_count, head_width = q_hat.shape
    block_count = tok_rows // BLOCK
    offsets = jnp.arange(BLOCK, dtype=jnp.float32)
    step_gap = offsets[:, None] - offsets[None, :]
    causal = step_gap >= 0
    intra_decay = jnp.where(
        causal[None], jnp.exp(logdec[:, None, None] * jnp.where(causal, step_gap, 0.0)[None]), 0.0
    )
    query_decay = jnp.exp(logdec[None, :] * (offsets[:, None] + 1.0))
    key_decay = jnp.exp(logdec[None, :] * (BLOCK - 1.0 - offsets[:, None]))
    block_decay = jnp.exp(logdec * BLOCK)

    def advance(carry_state, inputs):
        q_block, k_block, v_block = inputs
        scores = jnp.einsum("thd,shd->hts", q_block, k_block, preferred_element_type=jnp.float32)
        weights = (scores * intra_decay).astype(jnp.bfloat16)
        intra_part = jnp.einsum(
            "hts,shd->thd", weights, v_block, preferred_element_type=jnp.float32
        )
        carried = query_decay[:, :, None] * split_dot("thd,hde->the", q_block, carry_state)
        fresh_state = split_dot(
            "thd,the->hde", k_block, key_decay[:, :, None] * v_block.astype(jnp.float32)
        )
        return (carry_state * block_decay[:, None, None] + fresh_state, intra_part + carried)

    def split_blocks(array_in):
        return array_in.reshape(block_count, BLOCK, head_count, head_width)

    zero_state = jnp.zeros((head_count, head_width, head_width), jnp.float32)
    final_state, outputs = lax.scan(
        advance,
        zero_state,
        (split_blocks(q_hat), split_blocks(k_hat), split_blocks(value_linear)),
    )
    return (final_state, outputs.reshape(tok_rows, head_count, head_width))


def exclusive_scan(slab_state, logdec, tok_rows):
    count = lax.axis_size("ctx")
    decay = jnp.exp(logdec * tok_rows)[:, None, None]
    sent = slab_state.astype(jnp.bfloat16)
    running = lax.ppermute(sent, "ctx", [(i, i + 1) for i in range(count - 1)]).astype(jnp.float32)
    if count > 2:
        two_back = lax.ppermute(sent, "ctx", [(i, i + 2) for i in range(count - 2)])
        running = running + two_back.astype(jnp.float32) * decay
    offset = 2
    while offset < count:
        pairs = [(i, i + offset) for i in range(count - offset)]
        moved = lax.ppermute(running.astype(jnp.bfloat16), "ctx", pairs).astype(jnp.float32)
        scale = jnp.exp(logdec * (tok_rows * offset))
        running = running + moved * scale[:, None, None]
        offset *= 2
    return running


def split_dot(spec, exact, wide):
    high = wide.astype(jnp.bfloat16)
    low = (wide - high.astype(jnp.float32)).astype(jnp.bfloat16)
    first = jnp.einsum(spec, exact, high, preferred_element_type=jnp.float32)
    return first + jnp.einsum(spec, exact, low, preferred_element_type=jnp.float32)


def local(
    ring,
    query_linear,
    key_linear,
    value_linear,
    gate_logits,
    norm_gain,
    decay_code,
    query_soft,
    key_soft,
    yarn_factor,
):
    tok_rows, head_count, head_width = query_linear.shape
    my_slab = lax.axis_index("ctx")
    freq, logit_scale = yarn_table(yarn_factor, head_width)
    first_row = my_slab * tok_rows
    query_pos = first_row + jnp.arange(tok_rows, dtype=jnp.int32)
    positions = query_pos.astype(jnp.float32)
    query_rot = rotate(query_soft, positions, freq)
    key_rot = rotate(key_soft, positions, freq)
    count = len(ring)
    ring_table = jnp.asarray(ring, jnp.int32)
    spot_table = jnp.asarray(np.argsort(np.asarray(ring)), jnp.int32)
    my_spot = spot_table[my_slab]
    forward = [(ring[i], ring[(i + 1) % count]) for i in range(count)]
    backward = [(ring[i], ring[(i - 1) % count]) for i in range(count)]
    steps = []
    for step in range(1, count // 2 + 1):
        moves = [("ahead", forward, ring_table[(my_spot - step) % count])]
        if step <= (count - 1) // 2:
            moves.append(("behind", backward, ring_table[(my_spot + step) % count]))
        steps.append(moves)
    half = head_count // 2

    def travel(name, pairs):
        if name != "split":
            held[name] = lax.ppermute(held[name], "ctx", pairs)
            return held[name]
        front = lax.ppermute(held["ahead"][:, :half], "ctx", forward)
        back = lax.ppermute(held["behind"][:, half:], "ctx", backward)
        return jnp.concatenate([front, back], axis=1)

    def score_chunk(keys_in, slab):
        raw = jnp.einsum("thd,shd->hts", query_rot, keys_in, preferred_element_type=jnp.float32)
        key_pos = slab * tok_rows + jnp.arange(tok_rows, dtype=jnp.int32)
        allowed = key_pos[None, :] <= query_pos[:, None]
        return jnp.where(allowed[None], raw * logit_scale, -jnp.inf)

    held = {"ahead": key_rot, "behind": key_rot}
    score_chunks = [score_chunk(key_rot, my_slab)]

    def key_step(moves):
        for name, pairs, slab in moves:
            score_chunks.append(score_chunk(travel(name, pairs), slab))

    early = (len(steps) + 1) // 2
    for moves in steps[:early]:
        key_step(moves)
    gate_keys = (held["ahead"], held["behind"])
    logdec = jnp.log1p(-decay_code.astype(jnp.float32) * 2.0 ** (-20))
    q_hat = jax.nn.silu(query_linear.astype(jnp.float32)).astype(jnp.bfloat16)
    k_hat = jax.nn.silu(key_linear.astype(jnp.float32)).astype(jnp.bfloat16)
    slab_state, local_out = lightning_local(q_hat, k_hat, value_linear, logdec)
    for moves in steps[early:]:
        key_step(moves)
    incoming = exclusive_scan(slab_state, logdec, tok_rows)
    local_pos = jnp.arange(tok_rows, dtype=jnp.float32)
    query_decay = jnp.exp(logdec[None, :] * (local_pos[:, None] + 1.0))
    carried = query_decay[:, :, None] * split_dot("thd,hde->the", q_hat, incoming)
    linear_out = local_out + carried
    square_sum = jnp.sum(linear_out * linear_out, axis=(1, 2))
    total_square = lax.psum(square_sum, "head")
    mean_sq = total_square / (head_count * lax.axis_size("head") * head_width)
    normed = (
        linear_out
        * lax.rsqrt(mean_sq + norm_eps)[:, None, None]
        * norm_gain[None]
        * jax.nn.sigmoid(gate_logits.astype(jnp.float32))
    )
    values_soft = normed.astype(jnp.bfloat16)
    gate_keys, values_soft = lax.optimization_barrier((gate_keys, values_soft))
    top = score_chunks[0].max(axis=2)
    for chunk in score_chunks[1:]:
        top = jnp.maximum(top, chunk.max(axis=2))
    prob_chunks = [jnp.exp(chunk - top[:, :, None]) for chunk in score_chunks]
    total = prob_chunks[0].sum(axis=2)
    for chunk in prob_chunks[1:]:
        total = total + chunk.sum(axis=2)
    weight_chunks = [chunk.astype(jnp.bfloat16) for chunk in prob_chunks]

    held = {"ahead": values_soft, "behind": values_soft}
    accum = jnp.einsum(
        "hts,shd->htd", weight_chunks[0], values_soft, preferred_element_type=jnp.float32
    )
    chunk_at = 1
    for moves in steps:
        for name, pairs, slab in moves:
            accum = accum + jnp.einsum(
                "hts,shd->htd",
                weight_chunks[chunk_at],
                travel(name, pairs),
                preferred_element_type=jnp.float32,
            )
            chunk_at += 1
    result = accum / total[:, :, None]
    return result.transpose(1, 0, 2).astype(jnp.bfloat16)


def ring_of(mesh):
    devices = np.moveaxis(np.asarray(mesh.devices), mesh.axis_names.index("ctx"), 0)
    line = devices.reshape(devices.shape[0], -1)[:, 0]
    count = len(line)
    try:
        spots = [tuple(int(v) for v in dev.coords) for dev in line]
    except (AttributeError, TypeError):
        return list(range(count))
    varying = [k for k in range(len(spots[0])) if len({s[k] for s in spots}) > 1]
    if len(varying) != 2:
        return sorted(range(count), key=lambda c: spots[c])
    varying.sort(key=lambda k: len({s[k] for s in spots}))
    outer, inner = varying
    order = []
    for turn, value in enumerate(sorted({s[outer] for s in spots})):
        members = [c for c in range(count) if spots[c][outer] == value]
        members.sort(key=lambda c: spots[c][inner], reverse=turn % 2 == 1)
        order += members
    return order


def solution(mesh):
    in_specs = (
        P(("groups", "ctx"), "head", None),
        P(("groups", "ctx"), "head", None),
        P(("groups", "ctx"), "head", None),
        P(("groups", "ctx"), "head", None),
        P("head", None),
        P("head"),
        P(("groups", "ctx"), "head", None),
        P(("groups", "ctx"), "head", None),
        P(),
    )
    out_specs = P(("groups", "ctx"), "head", None)
    body = functools.partial(local, ring_of(mesh))
    return jax.shard_map(body, mesh=mesh, in_specs=in_specs, out_specs=out_specs, check_vma=False)
```

```python
import functools
import math

import jax
import numpy as np
import jax.numpy as jnp
from jax import lax
from jax.sharding import PartitionSpec as P

BLOCK = 64
ORIG_CTX = 8192


rope_base = 10000.0
beta_fast = 32.0
beta_slow = 1.0
norm_eps = 1e-05
low_floor = -1e30


def yarn_table(yarn_factor, head_width):
    factor = yarn_factor[0].astype(jnp.float32)
    pair_ids = jnp.arange(head_width // 2, dtype=jnp.float32)
    base_freq = rope_base ** (-2.0 * pair_ids / head_width)
    wavelength = 2.0 * math.pi / base_freq
    ramp = jnp.clip((ORIG_CTX / wavelength - beta_slow) / (beta_fast - beta_slow), 0.0, 1.0)
    freq = base_freq * (ramp + (1.0 - ramp) / factor)
    mscale = 0.1 * jnp.log(factor) + 1.0
    return (freq, mscale * mscale / math.sqrt(head_width))


def rotate(values_in, positions, freq):
    angle = positions[:, None] * freq[None, :]
    cosine = jnp.cos(angle)[:, None, :]
    sine = jnp.sin(angle)[:, None, :]
    half_width = values_in.shape[2] // 2
    first = values_in[:, :, :half_width].astype(jnp.float32)
    second = values_in[:, :, half_width:].astype(jnp.float32)
    joined = jnp.concatenate(
        [first * cosine - second * sine, second * cosine + first * sine], axis=2
    )
    return joined.astype(jnp.bfloat16)


def lightning_local(q_hat, k_hat, value_linear, logdec):
    tok_rows, head_count, head_width = q_hat.shape
    block_count = tok_rows // BLOCK
    offsets = jnp.arange(BLOCK, dtype=jnp.float32)
    step_gap = offsets[:, None] - offsets[None, :]
    causal = step_gap >= 0
    intra_decay = jnp.where(
        causal[None], jnp.exp(logdec[:, None, None] * jnp.where(causal, step_gap, 0.0)[None]), 0.0
    )
    query_decay = jnp.exp(logdec[None, :] * (offsets[:, None] + 1.0))
    key_decay = jnp.exp(logdec[None, :] * (BLOCK - 1.0 - offsets[:, None]))
    block_decay = jnp.exp(logdec * BLOCK)

    def advance(carry_state, inputs):
        q_block, k_block, v_block = inputs
        scores = jnp.einsum("thd,shd->hts", q_block, k_block, preferred_element_type=jnp.float32)
        weights = (scores * intra_decay).astype(jnp.bfloat16)
        intra_part = jnp.einsum(
            "hts,shd->thd", weights, v_block, preferred_element_type=jnp.float32
        )
        carried = query_decay[:, :, None] * split_dot("thd,hde->the", q_block, carry_state)
        fresh_state = split_dot(
            "thd,the->hde", k_block, key_decay[:, :, None] * v_block.astype(jnp.float32)
        )
        return (carry_state * block_decay[:, None, None] + fresh_state, intra_part + carried)

    def split_blocks(array_in):
        return array_in.reshape(block_count, BLOCK, head_count, head_width)

    zero_state = jnp.zeros((head_count, head_width, head_width), jnp.float32)
    final_state, outputs = lax.scan(
        advance,
        zero_state,
        (split_blocks(q_hat), split_blocks(k_hat), split_blocks(value_linear)),
        unroll=True,
    )
    return (final_state, outputs.reshape(tok_rows, head_count, head_width))


def exclusive_scan(slab_state, logdec, tok_rows):
    count = lax.axis_size("ctx")
    decay = jnp.exp(logdec * tok_rows)[:, None, None]
    sent = slab_state.astype(jnp.bfloat16)
    running = lax.ppermute(sent, "ctx", [(i, i + 1) for i in range(count - 1)]).astype(jnp.float32)
    if count > 2:
        two_back = lax.ppermute(sent, "ctx", [(i, i + 2) for i in range(count - 2)])
        running = running + two_back.astype(jnp.float32) * decay
    offset = 2
    while offset < count:
        pairs = [(i, i + offset) for i in range(count - offset)]
        moved = lax.ppermute(running.astype(jnp.bfloat16), "ctx", pairs).astype(jnp.float32)
        scale = jnp.exp(logdec * (tok_rows * offset))
        running = running + moved * scale[:, None, None]
        offset *= 2
    return running


def split_dot(spec, exact, wide):
    high = wide.astype(jnp.bfloat16)
    low = (wide - high.astype(jnp.float32)).astype(jnp.bfloat16)
    first = jnp.einsum(spec, exact, high, preferred_element_type=jnp.float32)
    return first + jnp.einsum(spec, exact, low, preferred_element_type=jnp.float32)


def local(
    ring,
    query_linear,
    key_linear,
    value_linear,
    gate_logits,
    norm_gain,
    decay_code,
    query_soft,
    key_soft,
    yarn_factor,
):
    tok_rows, head_count, head_width = query_linear.shape
    my_slab = lax.axis_index("ctx")
    freq, logit_scale = yarn_table(yarn_factor, head_width)
    first_row = my_slab * tok_rows
    query_pos = first_row + jnp.arange(tok_rows, dtype=jnp.int32)
    positions = query_pos.astype(jnp.float32)
    query_rot = rotate(query_soft, positions, freq)
    key_rot = rotate(key_soft, positions, freq)
    count = len(ring)
    ring_table = jnp.asarray(ring, jnp.int32)
    spot_table = jnp.asarray(np.argsort(np.asarray(ring)), jnp.int32)
    my_spot = spot_table[my_slab]
    forward = [(ring[i], ring[(i + 1) % count]) for i in range(count)]
    backward = [(ring[i], ring[(i - 1) % count]) for i in range(count)]
    steps = []
    for step in range(1, count // 2 + 1):
        moves = [("ahead", forward, ring_table[(my_spot - step) % count])]
        if 2 * step == count:
            moves = [("split", None, moves[0][2])]
        else:
            moves.append(("behind", backward, ring_table[(my_spot + step) % count]))
        steps.append(moves)
    half = head_count // 2

    def travel(name, pairs):
        if name != "split":
            held[name] = lax.ppermute(held[name], "ctx", pairs)
            return held[name]
        front = lax.ppermute(held["ahead"][:, :half], "ctx", forward)
        back = lax.ppermute(held["behind"][:, half:], "ctx", backward)
        return jnp.concatenate([front, back], axis=1)

    def score_chunk(keys_in, slab):
        raw = jnp.einsum("thd,shd->hts", query_rot, keys_in, preferred_element_type=jnp.float32)
        key_pos = slab * tok_rows + jnp.arange(tok_rows, dtype=jnp.int32)
        allowed = key_pos[None, :] <= query_pos[:, None]
        return jnp.where(allowed[None], raw * logit_scale, -jnp.inf)

    held = {"ahead": key_rot, "behind": key_rot}
    score_chunks = [score_chunk(key_rot, my_slab)]

    def key_step(moves):
        for name, pairs, slab in moves:
            score_chunks.append(score_chunk(travel(name, pairs), slab))

    early = (len(steps) + 1) // 2
    for moves in steps[:early]:
        key_step(moves)
    gate_keys = (held["ahead"], held["behind"])
    logdec = jnp.log1p(-decay_code.astype(jnp.float32) * 2.0 ** (-20))
    q_hat = jax.nn.silu(query_linear.astype(jnp.float32)).astype(jnp.bfloat16)
    k_hat = jax.nn.silu(key_linear.astype(jnp.float32)).astype(jnp.bfloat16)
    slab_state, local_out = lightning_local(q_hat, k_hat, value_linear, logdec)
    incoming = exclusive_scan(slab_state, logdec, tok_rows)
    local_pos = jnp.arange(tok_rows, dtype=jnp.float32)
    query_decay = jnp.exp(logdec[None, :] * (local_pos[:, None] + 1.0))
    carried = query_decay[:, :, None] * split_dot("thd,hde->the", q_hat, incoming)
    linear_out = local_out + carried
    square_sum = jnp.sum(linear_out * linear_out, axis=(1, 2))
    total_square = lax.psum(square_sum, "head")
    mean_sq = total_square / (head_count * lax.axis_size("head") * head_width)
    normed = (
        linear_out
        * lax.rsqrt(mean_sq + norm_eps)[:, None, None]
        * norm_gain[None]
        * jax.nn.sigmoid(gate_logits.astype(jnp.float32))
    )
    values_soft = normed.astype(jnp.bfloat16)
    gate_keys, values_soft = lax.optimization_barrier((gate_keys, values_soft))
    held["ahead"], held["behind"] = gate_keys
    for moves in steps[early:]:
        key_step(moves)
    top = score_chunks[0].max(axis=2)
    for chunk in score_chunks[1:]:
        top = jnp.maximum(top, chunk.max(axis=2))
    prob_chunks = [jnp.exp(chunk - top[:, :, None]) for chunk in score_chunks]
    total = prob_chunks[0].sum(axis=2)
    for chunk in prob_chunks[1:]:
        total = total + chunk.sum(axis=2)
    weight_chunks = [chunk.astype(jnp.bfloat16) for chunk in prob_chunks]

    held = {"ahead": values_soft, "behind": values_soft}
    accum = jnp.einsum(
        "hts,shd->htd", weight_chunks[0], values_soft, preferred_element_type=jnp.float32
    )
    chunk_at = 1
    for moves in steps:
        for name, pairs, slab in moves:
            accum = accum + jnp.einsum(
                "hts,shd->htd",
                weight_chunks[chunk_at],
                travel(name, pairs),
                preferred_element_type=jnp.float32,
            )
            chunk_at += 1
    result = accum / total[:, :, None]
    return result.transpose(1, 0, 2).astype(jnp.bfloat16)


def ring_of(mesh):
    devices = np.moveaxis(np.asarray(mesh.devices), mesh.axis_names.index("ctx"), 0)
    line = devices.reshape(devices.shape[0], -1)[:, 0]
    count = len(line)
    try:
        spots = [tuple(int(v) for v in dev.coords) for dev in line]
    except (AttributeError, TypeError):
        return list(range(count))
    varying = [k for k in range(len(spots[0])) if len({s[k] for s in spots}) > 1]
    if len(varying) != 2:
        return sorted(range(count), key=lambda c: spots[c])
    varying.sort(key=lambda k: len({s[k] for s in spots}))
    outer, inner = varying
    order = []
    for turn, value in enumerate(sorted({s[outer] for s in spots})):
        members = [c for c in range(count) if spots[c][outer] == value]
        members.sort(key=lambda c: spots[c][inner], reverse=turn % 2 == 1)
        order += members
    return order


def solution(mesh):
    in_specs = (
        P(("groups", "ctx"), "head", None),
        P(("groups", "ctx"), "head", None),
        P(("groups", "ctx"), "head", None),
        P(("groups", "ctx"), "head", None),
        P("head", None),
        P("head"),
        P(("groups", "ctx"), "head", None),
        P(("groups", "ctx"), "head", None),
        P(),
    )
    out_specs = P(("groups", "ctx"), "head", None)
    body = functools.partial(local, ring_of(mesh))
    return jax.shard_map(body, mesh=mesh, in_specs=in_specs, out_specs=out_specs, check_vma=False)
```

```python
import functools
import math

import jax
import numpy as np
import jax.numpy as jnp
from jax import lax
from jax.sharding import PartitionSpec as P

BLOCK = 64
ORIG_CTX = 8192


rope_base = 10000.0
beta_fast = 32.0
beta_slow = 1.0
norm_eps = 1e-05
low_floor = -1e30


def yarn_table(yarn_factor, head_width):
    factor = yarn_factor[0].astype(jnp.float32)
    pair_ids = jnp.arange(head_width // 2, dtype=jnp.float32)
    base_freq = rope_base ** (-2.0 * pair_ids / head_width)
    wavelength = 2.0 * math.pi / base_freq
    ramp = jnp.clip((ORIG_CTX / wavelength - beta_slow) / (beta_fast - beta_slow), 0.0, 1.0)
    freq = base_freq * (ramp + (1.0 - ramp) / factor)
    mscale = 0.1 * jnp.log(factor) + 1.0
    return (freq, mscale * mscale / math.sqrt(head_width))


def rotate(values_in, positions, freq):
    angle = positions[:, None] * freq[None, :]
    cosine = jnp.cos(angle)[:, None, :]
    sine = jnp.sin(angle)[:, None, :]
    half_width = values_in.shape[2] // 2
    first = values_in[:, :, :half_width].astype(jnp.float32)
    second = values_in[:, :, half_width:].astype(jnp.float32)
    joined = jnp.concatenate(
        [first * cosine - second * sine, second * cosine + first * sine], axis=2
    )
    return joined.astype(jnp.bfloat16)


def lightning_local(q_hat, k_hat, value_linear, logdec):
    tok_rows, head_count, head_width = q_hat.shape
    block_count = tok_rows // BLOCK
    offsets = jnp.arange(BLOCK, dtype=jnp.float32)
    step_gap = offsets[:, None] - offsets[None, :]
    causal = step_gap >= 0
    intra_decay = jnp.where(
        causal[None], jnp.exp(logdec[:, None, None] * jnp.where(causal, step_gap, 0.0)[None]), 0.0
    )
    query_decay = jnp.exp(logdec[None, :] * (offsets[:, None] + 1.0))
    key_decay = jnp.exp(logdec[None, :] * (BLOCK - 1.0 - offsets[:, None]))
    block_decay = jnp.exp(logdec * BLOCK)

    def advance(carry_state, inputs):
        q_block, k_block, v_block = inputs
        scores = jnp.einsum("thd,shd->hts", q_block, k_block, preferred_element_type=jnp.float32)
        weights = (scores * intra_decay).astype(jnp.bfloat16)
        intra_part = jnp.einsum(
            "hts,shd->thd", weights, v_block, preferred_element_type=jnp.float32
        )
        carried = query_decay[:, :, None] * split_dot("thd,hde->the", q_block, carry_state)
        fresh_state = split_dot(
            "thd,the->hde", k_block, key_decay[:, :, None] * v_block.astype(jnp.float32)
        )
        return (carry_state * block_decay[:, None, None] + fresh_state, intra_part + carried)

    def split_blocks(array_in):
        return array_in.reshape(block_count, BLOCK, head_count, head_width)

    zero_state = jnp.zeros((head_count, head_width, head_width), jnp.float32)
    final_state, outputs = lax.scan(
        advance,
        zero_state,
        (split_blocks(q_hat), split_blocks(k_hat), split_blocks(value_linear)),
        unroll=True,
    )
    return (final_state, outputs.reshape(tok_rows, head_count, head_width))


def exclusive_scan(slab_state, logdec, tok_rows):
    count = lax.axis_size("ctx")
    decay = jnp.exp(logdec * tok_rows)[:, None, None]
    sent = slab_state.astype(jnp.bfloat16)
    running = lax.ppermute(sent, "ctx", [(i, i + 1) for i in range(count - 1)]).astype(jnp.float32)
    if count > 2:
        two_back = lax.ppermute(sent, "ctx", [(i, i + 2) for i in range(count - 2)])
        running = running + two_back.astype(jnp.float32) * decay
    offset = 2
    while offset < count:
        pairs = [(i, i + offset) for i in range(count - offset)]
        moved = lax.ppermute(running.astype(jnp.bfloat16), "ctx", pairs).astype(jnp.float32)
        scale = jnp.exp(logdec * (tok_rows * offset))
        running = running + moved * scale[:, None, None]
        offset *= 2
    return running


def split_dot(spec, exact, wide):
    high = wide.astype(jnp.bfloat16)
    low = (wide - high.astype(jnp.float32)).astype(jnp.bfloat16)
    first = jnp.einsum(spec, exact, high, preferred_element_type=jnp.float32)
    return first + jnp.einsum(spec, exact, low, preferred_element_type=jnp.float32)


def local(
    ring,
    query_linear,
    key_linear,
    value_linear,
    gate_logits,
    norm_gain,
    decay_code,
    query_soft,
    key_soft,
    yarn_factor,
):
    tok_rows, head_count, head_width = query_linear.shape
    my_slab = lax.axis_index("ctx")
    freq, logit_scale = yarn_table(yarn_factor, head_width)
    first_row = my_slab * tok_rows
    query_pos = first_row + jnp.arange(tok_rows, dtype=jnp.int32)
    positions = query_pos.astype(jnp.float32)
    key_rot = rotate(key_soft, positions, freq)
    count = len(ring)
    ring_table = jnp.asarray(ring, jnp.int32)
    spot_table = jnp.asarray(np.argsort(np.asarray(ring)), jnp.int32)
    my_spot = spot_table[my_slab]
    forward = [(ring[i], ring[(i + 1) % count]) for i in range(count)]
    backward = [(ring[i], ring[(i - 1) % count]) for i in range(count)]
    steps = []
    for step in range(1, count // 2 + 1):
        moves = [("ahead", forward, ring_table[(my_spot - step) % count])]
        if 2 * step == count:
            moves = [("split", None, moves[0][2])]
        else:
            moves.append(("behind", backward, ring_table[(my_spot + step) % count]))
        steps.append(moves)
    half = head_count // 2

    def travel(name, pairs):
        if name != "split":
            held[name] = lax.ppermute(held[name], "ctx", pairs)
            return held[name]
        front = lax.ppermute(held["ahead"][:, :half], "ctx", forward)
        back = lax.ppermute(held["behind"][:, half:], "ctx", backward)
        return jnp.concatenate([front, back], axis=1)

    query_late, key_late = lax.optimization_barrier((query_soft, key_rot))
    query_rot = rotate(query_late, positions, freq)

    def score_chunk(keys_in, slab):
        raw = jnp.einsum("thd,shd->hts", query_rot, keys_in, preferred_element_type=jnp.float32)
        key_pos = slab * tok_rows + jnp.arange(tok_rows, dtype=jnp.int32)
        allowed = key_pos[None, :] <= query_pos[:, None]
        return jnp.where(allowed[None], raw * logit_scale, -jnp.inf)

    held = {"ahead": key_rot, "behind": key_rot}
    score_chunks = [score_chunk(key_rot, my_slab)]

    def key_step(moves):
        for name, pairs, slab in moves:
            score_chunks.append(score_chunk(travel(name, pairs), slab))

    early = (len(steps) + 1) // 2
    for moves in steps[:early]:
        key_step(moves)
    gate_keys = (held["ahead"], held["behind"])
    logdec = jnp.log1p(-decay_code.astype(jnp.float32) * 2.0 ** (-20))
    q_hat = jax.nn.silu(query_linear.astype(jnp.float32)).astype(jnp.bfloat16)
    k_hat = jax.nn.silu(key_linear.astype(jnp.float32)).astype(jnp.bfloat16)
    slab_state, local_out = lightning_local(q_hat, k_hat, value_linear, logdec)
    for moves in steps[early:]:
        key_step(moves)
    incoming = exclusive_scan(slab_state, logdec, tok_rows)
    local_pos = jnp.arange(tok_rows, dtype=jnp.float32)
    query_decay = jnp.exp(logdec[None, :] * (local_pos[:, None] + 1.0))
    carried = query_decay[:, :, None] * split_dot("thd,hde->the", q_hat, incoming)
    linear_out = local_out + carried
    square_sum = jnp.sum(linear_out * linear_out, axis=(1, 2))
    total_square = lax.psum(square_sum, "head")
    mean_sq = total_square / (head_count * lax.axis_size("head") * head_width)
    normed = (
        linear_out
        * lax.rsqrt(mean_sq + norm_eps)[:, None, None]
        * norm_gain[None]
        * jax.nn.sigmoid(gate_logits.astype(jnp.float32))
    )
    values_soft = normed.astype(jnp.bfloat16)
    gate_keys, values_soft = lax.optimization_barrier((gate_keys, values_soft))
    top = score_chunks[0].max(axis=2)
    for chunk in score_chunks[1:]:
        top = jnp.maximum(top, chunk.max(axis=2))
    prob_chunks = [jnp.exp(chunk - top[:, :, None]) for chunk in score_chunks]
    total = prob_chunks[0].sum(axis=2)
    for chunk in prob_chunks[1:]:
        total = total + chunk.sum(axis=2)
    weight_chunks = [chunk.astype(jnp.bfloat16) for chunk in prob_chunks]

    held = {"ahead": values_soft, "behind": values_soft}
    accum = jnp.einsum(
        "hts,shd->htd", weight_chunks[0], values_soft, preferred_element_type=jnp.float32
    )
    chunk_at = 1
    for moves in steps:
        for name, pairs, slab in moves:
            accum = accum + jnp.einsum(
                "hts,shd->htd",
                weight_chunks[chunk_at],
                travel(name, pairs),
                preferred_element_type=jnp.float32,
            )
            chunk_at += 1
    result = accum / total[:, :, None]
    return result.transpose(1, 0, 2).astype(jnp.bfloat16)


def ring_of(mesh):
    devices = np.moveaxis(np.asarray(mesh.devices), mesh.axis_names.index("ctx"), 0)
    line = devices.reshape(devices.shape[0], -1)[:, 0]
    count = len(line)
    try:
        spots = [tuple(int(v) for v in dev.coords) for dev in line]
    except (AttributeError, TypeError):
        return list(range(count))
    varying = [k for k in range(len(spots[0])) if len({s[k] for s in spots}) > 1]
    if len(varying) != 2:
        return sorted(range(count), key=lambda c: spots[c])
    varying.sort(key=lambda k: len({s[k] for s in spots}))
    outer, inner = varying
    order = []
    for turn, value in enumerate(sorted({s[outer] for s in spots})):
        members = [c for c in range(count) if spots[c][outer] == value]
        members.sort(key=lambda c: spots[c][inner], reverse=turn % 2 == 1)
        order += members
    return order


def solution(mesh):
    in_specs = (
        P(("groups", "ctx"), "head", None),
        P(("groups", "ctx"), "head", None),
        P(("groups", "ctx"), "head", None),
        P(("groups", "ctx"), "head", None),
        P("head", None),
        P("head"),
        P(("groups", "ctx"), "head", None),
        P(("groups", "ctx"), "head", None),
        P(),
    )
    out_specs = P(("groups", "ctx"), "head", None)
    body = functools.partial(local, ring_of(mesh))
    return jax.shard_map(body, mesh=mesh, in_specs=in_specs, out_specs=out_specs, check_vma=False)
```

```python
import functools
import math

import jax
import numpy as np
import jax.numpy as jnp
from jax import lax
from jax.sharding import PartitionSpec as P

BLOCK = 64
ORIG_CTX = 8192


rope_base = 10000.0
beta_fast = 32.0
beta_slow = 1.0
norm_eps = 1e-05
low_floor = -1e30


def yarn_table(yarn_factor, head_width):
    factor = yarn_factor[0].astype(jnp.float32)
    pair_ids = jnp.arange(head_width // 2, dtype=jnp.float32)
    base_freq = rope_base ** (-2.0 * pair_ids / head_width)
    wavelength = 2.0 * math.pi / base_freq
    ramp = jnp.clip((ORIG_CTX / wavelength - beta_slow) / (beta_fast - beta_slow), 0.0, 1.0)
    freq = base_freq * (ramp + (1.0 - ramp) / factor)
    mscale = 0.1 * jnp.log(factor) + 1.0
    return (freq, mscale * mscale / math.sqrt(head_width))


def rotate(values_in, positions, freq):
    angle = positions[:, None] * freq[None, :]
    cosine = jnp.cos(angle)[:, None, :]
    sine = jnp.sin(angle)[:, None, :]
    half_width = values_in.shape[2] // 2
    first = values_in[:, :, :half_width].astype(jnp.float32)
    second = values_in[:, :, half_width:].astype(jnp.float32)
    joined = jnp.concatenate(
        [first * cosine - second * sine, second * cosine + first * sine], axis=2
    )
    return joined.astype(jnp.bfloat16)


def lightning_local(q_hat, k_hat, value_linear, logdec):
    tok_rows, head_count, head_width = q_hat.shape
    block_count = tok_rows // BLOCK
    offsets = jnp.arange(BLOCK, dtype=jnp.float32)
    step_gap = offsets[:, None] - offsets[None, :]
    causal = step_gap >= 0
    intra_decay = jnp.where(
        causal[None], jnp.exp(logdec[:, None, None] * jnp.where(causal, step_gap, 0.0)[None]), 0.0
    )
    query_decay = jnp.exp(logdec[None, :] * (offsets[:, None] + 1.0))
    key_decay = jnp.exp(logdec[None, :] * (BLOCK - 1.0 - offsets[:, None]))
    block_decay = jnp.exp(logdec * BLOCK)

    def advance(carry_state, inputs):
        q_block, k_block, v_block = inputs
        scores = jnp.einsum("thd,shd->hts", q_block, k_block, preferred_element_type=jnp.float32)
        weights = (scores * intra_decay).astype(jnp.bfloat16)
        intra_part = jnp.einsum(
            "hts,shd->thd", weights, v_block, preferred_element_type=jnp.float32
        )
        carried = query_decay[:, :, None] * split_dot("thd,hde->the", q_block, carry_state)
        fresh_state = split_dot(
            "thd,the->hde", k_block, key_decay[:, :, None] * v_block.astype(jnp.float32)
        )
        return (carry_state * block_decay[:, None, None] + fresh_state, intra_part + carried)

    def split_blocks(array_in):
        return array_in.reshape(block_count, BLOCK, head_count, head_width)

    zero_state = jnp.zeros((head_count, head_width, head_width), jnp.float32)
    final_state, outputs = lax.scan(
        advance,
        zero_state,
        (split_blocks(q_hat), split_blocks(k_hat), split_blocks(value_linear)),
        unroll=True,
    )
    return (final_state, outputs.reshape(tok_rows, head_count, head_width))


def exclusive_scan(slab_state, logdec, tok_rows):
    count = lax.axis_size("ctx")
    decay = jnp.exp(logdec * tok_rows)[:, None, None]
    sent = slab_state.astype(jnp.bfloat16)
    running = lax.ppermute(sent, "ctx", [(i, i + 1) for i in range(count - 1)]).astype(jnp.float32)
    offset = 1
    while offset < count:
        pairs = [(i, i + offset) for i in range(count - offset)]
        moved = lax.ppermute(running.astype(jnp.bfloat16), "ctx", pairs).astype(jnp.float32)
        scale = jnp.exp(logdec * (tok_rows * offset))
        running = running + moved * scale[:, None, None]
        offset *= 2
    return running


def split_dot(spec, exact, wide):
    high = wide.astype(jnp.bfloat16)
    low = (wide - high.astype(jnp.float32)).astype(jnp.bfloat16)
    first = jnp.einsum(spec, exact, high, preferred_element_type=jnp.float32)
    return first + jnp.einsum(spec, exact, low, preferred_element_type=jnp.float32)


def local(
    ring,
    query_linear,
    key_linear,
    value_linear,
    gate_logits,
    norm_gain,
    decay_code,
    query_soft,
    key_soft,
    yarn_factor,
):
    tok_rows, head_count, head_width = query_linear.shape
    my_slab = lax.axis_index("ctx")
    freq, logit_scale = yarn_table(yarn_factor, head_width)
    first_row = my_slab * tok_rows
    query_pos = first_row + jnp.arange(tok_rows, dtype=jnp.int32)
    positions = query_pos.astype(jnp.float32)
    query_rot = rotate(query_soft, positions, freq)
    key_rot = rotate(key_soft, positions, freq)
    count = len(ring)
    ring_table = jnp.asarray(ring, jnp.int32)
    spot_table = jnp.asarray(np.argsort(np.asarray(ring)), jnp.int32)
    my_spot = spot_table[my_slab]
    forward = [(ring[i], ring[(i + 1) % count]) for i in range(count)]
    backward = [(ring[i], ring[(i - 1) % count]) for i in range(count)]
    steps = []
    for step in range(1, count // 2 + 1):
        moves = [("ahead", forward, ring_table[(my_spot - step) % count])]
        if 2 * step == count:
            moves = [("split", None, moves[0][2])]
        else:
            moves.append(("behind", backward, ring_table[(my_spot + step) % count]))
        steps.append(moves)
    half = head_count // 2

    def travel(name, pairs):
        if name != "split":
            held[name] = lax.ppermute(held[name], "ctx", pairs)
            return held[name]
        front = lax.ppermute(held["ahead"][:, :half], "ctx", forward)
        back = lax.ppermute(held["behind"][:, half:], "ctx", backward)
        return jnp.concatenate([front, back], axis=1)

    def score_chunk(keys_in, slab):
        raw = jnp.einsum("thd,shd->hts", query_rot, keys_in, preferred_element_type=jnp.float32)
        key_pos = slab * tok_rows + jnp.arange(tok_rows, dtype=jnp.int32)
        allowed = key_pos[None, :] <= query_pos[:, None]
        return jnp.where(allowed[None], raw * logit_scale, -jnp.inf)

    held = {"ahead": key_rot, "behind": key_rot}
    score_chunks = [score_chunk(key_rot, my_slab)]

    def key_step(moves):
        for name, pairs, slab in moves:
            score_chunks.append(score_chunk(travel(name, pairs), slab))

    early = (len(steps) + 1) // 2
    for moves in steps[:early]:
        key_step(moves)
    gate_keys = (held["ahead"], held["behind"])
    logdec = jnp.log1p(-decay_code.astype(jnp.float32) * 2.0 ** (-20))
    q_hat = jax.nn.silu(query_linear.astype(jnp.float32)).astype(jnp.bfloat16)
    k_hat = jax.nn.silu(key_linear.astype(jnp.float32)).astype(jnp.bfloat16)
    slab_state, local_out = lightning_local(q_hat, k_hat, value_linear, logdec)
    for moves in steps[early:]:
        key_step(moves)
    incoming = exclusive_scan(slab_state, logdec, tok_rows)
    local_pos = jnp.arange(tok_rows, dtype=jnp.float32)
    query_decay = jnp.exp(logdec[None, :] * (local_pos[:, None] + 1.0))
    carried = query_decay[:, :, None] * split_dot("thd,hde->the", q_hat, incoming)
    linear_out = local_out + carried
    square_sum = jnp.sum(linear_out * linear_out, axis=(1, 2))
    total_square = lax.psum(square_sum, "head")
    mean_sq = total_square / (head_count * lax.axis_size("head") * head_width)
    normed = (
        linear_out
        * lax.rsqrt(mean_sq + norm_eps)[:, None, None]
        * norm_gain[None]
        * jax.nn.sigmoid(gate_logits.astype(jnp.float32))
    )
    values_soft = normed.astype(jnp.bfloat16)
    gate_keys, values_soft = lax.optimization_barrier((gate_keys, values_soft))
    top = score_chunks[0].max(axis=2)
    for chunk in score_chunks[1:]:
        top = jnp.maximum(top, chunk.max(axis=2))
    prob_chunks = [jnp.exp(chunk - top[:, :, None]) for chunk in score_chunks]
    total = prob_chunks[0].sum(axis=2)
    for chunk in prob_chunks[1:]:
        total = total + chunk.sum(axis=2)
    weight_chunks = [chunk.astype(jnp.bfloat16) for chunk in prob_chunks]

    held = {"ahead": values_soft, "behind": values_soft}
    accum = jnp.einsum(
        "hts,shd->htd", weight_chunks[0], values_soft, preferred_element_type=jnp.float32
    )
    chunk_at = 1
    for moves in steps:
        for name, pairs, slab in moves:
            accum = accum + jnp.einsum(
                "hts,shd->htd",
                weight_chunks[chunk_at],
                travel(name, pairs),
                preferred_element_type=jnp.float32,
            )
            chunk_at += 1
    result = accum / total[:, :, None]
    return result.transpose(1, 0, 2).astype(jnp.bfloat16)


def ring_of(mesh):
    devices = np.moveaxis(np.asarray(mesh.devices), mesh.axis_names.index("ctx"), 0)
    line = devices.reshape(devices.shape[0], -1)[:, 0]
    count = len(line)
    try:
        spots = [tuple(int(v) for v in dev.coords) for dev in line]
    except (AttributeError, TypeError):
        return list(range(count))
    varying = [k for k in range(len(spots[0])) if len({s[k] for s in spots}) > 1]
    if len(varying) != 2:
        return sorted(range(count), key=lambda c: spots[c])
    varying.sort(key=lambda k: len({s[k] for s in spots}))
    outer, inner = varying
    order = []
    for turn, value in enumerate(sorted({s[outer] for s in spots})):
        members = [c for c in range(count) if spots[c][outer] == value]
        members.sort(key=lambda c: spots[c][inner], reverse=turn % 2 == 1)
        order += members
    return order


def solution(mesh):
    in_specs = (
        P(("groups", "ctx"), "head", None),
        P(("groups", "ctx"), "head", None),
        P(("groups", "ctx"), "head", None),
        P(("groups", "ctx"), "head", None),
        P("head", None),
        P("head"),
        P(("groups", "ctx"), "head", None),
        P(("groups", "ctx"), "head", None),
        P(),
    )
    out_specs = P(("groups", "ctx"), "head", None)
    body = functools.partial(local, ring_of(mesh))
    return jax.shard_map(body, mesh=mesh, in_specs=in_specs, out_specs=out_specs, check_vma=False)
```

```python
import functools
import math

import jax
import numpy as np
import jax.numpy as jnp
from jax import lax
from jax.sharding import PartitionSpec as P

BLOCK = 64
ORIG_CTX = 8192


rope_base = 10000.0
beta_fast = 32.0
beta_slow = 1.0
norm_eps = 1e-05
low_floor = -1e30


def yarn_table(yarn_factor, head_width):
    factor = yarn_factor[0].astype(jnp.float32)
    pair_ids = jnp.arange(head_width // 2, dtype=jnp.float32)
    base_freq = rope_base ** (-2.0 * pair_ids / head_width)
    wavelength = 2.0 * math.pi / base_freq
    ramp = jnp.clip((ORIG_CTX / wavelength - beta_slow) / (beta_fast - beta_slow), 0.0, 1.0)
    freq = base_freq * (ramp + (1.0 - ramp) / factor)
    mscale = 0.1 * jnp.log(factor) + 1.0
    return (freq, mscale * mscale / math.sqrt(head_width))


def rotate(values_in, positions, freq):
    angle = positions[:, None] * freq[None, :]
    cosine = jnp.cos(angle)[:, None, :]
    sine = jnp.sin(angle)[:, None, :]
    half_width = values_in.shape[2] // 2
    first = values_in[:, :, :half_width].astype(jnp.float32)
    second = values_in[:, :, half_width:].astype(jnp.float32)
    joined = jnp.concatenate(
        [first * cosine - second * sine, second * cosine + first * sine], axis=2
    )
    return joined.astype(jnp.bfloat16)


def lightning_local(q_hat, k_hat, value_linear, logdec):
    tok_rows, head_count, head_width = q_hat.shape
    block_count = tok_rows // BLOCK
    offsets = jnp.arange(BLOCK, dtype=jnp.float32)
    step_gap = offsets[:, None] - offsets[None, :]
    causal = step_gap >= 0
    intra_decay = jnp.where(
        causal[None], jnp.exp(logdec[:, None, None] * jnp.where(causal, step_gap, 0.0)[None]), 0.0
    )
    query_decay = jnp.exp(logdec[None, :] * (offsets[:, None] + 1.0))
    key_decay = jnp.exp(logdec[None, :] * (BLOCK - 1.0 - offsets[:, None]))
    block_decay = jnp.exp(logdec * BLOCK)

    def advance(carry_state, inputs):
        q_block, k_block, v_block = inputs
        scores = jnp.einsum("thd,shd->hts", q_block, k_block, preferred_element_type=jnp.float32)
        weights = (scores * intra_decay).astype(jnp.bfloat16)
        intra_part = jnp.einsum(
            "hts,shd->thd", weights, v_block, preferred_element_type=jnp.float32
        )
        carried = query_decay[:, :, None] * split_dot("thd,hde->the", q_block, carry_state)
        fresh_state = split_dot(
            "thd,the->hde", k_block, key_decay[:, :, None] * v_block.astype(jnp.float32)
        )
        return (carry_state * block_decay[:, None, None] + fresh_state, intra_part + carried)

    def split_blocks(array_in):
        return array_in.reshape(block_count, BLOCK, head_count, head_width)

    zero_state = jnp.zeros((head_count, head_width, head_width), jnp.float32)
    final_state, outputs = lax.scan(
        advance,
        zero_state,
        (split_blocks(q_hat), split_blocks(k_hat), split_blocks(value_linear)),
        unroll=True,
    )
    return (final_state, outputs.reshape(tok_rows, head_count, head_width))


def exclusive_scan(slab_state, logdec, tok_rows):
    count = lax.axis_size("ctx")
    decay = jnp.exp(logdec * tok_rows)[:, None, None]
    sent = slab_state.astype(jnp.bfloat16)
    running = lax.ppermute(sent, "ctx", [(i, i + 1) for i in range(count - 1)]).astype(jnp.float32)
    if count > 2:
        two_back = lax.ppermute(sent, "ctx", [(i, i + 2) for i in range(count - 2)])
        running = running + two_back.astype(jnp.float32) * decay
    offset = 2
    while offset < count:
        pairs = [(i, i + offset) for i in range(count - offset)]
        moved = lax.ppermute(running.astype(jnp.bfloat16), "ctx", pairs).astype(jnp.float32)
        scale = jnp.exp(logdec * (tok_rows * offset))
        running = running + moved * scale[:, None, None]
        offset *= 2
    return running


def split_dot(spec, exact, wide):
    high = wide.astype(jnp.bfloat16)
    low = (wide - high.astype(jnp.float32)).astype(jnp.bfloat16)
    first = jnp.einsum(spec, exact, high, preferred_element_type=jnp.float32)
    return first + jnp.einsum(spec, exact, low, preferred_element_type=jnp.float32)


def local(
    ring,
    query_linear,
    key_linear,
    value_linear,
    gate_logits,
    norm_gain,
    decay_code,
    query_soft,
    key_soft,
    yarn_factor,
):
    tok_rows, head_count, head_width = query_linear.shape
    my_slab = lax.axis_index("ctx")
    freq, logit_scale = yarn_table(yarn_factor, head_width)
    first_row = my_slab * tok_rows
    query_pos = first_row + jnp.arange(tok_rows, dtype=jnp.int32)
    positions = query_pos.astype(jnp.float32)
    query_rot = rotate(query_soft, positions, freq)
    key_rot = rotate(key_soft, positions, freq)
    count = len(ring)
    ring_table = jnp.asarray(ring, jnp.int32)
    spot_table = jnp.asarray(np.argsort(np.asarray(ring)), jnp.int32)
    my_spot = spot_table[my_slab]
    forward = [(ring[i], ring[(i + 1) % count]) for i in range(count)]
    backward = [(ring[i], ring[(i - 1) % count]) for i in range(count)]
    steps = []
    for step in range(1, count // 2 + 1):
        moves = [("ahead", forward, ring_table[(my_spot - step) % count])]
        if 2 * step == count:
            moves = [("split", None, moves[0][2])]
        else:
            moves.append(("behind", backward, ring_table[(my_spot + step) % count]))
        steps.append(moves)
    half = head_count // 2

    def travel(name, pairs):
        if name != "split":
            held[name] = lax.ppermute(held[name], "ctx", pairs)
            return held[name]
        front = lax.ppermute(held["ahead"][:, :half], "ctx", forward)
        back = lax.ppermute(held["behind"][:, half:], "ctx", backward)
        return jnp.concatenate([front, back], axis=1)

    def score_chunk(keys_in, slab):
        raw = jnp.einsum("thd,shd->hts", query_rot, keys_in, preferred_element_type=jnp.float32)
        key_pos = slab * tok_rows + jnp.arange(tok_rows, dtype=jnp.int32)
        allowed = key_pos[None, :] <= query_pos[:, None]
        return jnp.where(allowed[None], raw * logit_scale, -jnp.inf)

    held = {"ahead": key_rot, "behind": key_rot}
    score_chunks = [score_chunk(key_rot, my_slab)]

    def key_step(moves):
        for name, pairs, slab in moves:
            score_chunks.append(score_chunk(travel(name, pairs), slab))

    early = (len(steps) + 1) // 2
    for index, moves in enumerate(steps[:early]):
        key_step(moves)
        if index == 0:
            gate_keys = (held["ahead"], held["behind"])
    logdec = jnp.log1p(-decay_code.astype(jnp.float32) * 2.0 ** (-20))
    q_hat = jax.nn.silu(query_linear.astype(jnp.float32)).astype(jnp.bfloat16)
    k_hat = jax.nn.silu(key_linear.astype(jnp.float32)).astype(jnp.bfloat16)
    slab_state, local_out = lightning_local(q_hat, k_hat, value_linear, logdec)
    for moves in steps[early:]:
        key_step(moves)
    incoming = exclusive_scan(slab_state, logdec, tok_rows)
    local_pos = jnp.arange(tok_rows, dtype=jnp.float32)
    query_decay = jnp.exp(logdec[None, :] * (local_pos[:, None] + 1.0))
    carried = query_decay[:, :, None] * split_dot("thd,hde->the", q_hat, incoming)
    linear_out = local_out + carried
    square_sum = jnp.sum(linear_out * linear_out, axis=(1, 2))
    total_square = lax.psum(square_sum, "head")
    mean_sq = total_square / (head_count * lax.axis_size("head") * head_width)
    normed = (
        linear_out
        * lax.rsqrt(mean_sq + norm_eps)[:, None, None]
        * norm_gain[None]
        * jax.nn.sigmoid(gate_logits.astype(jnp.float32))
    )
    values_soft = normed.astype(jnp.bfloat16)
    gate_keys, values_soft = lax.optimization_barrier((gate_keys, values_soft))
    top = score_chunks[0].max(axis=2)
    for chunk in score_chunks[1:]:
        top = jnp.maximum(top, chunk.max(axis=2))
    prob_chunks = [jnp.exp(chunk - top[:, :, None]) for chunk in score_chunks]
    total = prob_chunks[0].sum(axis=2)
    for chunk in prob_chunks[1:]:
        total = total + chunk.sum(axis=2)
    weight_chunks = [chunk.astype(jnp.bfloat16) for chunk in prob_chunks]

    held = {"ahead": values_soft, "behind": values_soft}
    accum = jnp.einsum(
        "hts,shd->htd", weight_chunks[0], values_soft, preferred_element_type=jnp.float32
    )
    chunk_at = 1
    for moves in steps:
        for name, pairs, slab in moves:
            accum = accum + jnp.einsum(
                "hts,shd->htd",
                weight_chunks[chunk_at],
                travel(name, pairs),
                preferred_element_type=jnp.float32,
            )
            chunk_at += 1
    result = accum / total[:, :, None]
    return result.transpose(1, 0, 2).astype(jnp.bfloat16)


def ring_of(mesh):
    devices = np.moveaxis(np.asarray(mesh.devices), mesh.axis_names.index("ctx"), 0)
    line = devices.reshape(devices.shape[0], -1)[:, 0]
    count = len(line)
    try:
        spots = [tuple(int(v) for v in dev.coords) for dev in line]
    except (AttributeError, TypeError):
        return list(range(count))
    varying = [k for k in range(len(spots[0])) if len({s[k] for s in spots}) > 1]
    if len(varying) != 2:
        return sorted(range(count), key=lambda c: spots[c])
    varying.sort(key=lambda k: len({s[k] for s in spots}))
    outer, inner = varying
    order = []
    for turn, value in enumerate(sorted({s[outer] for s in spots})):
        members = [c for c in range(count) if spots[c][outer] == value]
        members.sort(key=lambda c: spots[c][inner], reverse=turn % 2 == 1)
        order += members
    return order


def solution(mesh):
    in_specs = (
        P(("groups", "ctx"), "head", None),
        P(("groups", "ctx"), "head", None),
        P(("groups", "ctx"), "head", None),
        P(("groups", "ctx"), "head", None),
        P("head", None),
        P("head"),
        P(("groups", "ctx"), "head", None),
        P(("groups", "ctx"), "head", None),
        P(),
    )
    out_specs = P(("groups", "ctx"), "head", None)
    body = functools.partial(local, ring_of(mesh))
    return jax.shard_map(body, mesh=mesh, in_specs=in_specs, out_specs=out_specs, check_vma=False)
```
